32 devices in a mesh: pipe: 1, seq: 32 (over z, y, x, core).
Axes of the slice: x: 2, y: 2, z: 4, core: 2. Of those that a mesh axis runs over, the one named last changes fastest.
Arguments:
- queries: bfloat16 [1, 4096, 4096], P('pipe', 'seq'), may hold values from -42 to 42
- key_rows: bfloat16 [1, 4096, 2048], P('pipe', 'seq'), may hold values from -14 to 14
- value_rows: bfloat16 [1, 4096, 2048], P('pipe', 'seq'), may hold values from -6 to 6
- arriving_grad: bfloat16 [1, 4096, 4096], P('pipe', 'seq'), may hold values from -6 to 6
- doc_blocks: int32 [1, 32], P('pipe'), may hold values from 0 to 3, never falling along the last dimension, each value on 1 to 16 neighbouring positions
Outputs:
- grad_query: bfloat16 [1, 4096, 4096], P('pipe', 'seq')
- grad_key: bfloat16 [1, 4096, 2048], P('pipe', 'seq')
- grad_value: bfloat16 [1, 4096, 2048], P('pipe', 'seq')
The draws below stay inside these ranges and needn't reach their ends.
Inputs may be any that keep to these rules, and one draw needn't show every extreme that they name: `doc_blocks`: in each section the document ids never fall from block to block, and each document covers 1 to 16 blocks, and at least one document of each section covers exactly 16.
All inputs are finite; a program needn't handle non-finite values.
Results may differ from the reference program's by a relative error of at most 0.015.
Values may be sent and summed in bfloat16 or wider, within the bound.
No kernel may reach another device: no remote copies, remote signals or barrier semaphores. Data moves between devices by JAX's collectives and lax.ppermute only.
A program may use at most 192 MiB of HBM per device.

```python
import math
import jax
import jax.numpy as jnp
import numpy as np
from jax import lax

HEADS = 32
KV_HEADS = 16
HEAD_DIM = 128
WINDOW = 1024
MBLK = 128
SECTIONS = 1
SEQLEN = 4096
BLOCKS = 32


def paired_draw(key):
    base = jax.random.fold_in(key, 7)
    key_query, key_keys = jax.random.split(base, 2)
    key_shape = (SECTIONS, SEQLEN, KV_HEADS, HEAD_DIM)
    query_shape = (SECTIONS, SEQLEN, HEADS, HEAD_DIM)
    keyvals = jnp.clip(jax.random.normal(key_keys, key_shape, jnp.float32), -4.0, 4.0)
    queryvals = jnp.clip(jax.random.normal(key_query, query_shape, jnp.float32), -4.0, 4.0)
    return (queryvals.reshape(SECTIONS, SEQLEN, HEADS * HEAD_DIM), keyvals.reshape(SECTIONS, SEQLEN, KV_HEADS * HEAD_DIM))


def draw_queries(key, part):
    return paired_draw(key)[0].astype(jnp.bfloat16)


def draw_key_rows(key, part):
    return paired_draw(key)[1].astype(jnp.bfloat16)


def levels(rng, dims, cuts, smallest, high):
    factor_of, own = 1.0, jax.random.fold_in(rng, 6)
    for dim, shards_of in cuts:
        steps = jnp.exp(jax.random.uniform(jax.random.fold_in(own, dim), (shards_of,), jnp.float32, smallest / len(cuts), high / len(cuts)))
        factor_of = factor_of * jnp.repeat(steps, dims[dim] // shards_of).reshape([-1 if axis == dim else 1 for axis in range(len(dims))])
    return factor_of


def length_profile(count, total, reach, skew):
    weights = [(1 << 20) // math.isqrt(grade ** skew) + 1 for grade in range(2, count + 1)]
    spare, counts = total - reach - (count - 1), [1] * (count - 1)
    while spare > 0:
        free = [i for i in range(count - 1) if counts[i] < reach]
        pool, left = sum([weights[i] for i in free]), spare
        for i in free:
            addition = min(reach - counts[i], max(1, left * weights[i] // pool), spare)
            counts[i] = counts[i] + addition
            spare = spare - addition
    return np.array([reach] + counts)


def uneven(own_key, count, total, reach, slope):
    if count == 2:
        one = jax.random.randint(own_key, (), max(1, total - reach), min(reach, total - 1) + 1)
        return jnp.stack([one, total - one])
    tallies = jnp.asarray(length_profile(count, total, reach, slope), jnp.int32)
    pairs = (count - 1) // 2
    source_of, receiver = tallies[1:1 + 2 * pairs:2], tallies[2:2 + 2 * pairs:2]
    margin = jnp.minimum(source_of - 1, reach - receiver)
    passed = jax.random.randint(jax.random.fold_in(own_key, 1), (pairs,), 0, 1 << 20) % (margin + 1)
    tallies = tallies.at[1:1 + 2 * pairs:2].set(source_of - passed).at[2:2 + 2 * pairs:2].set(receiver + passed)
    return tallies[jax.random.permutation(jax.random.fold_in(own_key, 2), count)]


def normal_values(key, extent, scale, limit, shards=(), held_as=jnp.bfloat16):
    loudness = levels(key, extent, shards, -0.22, 0.18) if shards else 1.0
    values = jax.random.normal(key, extent, jnp.float32) * scale * loudness
    return jnp.minimum(jnp.maximum(values, -limit), limit).astype(held_as)


def setup_inputs(seed: int = 0) -> dict:
    splits = jax.random.split(jax.random.key(seed), 6)
    return {
        "queries": draw_queries(jax.random.fold_in(splits[5], 71), 0),
        "key_rows": draw_key_rows(jax.random.fold_in(splits[5], 71), 0),
        "value_rows": normal_values(splits[2], (SECTIONS, SEQLEN, KV_HEADS * HEAD_DIM), 1.0, 6.0, ((1, 32),)),
        "arriving_grad": normal_values(splits[3], (SECTIONS, SEQLEN, HEADS * HEAD_DIM), 1.0, 6.0, ((1, 32),)),
        "doc_blocks": jax.vmap(lambda own: jnp.searchsorted(jnp.cumsum(uneven(own, max(2, BLOCKS // 8), BLOCKS, BLOCKS // 2, 1)), jnp.arange(BLOCKS), side="right"))(jax.random.split(splits[4], SECTIONS)).reshape((SECTIONS, BLOCKS)).astype(jnp.int32),
    }


SCORE_SCALE = 168.0 ** -0.5
MASKED_SCORE = -1.0e30


def rounded(values):
    return lax.optimization_barrier(values.astype(jnp.bfloat16)).astype(jnp.float32)


def section_grads(operands):
    queries, key_rows, value_rows, grad_out, doc_row = operands
    length = queries.shape[0]
    group_size = HEADS // KV_HEADS
    query3 = queries.reshape(length, HEADS, HEAD_DIM).astype(jnp.float32)
    grad3 = grad_out.reshape(length, HEADS, HEAD_DIM).astype(jnp.float32)
    key3 = jnp.repeat(key_rows.reshape(length, KV_HEADS, HEAD_DIM), group_size, axis=1).astype(jnp.float32)
    value3 = jnp.repeat(value_rows.reshape(length, KV_HEADS, HEAD_DIM), group_size, axis=1).astype(jnp.float32)
    key_pad = jnp.pad(key3, ((WINDOW, 0), (0, 0), (0, 0)))
    value_pad = jnp.pad(value3, ((WINDOW, 0), (0, 0), (0, 0)))
    token_doc = jnp.repeat(doc_row.astype(jnp.int32), MBLK)
    doc_pad = jnp.concatenate([jnp.full((WINDOW,), -1, jnp.int32), token_doc])
    key_span = WINDOW + MBLK

    def one_block(carried, block_index):
        key_acc, value_acc = carried
        offset = (block_index * MBLK).astype(jnp.int32)
        query_blk = lax.dynamic_slice_in_dim(query3, offset, MBLK, 0)
        grad_blk = lax.dynamic_slice_in_dim(grad3, offset, MBLK, 0)
        key_blk = lax.dynamic_slice_in_dim(key_pad, offset, key_span, 0)
        value_blk = lax.dynamic_slice_in_dim(value_pad, offset, key_span, 0)
        query_doc = lax.dynamic_slice_in_dim(token_doc, offset, MBLK, 0)
        key_doc = lax.dynamic_slice_in_dim(doc_pad, offset, key_span, 0)
        query_pos = offset + jnp.arange(MBLK, dtype=jnp.int32)
        key_pos = offset - WINDOW + jnp.arange(key_span, dtype=jnp.int32)
        distance = query_pos[:, None] - key_pos[None, :]
        allowed = (distance >= 0) & (distance < WINDOW) & (query_doc[:, None] == key_doc[None, :])
        scores = jnp.einsum("qhd,khd->hqk", query_blk, key_blk) * SCORE_SCALE
        scores = jnp.where(allowed[None], scores, MASKED_SCORE)
        largest = jnp.max(scores, axis=2, keepdims=True)
        unscaled = jnp.where(allowed[None], jnp.exp(scores - largest), 0.0)
        attn = unscaled / jnp.sum(unscaled, axis=2, keepdims=True)
        attn_low = rounded(attn)
        dattn = jnp.einsum("qhd,khd->hqk", grad_blk, value_blk)
        row_delta = jnp.sum(attn * dattn, axis=2, keepdims=True)
        dscores = rounded(attn * (dattn - row_delta))
        grad_q = jnp.einsum("hqk,khd->qhd", dscores, key_blk) * SCORE_SCALE
        grad_k = jnp.einsum("hqk,qhd->khd", dscores, query_blk) * SCORE_SCALE
        grad_v = jnp.einsum("hqk,qhd->khd", attn_low, grad_blk)
        key_acc = lax.dynamic_update_slice_in_dim(key_acc, lax.dynamic_slice_in_dim(key_acc, offset, key_span, 0) + grad_k, offset, 0)
        value_acc = lax.dynamic_update_slice_in_dim(value_acc, lax.dynamic_slice_in_dim(value_acc, offset, key_span, 0) + grad_v, offset, 0)
        return (key_acc, value_acc), grad_q.astype(jnp.bfloat16)

    zeros = jnp.zeros((length + WINDOW, HEADS, HEAD_DIM), jnp.float32)
    finals, query_blocks = lax.scan(one_block, (zeros, zeros), jnp.arange(length // MBLK, dtype=jnp.int32))
    grad_query = query_blocks.reshape(length, HEADS * HEAD_DIM)
    grad_key = finals[0][WINDOW:].reshape(length, KV_HEADS, group_size, HEAD_DIM).sum(axis=2)
    grad_value = finals[1][WINDOW:].reshape(length, KV_HEADS, group_size, HEAD_DIM).sum(axis=2)
    return (grad_query,
            grad_key.reshape(length, KV_HEADS * HEAD_DIM).astype(jnp.bfloat16),
            grad_value.reshape(length, KV_HEADS * HEAD_DIM).astype(jnp.bfloat16))


def reference(queries, key_rows, value_rows, arriving_grad, doc_blocks):
    out_grad = jnp.roll(arriving_grad, -1, axis=0)
    results = lax.map(section_grads, (queries, key_rows, value_rows, out_grad, doc_blocks))
    return (results[0], results[1], results[2])
```

```python
import jax
import jax.numpy as jnp
from jax import lax
from jax.sharding import PartitionSpec as P

HEADS = 32
KV_HEADS = 16
HEAD_DIM = 128
WINDOW = 1024
MBLK = 128
CHUNKS = 2


SCORE_SCALE = 168.0 ** (-0.5)
MASKED_SCORE = -1e30


def passed_along(value, axis, steps):
    count = lax.axis_size(axis)
    pairs = [(source, (source + steps) % count) for source in range(count)]
    return lax.ppermute(value, axis, pairs)


def moved(value, pairs):
    return lax.ppermute(value, "seq", pairs)


def allowed_mask(query_pos, query_doc, key_pos, key_doc):
    distance = query_pos[:, None] - key_pos[None, :]
    return (distance >= 0) & (distance < WINDOW) & (query_doc[:, None] == key_doc[None, :])


def grouped_grads(query_part, key_part, value_part, grad_part, allowed):
    scores = (
        jnp.einsum("tgrd,kgd->gtrk", query_part, key_part, preferred_element_type=jnp.float32)
        * SCORE_SCALE
    )
    visible = allowed[None, :, None, :]
    scores = jnp.where(visible, scores, MASKED_SCORE)
    largest = jnp.max(scores, axis=3, keepdims=True)
    unscaled = jnp.where(visible, jnp.exp(scores - largest), 0.0)
    attn = unscaled / jnp.sum(unscaled, axis=3, keepdims=True)
    attn_low = attn.astype(jnp.bfloat16)
    dattn = jnp.einsum("tgrd,kgd->gtrk", grad_part, value_part, preferred_element_type=jnp.float32)
    row_delta = jnp.sum(attn * dattn, axis=3, keepdims=True)
    dscores = (attn * (dattn - row_delta)).astype(jnp.bfloat16)
    grad_q = (
        jnp.einsum("gtrk,kgd->tgrd", dscores, key_part, preferred_element_type=jnp.float32)
        * SCORE_SCALE
    )
    grad_k = (
        jnp.einsum("gtrk,tgrd->kgd", dscores, query_part, preferred_element_type=jnp.float32)
        * SCORE_SCALE
    )
    grad_v = jnp.einsum("gtrk,tgrd->kgd", attn_low, grad_part, preferred_element_type=jnp.float32)
    return (grad_q, grad_k, grad_v)


class Routes:
    def __init__(self, count, reach):
        self.count = count
        self.reach = reach
        self.chips = reach // 2
        group_chip = lambda i: (i % reach) // 2
        self.hop = [(i, i + reach) for i in range(count - reach)]
        self.up = []
        self.down = []
        for e in range(1, self.chips):
            self.up.append([(i, i + 2 * e) for i in range(count) if group_chip(i) + e < self.chips])
            self.down.append(
                [(i, i + 2 * e - reach) for i in range(count) if group_chip(i) + e >= self.chips]
            )
        self.even_odd = [(i, i + 1) for i in range(0, count, 2)]
        self.odd_even = [(i + 1, i) for i in range(0, count, 2)]

    @staticmethod
    def reverse(pairs):
        return [(t, s) for (s, t) in pairs]


def gather_window(own, routes, chip_in_group, core):
    prev = moved(own, routes.hop)
    recv = []
    for e in range(1, routes.chips):
        up = moved(own, routes.up[e - 1])
        down = moved(prev, routes.down[e - 1])
        recv.append(jnp.where(chip_in_group >= e, up, down))
    to_odd = jnp.stack([own] + recv)
    to_even = jnp.stack(recv + [prev])
    sib = jnp.where(
        core == 0,
        moved(to_even, routes.odd_even),
        moved(to_odd, routes.even_odd),
    )
    ordered = [prev]
    for k in range(routes.chips - 1, -1, -1):
        ordered.append(sib[k])
        ordered.append(recv[k - 1] if k > 0 else own)
    return ordered


def scatter_window(parts, routes, chip_in_group, core):
    chips = routes.chips
    link = jnp.bfloat16
    prev = parts[0]
    own = parts[-1]
    recv = [parts[2 * (chips - e)] for e in range(1, chips)]
    sib = jnp.stack([parts[2 * chips - 1 - 2 * k] for k in range(chips)]).astype(link)
    from_odd = moved(sib, Routes.reverse(routes.even_odd)).astype(jnp.float32)
    from_even = moved(sib, Routes.reverse(routes.odd_even)).astype(jnp.float32)
    is_even = core == 0
    own = own + jnp.where(is_even, from_odd[0], 0.0)
    prev = prev + jnp.where(is_even, 0.0, from_even[chips - 1])
    for e in range(1, chips):
        recv[e - 1] = recv[e - 1] + jnp.where(is_even, from_odd[e], from_even[e - 1])
    for e in range(1, chips):
        sent = recv[e - 1].astype(link)
        own = own + moved(sent, Routes.reverse(routes.up[e - 1])).astype(jnp.float32)
        prev = prev + moved(sent, Routes.reverse(routes.down[e - 1])).astype(jnp.float32)
    own = own + moved(prev.astype(link), Routes.reverse(routes.hop)).astype(jnp.float32)
    return own


def local(queries, key_rows, value_rows, arriving_grad, doc_blocks):
    tokens = queries.shape[1]
    group_size = HEADS // KV_HEADS
    count = lax.axis_size("seq")
    grad_out = passed_along(arriving_grad, "pipe", -1)[0]
    token_doc = jnp.repeat(doc_blocks[0], MBLK)
    position = lax.axis_index("seq")
    reach_back = (WINDOW - 1) // tokens + 1
    assert reach_back % 2 == 0 and count % reach_back == 0 and WINDOW % tokens == 0
    routes = Routes(count, reach_back)
    chip_in_group = (position % reach_back) // 2
    core = position % 2
    key_count = (reach_back + 1) * tokens
    key_pos = (position - reach_back) * tokens + jnp.arange(key_count, dtype=jnp.int32)
    key_doc = jnp.where(key_pos >= 0, jnp.take(token_doc, jnp.maximum(key_pos, 0)), -1)
    query_pos = position * tokens + jnp.arange(tokens, dtype=jnp.int32)
    query_doc = lax.dynamic_slice_in_dim(token_doc, position * tokens, tokens, 0)
    allowed = allowed_mask(query_pos, query_doc, key_pos, key_doc)
    query4 = queries[0].reshape(tokens, KV_HEADS, group_size, HEAD_DIM)
    grad4 = grad_out.reshape(tokens, KV_HEADS, group_size, HEAD_DIM)
    heads_per = KV_HEADS // CHUNKS
    width = heads_per * HEAD_DIM
    query_parts, key_parts, value_parts = [], [], []
    for chunk in range(CHUNKS):
        lower = chunk * heads_per
        upper = lower + heads_per
        packed = jnp.stack(
            [key_rows[0][:, lower * HEAD_DIM : upper * HEAD_DIM],
             value_rows[0][:, lower * HEAD_DIM : upper * HEAD_DIM]]
        )
        window = gather_window(packed, routes, chip_in_group, core)
        gathered = jnp.concatenate(window, axis=1)
        key4 = gathered[0].reshape(key_count, heads_per, HEAD_DIM)
        value4 = gathered[1].reshape(key_count, heads_per, HEAD_DIM)
        grad_q, grad_k, grad_v = grouped_grads(
            query4[:, lower:upper], key4, value4, grad4[:, lower:upper], allowed
        )
        query_parts.append(grad_q)
        partial = jnp.stack([grad_k, grad_v]).reshape(2, key_count, width)
        parts = [partial[:, k * tokens : (k + 1) * tokens] for k in range(reach_back + 1)]
        summed = scatter_window(parts, routes, chip_in_group, core)
        key_parts.append(summed[0])
        value_parts.append(summed[1])
    grad_query = jnp.concatenate(query_parts, axis=1).reshape(tokens, HEADS * HEAD_DIM)
    grad_key = jnp.concatenate(key_parts, axis=1)
    grad_value = jnp.concatenate(value_parts, axis=1)
    return (
        grad_query.astype(jnp.bfloat16)[None],
        grad_key.astype(jnp.bfloat16)[None],
        grad_value.astype(jnp.bfloat16)[None],
    )


def solution(mesh):
    placed = (
        P("pipe", "seq", None),
        P("pipe", "seq", None),
        P("pipe", "seq", None),
        P("pipe", "seq", None),
        P("pipe", None),
    )
    return jax.shard_map(
        local,
        mesh=mesh,
        in_specs=placed,
        out_specs=(P("pipe", "seq", None), P("pipe", "seq", None), P("pipe", "seq", None)),
        check_vma=False,
    )
```

```python
import jax
import jax.numpy as jnp
from jax import lax
from jax.experimental import pallas as pl
from jax.sharding import PartitionSpec as P

HEADS = 32
KV_HEADS = 16
HEAD_DIM = 128
WINDOW = 1024
MBLK = 128
CHUNKS = 1


SCORE_SCALE = 168.0 ** (-0.5)
MASKED_SCORE = -1e30


def passed_along(value, axis, steps):
    count = lax.axis_size(axis)
    pairs = [(source, (source + steps) % count) for source in range(count)]
    return lax.ppermute(value, axis, pairs)


def moved(value, pairs):
    return lax.ppermute(value, "seq", pairs)


def allowed_mask(query_pos, query_doc, key_pos, key_doc):
    distance = query_pos[:, None] - key_pos[None, :]
    return (distance >= 0) & (distance < WINDOW) & (query_doc[:, None] == key_doc[None, :])


def attention_kernel(mask_ref, q_ref, do_ref, k_ref, v_ref, dq_ref, dk_ref, dv_ref):
    tokens = q_ref.shape[0]
    visible = mask_ref[...] > 0.0
    visible = jnp.concatenate([visible, visible], axis=0)
    q = q_ref[...]
    do = do_ref[...]
    qs = jnp.concatenate([q[:, :HEAD_DIM], q[:, HEAD_DIM:]], axis=0)
    dos = jnp.concatenate([do[:, :HEAD_DIM], do[:, HEAD_DIM:]], axis=0)
    k = k_ref[...]
    v = v_ref[...]
    contract_last = (((1,), (1,)), ((), ()))
    contract_first = (((0,), (0,)), ((), ()))
    scores = lax.dot_general(qs, k, contract_last, preferred_element_type=jnp.float32) * SCORE_SCALE
    scores = jnp.where(visible, scores, MASKED_SCORE)
    largest = jnp.max(scores, axis=1, keepdims=True)
    unscaled = jnp.where(visible, jnp.exp(scores - largest), 0.0)
    attn = unscaled * (1.0 / jnp.sum(unscaled, axis=1, keepdims=True))
    dattn = lax.dot_general(dos, v, contract_last, preferred_element_type=jnp.float32)
    row_delta = jnp.sum(attn * dattn, axis=1, keepdims=True)
    dscores = (attn * (dattn - row_delta)).astype(jnp.bfloat16)
    grad_q = jnp.dot(dscores, k, preferred_element_type=jnp.float32) * SCORE_SCALE
    dq_ref[:, :HEAD_DIM] = grad_q[:tokens].astype(dq_ref.dtype)
    dq_ref[:, HEAD_DIM:] = grad_q[tokens:].astype(dq_ref.dtype)
    dk_ref[...] = (
        lax.dot_general(dscores, qs, contract_first, preferred_element_type=jnp.float32)
        * SCORE_SCALE
    )
    dv_ref[...] = lax.dot_general(
        attn.astype(jnp.bfloat16), dos, contract_first, preferred_element_type=jnp.float32
    )


def attention_grads(mask, queries, grad_out, keys, values):
    tokens = queries.shape[0]
    key_count = keys.shape[0]
    heads = keys.shape[1] // HEAD_DIM
    pair = 2 * HEAD_DIM
    flops = 2 * 5 * (2 * tokens) * key_count * HEAD_DIM * heads
    moved_bytes = 2 * (3 * queries.size + 2 * keys.size) + 8 * keys.size + mask.size * 4
    return pl.pallas_call(
        attention_kernel,
        grid=(heads,),
        in_specs=[
            pl.BlockSpec((tokens, key_count), lambda g: (0, 0)),
            pl.BlockSpec((tokens, pair), lambda g: (0, g)),
            pl.BlockSpec((tokens, pair), lambda g: (0, g)),
            pl.BlockSpec((key_count, HEAD_DIM), lambda g: (0, g)),
            pl.BlockSpec((key_count, HEAD_DIM), lambda g: (0, g)),
        ],
        out_specs=[
            pl.BlockSpec((tokens, pair), lambda g: (0, g)),
            pl.BlockSpec((key_count, HEAD_DIM), lambda g: (0, g)),
            pl.BlockSpec((key_count, HEAD_DIM), lambda g: (0, g)),
        ],
        out_shape=[
            jax.ShapeDtypeStruct(queries.shape, jnp.bfloat16),
            jax.ShapeDtypeStruct(keys.shape, jnp.float32),
            jax.ShapeDtypeStruct(keys.shape, jnp.float32),
        ],
        cost_estimate=pl.CostEstimate(
            flops=flops, transcendentals=2 * tokens * key_count * heads, bytes_accessed=moved_bytes
        ),
    )(mask, queries, grad_out, keys, values)


class Routes:
    def __init__(self, count, reach):
        self.count = count
        self.reach = reach
        self.chips = reach // 2
        group_chip = lambda i: (i % reach) // 2
        self.hop = [(i, i + reach) for i in range(count - reach)]
        self.up = []
        self.down = []
        for e in range(1, self.chips):
            self.up.append([(i, i + 2 * e) for i in range(count) if group_chip(i) + e < self.chips])
            self.down.append(
                [(i, i + 2 * e - reach) for i in range(count) if group_chip(i) + e >= self.chips]
            )
        self.even_odd = [(i, i + 1) for i in range(0, count, 2)]
        self.odd_even = [(i + 1, i) for i in range(0, count, 2)]

    @staticmethod
    def reverse(pairs):
        return [(t, s) for (s, t) in pairs]


def gather_window(own, routes, chip_in_group, core):
    prev = moved(own, routes.hop)
    recv = []
    for e in range(1, routes.chips):
        sent = jnp.where(chip_in_group + e < routes.chips, own, prev)
        recv.append(moved(sent, routes.up[e - 1] + routes.down[e - 1]))
    stacked = jnp.stack([own] + recv + [prev])
    sent = lax.dynamic_slice_in_dim(stacked, core, routes.chips, 0)
    sib = moved(sent, routes.even_odd + routes.odd_even)
    ordered = [prev]
    for k in range(routes.chips - 1, -1, -1):
        ordered.append(sib[k])
        ordered.append(recv[k - 1] if k > 0 else own)
    return ordered


def scatter_window(parts, routes, chip_in_group, core):
    chips = routes.chips
    link = jnp.bfloat16
    prev = parts[0]
    own = parts[-1]
    recv = [parts[2 * (chips - e)] for e in range(1, chips)]
    sib = jnp.stack([parts[2 * chips - 1 - 2 * k] for k in range(chips)]).astype(link)
    back = moved(sib, routes.even_odd + routes.odd_even).astype(jnp.float32)
    is_even = core == 0
    own = own + jnp.where(is_even, back[0], 0.0)
    prev = prev + jnp.where(is_even, 0.0, back[chips - 1])
    for e in range(1, chips):
        recv[e - 1] = recv[e - 1] + jnp.where(is_even, back[e], back[e - 1])
    for e in range(1, chips):
        pairs = Routes.reverse(routes.up[e - 1] + routes.down[e - 1])
        got = moved(recv[e - 1].astype(link), pairs).astype(jnp.float32)
        upward = chip_in_group + e < chips
        own = own + jnp.where(upward, got, 0.0)
        prev = prev + jnp.where(upward, 0.0, got)
    own = own + moved(prev.astype(link), Routes.reverse(routes.hop)).astype(jnp.float32)
    return own


def local(queries, key_rows, value_rows, arriving_grad, doc_blocks):
    tokens = queries.shape[1]
    group_size = HEADS // KV_HEADS
    count = lax.axis_size("seq")
    grad_out = passed_along(arriving_grad, "pipe", -1)[0]
    token_doc = jnp.repeat(doc_blocks[0], MBLK)
    position = lax.axis_index("seq")
    reach_back = (WINDOW - 1) // tokens + 1
    assert reach_back % 2 == 0 and count % reach_back == 0 and WINDOW % tokens == 0
    routes = Routes(count, reach_back)
    chip_in_group = (position % reach_back) // 2
    core = position % 2
    key_count = (reach_back + 1) * tokens
    key_pos = (position - reach_back) * tokens + jnp.arange(key_count, dtype=jnp.int32)
    key_doc = jnp.where(key_pos >= 0, jnp.take(token_doc, jnp.maximum(key_pos, 0)), -1)
    query_pos = position * tokens + jnp.arange(tokens, dtype=jnp.int32)
    query_doc = lax.dynamic_slice_in_dim(token_doc, position * tokens, tokens, 0)
    allowed = allowed_mask(query_pos, query_doc, key_pos, key_doc)
    mask = allowed.astype(jnp.float32)
    heads_per = KV_HEADS // CHUNKS
    width = heads_per * HEAD_DIM
    query_parts, key_parts, value_parts = [], [], []
    for chunk in range(CHUNKS):
        keys = slice(chunk * width, (chunk + 1) * width)
        pairs = slice(chunk * group_size * width, (chunk + 1) * group_size * width)
        packed = jnp.stack([key_rows[0][:, keys], value_rows[0][:, keys]])
        window = gather_window(packed, routes, chip_in_group, core)
        gathered = jnp.concatenate(window, axis=1)
        grad_q, grad_k, grad_v = attention_grads(
            mask, queries[0][:, pairs], grad_out[:, pairs], gathered[0], gathered[1]
        )
        query_parts.append(grad_q)
        partial = jnp.stack([grad_k, grad_v])
        parts = [partial[:, k * tokens : (k + 1) * tokens] for k in range(reach_back + 1)]
        summed = scatter_window(parts, routes, chip_in_group, core)
        key_parts.append(summed[0])
        value_parts.append(summed[1])
    grad_query = jnp.concatenate(query_parts, axis=1)
    grad_key = jnp.concatenate(key_parts, axis=1)
    grad_value = jnp.concatenate(value_parts, axis=1)
    return (
        grad_query.astype(jnp.bfloat16)[None],
        grad_key.astype(jnp.bfloat16)[None],
        grad_value.astype(jnp.bfloat16)[None],
    )


def solution(mesh):
    placed = (
        P("pipe", "seq", None),
        P("pipe", "seq", None),
        P("pipe", "seq", None),
        P("pipe", "seq", None),
        P("pipe", None),
    )
    return jax.shard_map(
        local,
        mesh=mesh,
        in_specs=placed,
        out_specs=(P("pipe", "seq", None), P("pipe", "seq", None), P("pipe", "seq", None)),
        check_vma=False,
    )
```

```python
import jax
import jax.numpy as jnp
from jax import lax
from jax.experimental import pallas as pl
from jax.sharding import PartitionSpec as P

HEADS = 32
KV_HEADS = 16
HEAD_DIM = 128
WINDOW = 1024
MBLK = 128


SCORE_SCALE = 168.0 ** (-0.5)
MASKED_SCORE = -1e30


def passed_along(value, axis, steps):
    count = lax.axis_size(axis)
    pairs = [(source, (source + steps) % count) for source in range(count)]
    return lax.ppermute(value, axis, pairs)


def moved(value, pairs):
    return lax.ppermute(value, "seq", pairs)


def reverse(pairs):
    return [(t, s) for (s, t) in pairs]


class Routes:
    def __init__(self, count, reach):
        self.reach = reach
        self.chips = reach // 2
        group_chip = lambda i: (i % reach) // 2
        self.hop = [(i, i + reach) for i in range(count - reach)]
        self.up = []
        self.down = []
        for e in range(1, self.chips):
            self.up.append([(i, i + 2 * e) for i in range(count) if group_chip(i) + e < self.chips])
            self.down.append(
                [(i, i + 2 * e - reach) for i in range(count) if group_chip(i) + e >= self.chips]
            )
        self.sibling = [(i, i ^ 1) for i in range(count)]


def gather_window(own, routes, chip_in_group, core):
    prev = moved(own, routes.hop)
    direct = [own]
    for e in range(1, routes.chips):
        up = moved(own, routes.up[e - 1])
        down = moved(prev, routes.down[e - 1])
        direct.append(jnp.where(chip_in_group >= e, up, down))
    later = direct[1:] + [prev]
    sent = jnp.where(core == 0, jnp.stack(direct), jnp.stack(later))
    sib = moved(sent, routes.sibling)
    return prev, direct, sib


def scatter_window(prev, direct, sib, routes, chip_in_group, core):
    chips = routes.chips
    link = jnp.bfloat16
    back = moved(sib, routes.sibling).astype(jnp.float32)
    is_even = core == 0
    own = direct[0] + jnp.where(is_even, back[0], 0.0)
    prev = prev + jnp.where(is_even, 0.0, back[chips - 1])
    sums = [direct[e] + jnp.where(is_even, back[e], back[e - 1]) for e in range(1, chips)]
    for e in range(1, chips):
        sent = sums[e - 1].astype(link)
        prev = prev + moved(sent, reverse(routes.down[e - 1])).astype(jnp.float32)
    for e in range(1, chips):
        sent = sums[e - 1].astype(link)
        own = own + moved(sent, reverse(routes.up[e - 1])).astype(jnp.float32)
    own = own + moved(prev.astype(link), reverse(routes.hop)).astype(jnp.float32)
    return own


def attention_kernel(chips, mask_ref, q_ref, do_ref, prev_ref, *refs):
    direct_refs = refs[:chips]
    sib_ref = refs[chips]
    dq_ref, dprev_ref = refs[chips + 1], refs[chips + 2]
    ddirect_refs = refs[chips + 3 : 2 * chips + 3]
    dsib_ref = refs[2 * chips + 3]
    tokens = q_ref.shape[0]
    blocks = [prev_ref]
    for k in range(chips - 1, -1, -1):
        blocks.append(sib_ref.at[k])
        blocks.append(direct_refs[k])
    k = jnp.concatenate([b[0] for b in blocks], axis=0)
    v = jnp.concatenate([b[1] for b in blocks], axis=0)
    visible = mask_ref[...] > 0.0
    visible = jnp.concatenate([visible, visible], axis=0)
    q = q_ref[...]
    do = do_ref[...]
    qs = jnp.concatenate([q[:, :HEAD_DIM], q[:, HEAD_DIM:]], axis=0)
    dos = jnp.concatenate([do[:, :HEAD_DIM], do[:, HEAD_DIM:]], axis=0)
    contract_last = (((1,), (1,)), ((), ()))
    contract_first = (((0,), (0,)), ((), ()))
    scores = lax.dot_general(qs, k, contract_last, preferred_element_type=jnp.float32) * SCORE_SCALE
    scores = jnp.where(visible, scores, MASKED_SCORE)
    largest = jnp.max(scores, axis=1, keepdims=True)
    unscaled = jnp.where(visible, jnp.exp(scores - largest), 0.0)
    attn = unscaled * (1.0 / jnp.sum(unscaled, axis=1, keepdims=True))
    dattn = lax.dot_general(dos, v, contract_last, preferred_element_type=jnp.float32)
    row_delta = jnp.sum(attn * dattn, axis=1, keepdims=True)
    dscores = (attn * (dattn - row_delta)).astype(jnp.bfloat16)
    grad_q = jnp.dot(dscores, k, preferred_element_type=jnp.float32) * SCORE_SCALE
    dq_ref[:, :HEAD_DIM] = grad_q[:tokens].astype(dq_ref.dtype)
    dq_ref[:, HEAD_DIM:] = grad_q[tokens:].astype(dq_ref.dtype)
    grad_k = (
        lax.dot_general(dscores, qs, contract_first, preferred_element_type=jnp.float32)
        * SCORE_SCALE
    )
    grad_v = lax.dot_general(
        attn.astype(jnp.bfloat16), dos, contract_first, preferred_element_type=jnp.float32
    )
    outs = [dprev_ref]
    for kk in range(chips - 1, -1, -1):
        outs.append(dsib_ref.at[kk])
        outs.append(ddirect_refs[kk])
    for j, out in enumerate(outs):
        rows = slice(j * tokens, (j + 1) * tokens)
        out[0] = grad_k[rows].astype(out.dtype)
        out[1] = grad_v[rows].astype(out.dtype)


def attention_grads(mask, queries, grad_out, prev, direct, sib):
    tokens = queries.shape[0]
    chips = len(direct)
    key_count = mask.shape[1]
    width = prev.shape[2]
    heads = width // HEAD_DIM
    pair = 2 * HEAD_DIM
    block = pl.BlockSpec((2, tokens, HEAD_DIM), lambda g: (0, 0, g))
    sib_block = pl.BlockSpec((chips, 2, tokens, HEAD_DIM), lambda g: (0, 0, 0, g))
    pair_block = pl.BlockSpec((tokens, pair), lambda g: (0, g))
    part = jax.ShapeDtypeStruct(prev.shape, jnp.float32)
    flops = 2 * 5 * (2 * tokens) * key_count * HEAD_DIM * heads
    moved_bytes = 2 * 3 * queries.size + 2 * 2 * key_count * width * 3 + mask.size * 4
    return pl.pallas_call(
        lambda *refs: attention_kernel(chips, *refs),
        grid=(heads,),
        in_specs=[pl.BlockSpec((tokens, key_count), lambda g: (0, 0)), pair_block, pair_block]
        + [block] * (chips + 1)
        + [sib_block],
        out_specs=[pair_block] + [block] * (chips + 1) + [sib_block],
        out_shape=[jax.ShapeDtypeStruct(queries.shape, jnp.bfloat16)]
        + [part] * (chips + 1)
        + [jax.ShapeDtypeStruct(sib.shape, jnp.bfloat16)],
        cost_estimate=pl.CostEstimate(
            flops=flops, transcendentals=2 * tokens * key_count * heads, bytes_accessed=moved_bytes
        ),
    )(mask, queries, grad_out, prev, *direct, sib)


def local(queries, key_rows, value_rows, arriving_grad, doc_blocks):
    tokens = queries.shape[1]
    count = lax.axis_size("seq")
    grad_out = passed_along(arriving_grad, "pipe", -1)[0]
    position = lax.axis_index("seq")
    reach_back = (WINDOW - 1) // tokens + 1
    assert reach_back % 2 == 0 and count % reach_back == 0 and WINDOW % tokens == 0
    routes = Routes(count, reach_back)
    chip_in_group = (position % reach_back) // 2
    core = position % 2
    key_count = (reach_back + 1) * tokens
    token_doc = jnp.repeat(doc_blocks[0], MBLK)
    doc_pad = jnp.concatenate([jnp.full((reach_back * tokens,), -1, jnp.int32), token_doc])
    key_doc = lax.dynamic_slice_in_dim(doc_pad, position * tokens, key_count, 0)
    key_pos = (position - reach_back) * tokens + jnp.arange(key_count, dtype=jnp.int32)
    query_pos = position * tokens + jnp.arange(tokens, dtype=jnp.int32)
    query_doc = lax.dynamic_slice_in_dim(token_doc, position * tokens, tokens, 0)
    distance = query_pos[:, None] - key_pos[None, :]
    allowed = (distance >= 0) & (distance < WINDOW) & (query_doc[:, None] == key_doc[None, :])
    mask = allowed.astype(jnp.float32)
    packed = jnp.stack([key_rows[0], value_rows[0]])
    prev, direct, sib = gather_window(packed, routes, chip_in_group, core)
    outs = attention_grads(mask, queries[0], grad_out, prev, direct, sib)
    grad_query, dprev, ddirect, dsib = outs[0], outs[1], outs[2 : 2 + routes.chips], outs[-1]
    summed = scatter_window(dprev, ddirect, dsib, routes, chip_in_group, core)
    return (
        grad_query[None],
        summed[0].astype(jnp.bfloat16)[None],
        summed[1].astype(jnp.bfloat16)[None],
    )


def solution(mesh):
    placed = (
        P("pipe", "seq", None),
        P("pipe", "seq", None),
        P("pipe", "seq", None),
        P("pipe", "seq", None),
        P("pipe", None),
    )
    return jax.shard_map(
        local,
        mesh=mesh,
        in_specs=placed,
        out_specs=(P("pipe", "seq", None), P("pipe", "seq", None), P("pipe", "seq", None)),
        check_vma=False,
    )
```

```python
import jax
import jax.numpy as jnp
from jax import lax
from jax.experimental import pallas as pl
from jax.sharding import PartitionSpec as P

HEADS = 32
KV_HEADS = 16
HEAD_DIM = 128
WINDOW = 1024
MBLK = 128
CHUNKS = 2


SCORE_SCALE = 168.0 ** (-0.5)
MASKED_SCORE = -1e30


def passed_along(value, axis, steps):
    count = lax.axis_size(axis)
    pairs = [(source, (source + steps) % count) for source in range(count)]
    return lax.ppermute(value, axis, pairs)


def moved(value, pairs):
    return lax.ppermute(value, "seq", pairs)


def reverse(pairs):
    return [(t, s) for (s, t) in pairs]


class Routes:
    def __init__(self, count, reach):
        self.reach = reach
        self.chips = reach // 2
        group_chip = lambda i: (i % reach) // 2
        self.hop = [(i, i + reach) for i in range(count - reach)]
        self.up = []
        self.down = []
        for e in range(1, self.chips):
            self.up.append([(i, i + 2 * e) for i in range(count) if group_chip(i) + e < self.chips])
            self.down.append(
                [(i, i + 2 * e - reach) for i in range(count) if group_chip(i) + e >= self.chips]
            )
        self.sibling = [(i, i ^ 1) for i in range(count)]


def gather_window(own, routes, chip_in_group, core):
    prev = moved(own, routes.hop)
    direct = [own]
    for e in range(1, routes.chips):
        up = moved(own, routes.up[e - 1])
        down = moved(prev, routes.down[e - 1])
        direct.append(jnp.where(chip_in_group >= e, up, down))
    later = direct[1:] + [prev]
    sent = jnp.where(core == 0, jnp.stack(direct), jnp.stack(later))
    sib = moved(sent, routes.sibling)
    return prev, direct, sib


def scatter_window(prev, direct, sib, routes, chip_in_group, core):
    chips = routes.chips
    link = jnp.bfloat16
    back = moved(sib, routes.sibling).astype(jnp.float32)
    is_even = core == 0
    own = direct[0] + jnp.where(is_even, back[0], 0.0)
    prev = prev + jnp.where(is_even, 0.0, back[chips - 1])
    sums = [direct[e] + jnp.where(is_even, back[e], back[e - 1]) for e in range(1, chips)]
    for e in range(1, chips):
        sent = sums[e - 1].astype(link)
        prev = prev + moved(sent, reverse(routes.down[e - 1])).astype(jnp.float32)
    for e in range(1, chips):
        sent = sums[e - 1].astype(link)
        own = own + moved(sent, reverse(routes.up[e - 1])).astype(jnp.float32)
    own = own + moved(prev.astype(link), reverse(routes.hop)).astype(jnp.float32)
    return own


def attention_kernel(chips, mask_ref, q_ref, do_ref, prev_ref, *refs):
    direct_refs = refs[:chips]
    sib_ref = refs[chips]
    dq_ref, dprev_ref = refs[chips + 1], refs[chips + 2]
    ddirect_refs = refs[chips + 3 : 2 * chips + 3]
    dsib_ref = refs[2 * chips + 3]
    tokens = q_ref.shape[0]
    blocks = [prev_ref]
    for k in range(chips - 1, -1, -1):
        blocks.append(sib_ref.at[k])
        blocks.append(direct_refs[k])
    k = jnp.concatenate([b[0] for b in blocks], axis=0)
    v = jnp.concatenate([b[1] for b in blocks], axis=0)
    visible = mask_ref[...] > 0.0
    visible = jnp.concatenate([visible, visible], axis=0)
    q = q_ref[...]
    do = do_ref[...]
    qs = jnp.concatenate([q[:, :HEAD_DIM], q[:, HEAD_DIM:]], axis=0)
    dos = jnp.concatenate([do[:, :HEAD_DIM], do[:, HEAD_DIM:]], axis=0)
    contract_last = (((1,), (1,)), ((), ()))
    contract_first = (((0,), (0,)), ((), ()))
    scores = lax.dot_general(qs, k, contract_last, preferred_element_type=jnp.float32) * SCORE_SCALE
    scores = jnp.where(visible, scores, MASKED_SCORE)
    largest = jnp.max(scores, axis=1, keepdims=True)
    unscaled = jnp.where(visible, jnp.exp(scores - largest), 0.0)
    attn = unscaled * (1.0 / jnp.sum(unscaled, axis=1, keepdims=True))
    dattn = lax.dot_general(dos, v, contract_last, preferred_element_type=jnp.float32)
    row_delta = jnp.sum(attn * dattn, axis=1, keepdims=True)
    dscores = (attn * (dattn - row_delta)).astype(jnp.bfloat16)
    grad_q = jnp.dot(dscores, k, preferred_element_type=jnp.float32) * SCORE_SCALE
    dq_ref[:, :HEAD_DIM] = grad_q[:tokens].astype(dq_ref.dtype)
    dq_ref[:, HEAD_DIM:] = grad_q[tokens:].astype(dq_ref.dtype)
    grad_k = (
        lax.dot_general(dscores, qs, contract_first, preferred_element_type=jnp.float32)
        * SCORE_SCALE
    )
    grad_v = lax.dot_general(
        attn.astype(jnp.bfloat16), dos, contract_first, preferred_element_type=jnp.float32
    )
    outs = [dprev_ref]
    for kk in range(chips - 1, -1, -1):
        outs.append(dsib_ref.at[kk])
        outs.append(ddirect_refs[kk])
    for j, out in enumerate(outs):
        rows = slice(j * tokens, (j + 1) * tokens)
        out[0] = grad_k[rows].astype(out.dtype)
        out[1] = grad_v[rows].astype(out.dtype)


def attention_grads(mask, queries, grad_out, prev, direct, sib):
    tokens = queries.shape[0]
    chips = len(direct)
    key_count = mask.shape[1]
    width = prev.shape[2]
    heads = width // HEAD_DIM
    pair = 2 * HEAD_DIM
    block = pl.BlockSpec((2, tokens, HEAD_DIM), lambda g: (0, 0, g))
    sib_block = pl.BlockSpec((chips, 2, tokens, HEAD_DIM), lambda g: (0, 0, 0, g))
    pair_block = pl.BlockSpec((tokens, pair), lambda g: (0, g))
    part = jax.ShapeDtypeStruct(prev.shape, jnp.float32)
    flops = 2 * 5 * (2 * tokens) * key_count * HEAD_DIM * heads
    moved_bytes = 2 * 3 * queries.size + 2 * 2 * key_count * width * 3 + mask.size * 4
    return pl.pallas_call(
        lambda *refs: attention_kernel(chips, *refs),
        grid=(heads,),
        in_specs=[pl.BlockSpec((tokens, key_count), lambda g: (0, 0)), pair_block, pair_block]
        + [block] * (chips + 1)
        + [sib_block],
        out_specs=[pair_block] + [block] * (chips + 1) + [sib_block],
        out_shape=[jax.ShapeDtypeStruct(queries.shape, jnp.bfloat16)]
        + [part] * (chips + 1)
        + [jax.ShapeDtypeStruct(sib.shape, jnp.bfloat16)],
        cost_estimate=pl.CostEstimate(
            flops=flops, transcendentals=2 * tokens * key_count * heads, bytes_accessed=moved_bytes
        ),
    )(mask, queries, grad_out, prev, *direct, sib)


def local(queries, key_rows, value_rows, arriving_grad, doc_blocks):
    tokens = queries.shape[1]
    count = lax.axis_size("seq")
    grad_out = passed_along(arriving_grad, "pipe", -1)[0]
    position = lax.axis_index("seq")
    reach_back = (WINDOW - 1) // tokens + 1
    assert reach_back % 2 == 0 and count % reach_back == 0 and WINDOW % tokens == 0
    routes = Routes(count, reach_back)
    chip_in_group = (position % reach_back) // 2
    core = position % 2
    key_count = (reach_back + 1) * tokens
    token_doc = jnp.repeat(doc_blocks[0], MBLK)
    doc_pad = jnp.concatenate([jnp.full((reach_back * tokens,), -1, jnp.int32), token_doc])
    key_doc = lax.dynamic_slice_in_dim(doc_pad, position * tokens, key_count, 0)
    key_pos = (position - reach_back) * tokens + jnp.arange(key_count, dtype=jnp.int32)
    query_pos = position * tokens + jnp.arange(tokens, dtype=jnp.int32)
    query_doc = lax.dynamic_slice_in_dim(token_doc, position * tokens, tokens, 0)
    distance = query_pos[:, None] - key_pos[None, :]
    allowed = (distance >= 0) & (distance < WINDOW) & (query_doc[:, None] == key_doc[None, :])
    mask = allowed.astype(jnp.float32)
    width = KV_HEADS * HEAD_DIM // CHUNKS
    query_parts, key_parts, value_parts = [], [], []
    for chunk in range(CHUNKS):
        keys = slice(chunk * width, (chunk + 1) * width)
        pairs = slice(2 * chunk * width, 2 * (chunk + 1) * width)
        packed = jnp.stack([key_rows[0][:, keys], value_rows[0][:, keys]])
        if chunk > 0:
            packed, _ = lax.optimization_barrier((packed, outs[0]))
        prev, direct, sib = gather_window(packed, routes, chip_in_group, core)
        if chunk > 0:
            (prev, direct, sib), _ = lax.optimization_barrier(((prev, direct, sib), summed))
        outs = attention_grads(mask, queries[0][:, pairs], grad_out[:, pairs], prev, direct, sib)
        dprev, ddirect, dsib = outs[1], outs[2 : 2 + routes.chips], outs[-1]
        summed = scatter_window(dprev, ddirect, dsib, routes, chip_in_group, core)
        query_parts.append(outs[0])
        key_parts.append(summed[0].astype(jnp.bfloat16))
        value_parts.append(summed[1].astype(jnp.bfloat16))
    return (
        jnp.concatenate(query_parts, axis=1)[None],
        jnp.concatenate(key_parts, axis=1)[None],
        jnp.concatenate(value_parts, axis=1)[None],
    )


def solution(mesh):
    placed = (
        P("pipe", "seq", None),
        P("pipe", "seq", None),
        P("pipe", "seq", None),
        P("pipe", "seq", None),
        P("pipe", None),
    )
    return jax.shard_map(
        local,
        mesh=mesh,
        in_specs=placed,
        out_specs=(P("pipe", "seq", None), P("pipe", "seq", None), P("pipe", "seq", None)),
        check_vma=False,
    )
```

```python
import jax
import jax.numpy as jnp
from jax import lax
from jax.experimental import pallas as pl
from jax.sharding import PartitionSpec as P

HEADS = 32
KV_HEADS = 16
HEAD_DIM = 128
WINDOW = 1024
MBLK = 128
CHUNKS = 1


SCORE_SCALE = 168.0 ** (-0.5)
MASKED_SCORE = -1e30


def passed_along(value, axis, steps):
    count = lax.axis_size(axis)
    pairs = [(source, (source + steps) % count) for source in range(count)]
    return lax.ppermute(value, axis, pairs)


def moved(value, pairs):
    return lax.ppermute(value, "seq", pairs)


def reverse(pairs):
    return [(t, s) for (s, t) in pairs]


class Routes:
    def __init__(self, count, reach):
        self.reach = reach
        self.chips = reach // 2
        group_chip = lambda i: (i % reach) // 2
        self.hop = [(i, i + reach) for i in range(count - reach)]
        self.up = []
        self.down = []
        for e in range(1, self.chips):
            self.up.append([(i, i + 2 * e) for i in range(count) if group_chip(i) + e < self.chips])
            self.down.append(
                [(i, i + 2 * e - reach) for i in range(count) if group_chip(i) + e >= self.chips]
            )
        self.sibling = [(i, i ^ 1) for i in range(count)]


def gather_window(own, routes, chip_in_group, core):
    prev = moved(own, routes.hop)
    direct = [own]
    for e in range(1, routes.chips):
        up = moved(own, routes.up[e - 1])
        down = moved(prev, routes.down[e - 1])
        direct.append(jnp.where(chip_in_group >= e, up, down))
    later = direct[1:] + [prev]
    sent = jnp.where(core == 0, jnp.stack(direct), jnp.stack(later))
    sib = moved(sent, routes.sibling)
    return prev, direct, sib


def scatter_window(prev, direct, sib, routes, chip_in_group, core):
    chips = routes.chips
    link = jnp.bfloat16
    back = moved(sib, routes.sibling).astype(jnp.float32)
    is_even = core == 0
    own = direct[0] + jnp.where(is_even, back[0], 0.0)
    prev = prev + jnp.where(is_even, 0.0, back[chips - 1])
    sums = [direct[e] + jnp.where(is_even, back[e], back[e - 1]) for e in range(1, chips)]
    for e in range(1, chips):
        sent = sums[e - 1].astype(link)
        prev = prev + moved(sent, reverse(routes.down[e - 1])).astype(jnp.float32)
    for e in range(1, chips):
        sent = sums[e - 1].astype(link)
        own = own + moved(sent, reverse(routes.up[e - 1])).astype(jnp.float32)
    own = own + moved(prev.astype(link), reverse(routes.hop)).astype(jnp.float32)
    return own


def attention_kernel(chips, mask_ref, q_ref, do_ref, prev_ref, *refs):
    direct_refs = refs[:chips]
    sib_ref = refs[chips]
    dq_ref, dprev_ref = refs[chips + 1], refs[chips + 2]
    ddirect_refs = refs[chips + 3 : 2 * chips + 3]
    dsib_ref = refs[2 * chips + 3]
    tokens = q_ref.shape[0]
    blocks = [prev_ref]
    for k in range(chips - 1, -1, -1):
        blocks.append(sib_ref.at[k])
        blocks.append(direct_refs[k])
    k = jnp.concatenate([b[0] for b in blocks], axis=0)
    v = jnp.concatenate([b[1] for b in blocks], axis=0)
    visible = mask_ref[...] > 0.0
    visible = jnp.concatenate([visible, visible], axis=1)
    q = q_ref[...]
    do = do_ref[...]
    qs = jnp.concatenate([q[:, :HEAD_DIM], q[:, HEAD_DIM:]], axis=0)
    dos = jnp.concatenate([do[:, :HEAD_DIM], do[:, HEAD_DIM:]], axis=0)
    contract_last = (((1,), (1,)), ((), ()))
    contract_first = (((0,), (0,)), ((), ()))
    scores = lax.dot_general(k, qs, contract_last, preferred_element_type=jnp.float32) * SCORE_SCALE
    scores = jnp.where(visible, scores, MASKED_SCORE)
    largest = jnp.max(scores, axis=0, keepdims=True)
    unscaled = jnp.where(visible, jnp.exp(scores - largest), 0.0)
    attn = unscaled * (1.0 / jnp.sum(unscaled, axis=0, keepdims=True))
    dattn = lax.dot_general(v, dos, contract_last, preferred_element_type=jnp.float32)
    row_delta = jnp.sum(attn * dattn, axis=0, keepdims=True)
    dscores = (attn * (dattn - row_delta)).astype(jnp.bfloat16)
    grad_q = (
        lax.dot_general(dscores, k, contract_first, preferred_element_type=jnp.float32)
        * SCORE_SCALE
    )
    dq_ref[:, :HEAD_DIM] = grad_q[:tokens].astype(dq_ref.dtype)
    dq_ref[:, HEAD_DIM:] = grad_q[tokens:].astype(dq_ref.dtype)
    grad_k = jnp.dot(dscores, qs, preferred_element_type=jnp.float32) * SCORE_SCALE
    grad_v = jnp.dot(attn.astype(jnp.bfloat16), dos, preferred_element_type=jnp.float32)
    outs = [dprev_ref]
    for kk in range(chips - 1, -1, -1):
        outs.append(dsib_ref.at[kk])
        outs.append(ddirect_refs[kk])
    for j, out in enumerate(outs):
        rows = slice(j * tokens, (j + 1) * tokens)
        out[0] = grad_k[rows].astype(out.dtype)
        out[1] = grad_v[rows].astype(out.dtype)


def attention_grads(mask, queries, grad_out, prev, direct, sib):
    tokens = queries.shape[0]
    chips = len(direct)
    key_count = mask.shape[0]
    width = prev.shape[2]
    heads = width // HEAD_DIM
    pair = 2 * HEAD_DIM
    block = pl.BlockSpec((2, tokens, HEAD_DIM), lambda g: (0, 0, g))
    sib_block = pl.BlockSpec((chips, 2, tokens, HEAD_DIM), lambda g: (0, 0, 0, g))
    pair_block = pl.BlockSpec((tokens, pair), lambda g: (0, g))
    part = jax.ShapeDtypeStruct(prev.shape, jnp.float32)
    flops = 2 * 5 * (2 * tokens) * key_count * HEAD_DIM * heads
    moved_bytes = 2 * 3 * queries.size + 2 * 2 * key_count * width * 3 + mask.size * 4
    return pl.pallas_call(
        lambda *refs: attention_kernel(chips, *refs),
        grid=(heads,),
        in_specs=[pl.BlockSpec((key_count, tokens), lambda g: (0, 0)), pair_block, pair_block]
        + [block] * (chips + 1)
        + [sib_block],
        out_specs=[pair_block] + [block] * (chips + 1) + [sib_block],
        out_shape=[jax.ShapeDtypeStruct(queries.shape, jnp.bfloat16)]
        + [part] * (chips + 1)
        + [jax.ShapeDtypeStruct(sib.shape, jnp.bfloat16)],
        cost_estimate=pl.CostEstimate(
            flops=flops, transcendentals=2 * tokens * key_count * heads, bytes_accessed=moved_bytes
        ),
    )(mask, queries, grad_out, prev, *direct, sib)


def local(queries, key_rows, value_rows, arriving_grad, doc_blocks):
    tokens = queries.shape[1]
    count = lax.axis_size("seq")
    grad_out = passed_along(arriving_grad, "pipe", -1)[0]
    position = lax.axis_index("seq")
    reach_back = (WINDOW - 1) // tokens + 1
    assert reach_back % 2 == 0 and count % reach_back == 0 and WINDOW % tokens == 0
    routes = Routes(count, reach_back)
    chip_in_group = (position % reach_back) // 2
    core = position % 2
    key_count = (reach_back + 1) * tokens
    token_doc = jnp.repeat(doc_blocks[0], MBLK)
    doc_pad = jnp.concatenate([jnp.full((reach_back * tokens,), -1, jnp.int32), token_doc])
    key_doc = lax.dynamic_slice_in_dim(doc_pad, position * tokens, key_count, 0)
    key_pos = (position - reach_back) * tokens + jnp.arange(key_count, dtype=jnp.int32)
    query_pos = position * tokens + jnp.arange(tokens, dtype=jnp.int32)
    query_doc = lax.dynamic_slice_in_dim(token_doc, position * tokens, tokens, 0)
    distance = query_pos[:, None] - key_pos[None, :]
    allowed = (distance >= 0) & (distance < WINDOW) & (query_doc[:, None] == key_doc[None, :])
    mask = allowed.T.astype(jnp.float32)
    width = KV_HEADS * HEAD_DIM // CHUNKS
    query_parts, key_parts, value_parts = [], [], []
    for chunk in range(CHUNKS):
        keys = slice(chunk * width, (chunk + 1) * width)
        pairs = slice(2 * chunk * width, 2 * (chunk + 1) * width)
        packed = jnp.stack([key_rows[0][:, keys], value_rows[0][:, keys]])
        if chunk > 0:
            packed, _ = lax.optimization_barrier((packed, outs[0]))
        prev, direct, sib = gather_window(packed, routes, chip_in_group, core)
        if chunk > 0:
            (prev, direct, sib), _ = lax.optimization_barrier(((prev, direct, sib), summed))
        outs = attention_grads(mask, queries[0][:, pairs], grad_out[:, pairs], prev, direct, sib)
        dprev, ddirect, dsib = outs[1], outs[2 : 2 + routes.chips], outs[-1]
        summed = scatter_window(dprev, ddirect, dsib, routes, chip_in_group, core)
        query_parts.append(outs[0])
        key_parts.append(summed[0].astype(jnp.bfloat16))
        value_parts.append(summed[1].astype(jnp.bfloat16))
    return (
        jnp.concatenate(query_parts, axis=1)[None],
        jnp.concatenate(key_parts, axis=1)[None],
        jnp.concatenate(value_parts, axis=1)[None],
    )


def solution(mesh):
    placed = (
        P("pipe", "seq", None),
        P("pipe", "seq", None),
        P("pipe", "seq", None),
        P("pipe", "seq", None),
        P("pipe", None),
    )
    return jax.shard_map(
        local,
        mesh=mesh,
        in_specs=placed,
        out_specs=(P("pipe", "seq", None), P("pipe", "seq", None), P("pipe", "seq", None)),
        check_vma=False,
    )
```

```python
import jax
import jax.numpy as jnp
from jax import lax
from jax.experimental import pallas as pl
from jax.sharding import PartitionSpec as P

HEADS = 32
KV_HEADS = 16
HEAD_DIM = 128
WINDOW = 1024
MBLK = 128


SCORE_SCALE = 168.0 ** (-0.5)
MASKED_SCORE = -1e30


def passed_along(value, axis, steps):
    count = lax.axis_size(axis)
    pairs = [(source, (source + steps) % count) for source in range(count)]
    return lax.ppermute(value, axis, pairs)


def moved(value, pairs):
    return lax.ppermute(value, "seq", pairs)


def reverse(pairs):
    return [(t, s) for (s, t) in pairs]


class Routes:
    def __init__(self, count, reach):
        self.reach = reach
        self.chips = reach // 2
        group_chip = lambda i: (i % reach) // 2
        self.hop = [(i, i + reach) for i in range(count - reach)]
        self.up = []
        self.down = []
        for e in range(1, self.chips):
            self.up.append([(i, i + 2 * e) for i in range(count) if group_chip(i) + e < self.chips])
            self.down.append(
                [(i, i + 2 * e - reach) for i in range(count) if group_chip(i) + e >= self.chips]
            )
        self.sibling = [(i, i ^ 1) for i in range(count)]


def gather_window(own, routes, chip_in_group, core):
    prev = moved(own, routes.hop)
    direct = [own]
    for e in range(1, routes.chips):
        up = moved(own, routes.up[e - 1])
        down = moved(prev, routes.down[e - 1])
        direct.append(jnp.where(chip_in_group >= e, up, down))
    later = direct[1:] + [prev]
    sent = jnp.where(core == 0, jnp.stack(direct), jnp.stack(later))
    sib = moved(sent, routes.sibling)
    return prev, direct, sib


def scatter_window(prev, direct, sib, routes, chip_in_group, core):
    chips = routes.chips
    link = jnp.bfloat16
    back = moved(sib, routes.sibling).astype(jnp.float32)
    is_even = core == 0
    own = direct[0] + jnp.where(is_even, back[0], 0.0)
    prev = prev + jnp.where(is_even, 0.0, back[chips - 1])
    sums = [direct[e] + jnp.where(is_even, back[e], back[e - 1]) for e in range(1, chips)]
    for e in range(1, chips):
        sent = sums[e - 1].astype(link)
        prev = prev + moved(sent, reverse(routes.down[e - 1])).astype(jnp.float32)
    for e in range(1, chips):
        sent = sums[e - 1].astype(link)
        own = own + moved(sent, reverse(routes.up[e - 1])).astype(jnp.float32)
    own = own + moved(prev.astype(link), reverse(routes.hop)).astype(jnp.float32)
    return own


def attention_kernel(chips, heads, bias_ref, q_ref, do_ref, prev_ref, *refs):
    direct_refs = refs[:chips]
    sib_ref = refs[chips]
    dq_ref, dprev_ref = refs[chips + 1], refs[chips + 2]
    ddirect_refs = refs[chips + 3 : 2 * chips + 3]
    dsib_ref = refs[2 * chips + 3]
    tokens = q_ref.shape[0]
    blocks = [prev_ref]
    outs = [dprev_ref]
    for k in range(chips - 1, -1, -1):
        blocks += [sib_ref.at[k], direct_refs[k]]
        outs += [dsib_ref.at[k], ddirect_refs[k]]
    bias = bias_ref[...]
    contract_last = (((1,), (1,)), ((), ()))
    contract_first = (((0,), (0,)), ((), ()))
    for h in range(heads):
        cols = slice(h * HEAD_DIM, (h + 1) * HEAD_DIM)
        pair = slice(2 * h * HEAD_DIM, (2 * h + 1) * HEAD_DIM)
        pair2 = slice((2 * h + 1) * HEAD_DIM, (2 * h + 2) * HEAD_DIM)
        k = jnp.concatenate([b[0, :, cols] for b in blocks], axis=0)
        v = jnp.concatenate([b[1, :, cols] for b in blocks], axis=0)
        qs = jnp.concatenate([q_ref[:, pair], q_ref[:, pair2]], axis=0)
        dos = jnp.concatenate([do_ref[:, pair], do_ref[:, pair2]], axis=0)
        scores = lax.dot_general(qs, k, contract_last, preferred_element_type=jnp.float32)
        scores = scores * SCORE_SCALE + bias
        largest = jnp.max(scores, axis=1, keepdims=True)
        unscaled = jnp.exp(scores - largest)
        attn = unscaled * (1.0 / jnp.sum(unscaled, axis=1, keepdims=True))
        dattn = lax.dot_general(dos, v, contract_last, preferred_element_type=jnp.float32)
        row_delta = jnp.sum(attn * dattn, axis=1, keepdims=True)
        dscores = (attn * (dattn - row_delta)).astype(jnp.bfloat16)
        grad_q = jnp.dot(dscores, k, preferred_element_type=jnp.float32) * SCORE_SCALE
        dq_ref[:, pair] = grad_q[:tokens].astype(dq_ref.dtype)
        dq_ref[:, pair2] = grad_q[tokens:].astype(dq_ref.dtype)
        grad_k = (
            lax.dot_general(dscores, qs, contract_first, preferred_element_type=jnp.float32)
            * SCORE_SCALE
        )
        grad_v = lax.dot_general(
            attn.astype(jnp.bfloat16), dos, contract_first, preferred_element_type=jnp.float32
        )
        for j, out in enumerate(outs):
            rows = slice(j * tokens, (j + 1) * tokens)
            out[0, :, cols] = grad_k[rows].astype(out.dtype)
            out[1, :, cols] = grad_v[rows].astype(out.dtype)


def attention_grads(bias, queries, grad_out, prev, direct, sib, per_step=2):
    tokens = queries.shape[0]
    chips = len(direct)
    key_count = bias.shape[1]
    width = prev.shape[2]
    heads = width // HEAD_DIM
    cols = per_step * HEAD_DIM
    block = pl.BlockSpec((2, tokens, cols), lambda g: (0, 0, g))
    sib_block = pl.BlockSpec((chips, 2, tokens, cols), lambda g: (0, 0, 0, g))
    pair_block = pl.BlockSpec((tokens, 2 * cols), lambda g: (0, g))
    part = jax.ShapeDtypeStruct(prev.shape, jnp.float32)
    flops = 2 * 5 * (2 * tokens) * key_count * HEAD_DIM * heads
    moved_bytes = 2 * 3 * queries.size + 2 * 2 * key_count * width * 3 + bias.size * 4
    return pl.pallas_call(
        lambda *refs: attention_kernel(chips, per_step, *refs),
        grid=(heads // per_step,),
        in_specs=[pl.BlockSpec(bias.shape, lambda g: (0, 0)), pair_block, pair_block]
        + [block] * (chips + 1)
        + [sib_block],
        out_specs=[pair_block] + [block] * (chips + 1) + [sib_block],
        out_shape=[jax.ShapeDtypeStruct(queries.shape, jnp.bfloat16)]
        + [part] * (chips + 1)
        + [jax.ShapeDtypeStruct(sib.shape, jnp.bfloat16)],
        cost_estimate=pl.CostEstimate(
            flops=flops, transcendentals=2 * tokens * key_count * heads, bytes_accessed=moved_bytes
        ),
    )(bias, queries, grad_out, prev, *direct, sib)


def local(queries, key_rows, value_rows, arriving_grad, doc_blocks):
    tokens = queries.shape[1]
    count = lax.axis_size("seq")
    grad_out = passed_along(arriving_grad, "pipe", -1)[0]
    position = lax.axis_index("seq")
    reach_back = (WINDOW - 1) // tokens + 1
    assert reach_back % 2 == 0 and count % reach_back == 0 and WINDOW % tokens == 0
    routes = Routes(count, reach_back)
    chip_in_group = (position % reach_back) // 2
    core = position % 2
    key_count = (reach_back + 1) * tokens
    token_doc = jnp.repeat(doc_blocks[0], MBLK)
    doc_pad = jnp.concatenate([jnp.full((reach_back * tokens,), -1, jnp.int32), token_doc])
    key_doc = lax.dynamic_slice_in_dim(doc_pad, position * tokens, key_count, 0)
    key_pos = (position - reach_back) * tokens + jnp.arange(key_count, dtype=jnp.int32)
    query_pos = position * tokens + jnp.arange(tokens, dtype=jnp.int32)
    query_doc = lax.dynamic_slice_in_dim(token_doc, position * tokens, tokens, 0)
    distance = query_pos[:, None] - key_pos[None, :]
    allowed = (distance >= 0) & (distance < WINDOW) & (query_doc[:, None] == key_doc[None, :])
    bias = jnp.where(allowed, 0.0, MASKED_SCORE).astype(jnp.float32)
    bias = jnp.concatenate([bias, bias], axis=0)
    packed = jnp.stack([key_rows[0], value_rows[0]])
    prev, direct, sib = gather_window(packed, routes, chip_in_group, core)
    outs = attention_grads(bias, queries[0], grad_out, prev, direct, sib)
    grad_query, dprev, ddirect, dsib = outs[0], outs[1], outs[2 : 2 + routes.chips], outs[-1]
    summed = scatter_window(dprev, ddirect, dsib, routes, chip_in_group, core)
    return (
        grad_query[None],
        summed[0].astype(jnp.bfloat16)[None],
        summed[1].astype(jnp.bfloat16)[None],
    )


def solution(mesh):
    placed = (
        P("pipe", "seq", None),
        P("pipe", "seq", None),
        P("pipe", "seq", None),
        P("pipe", "seq", None),
        P("pipe", None),
    )
    return jax.shard_map(
        local,
        mesh=mesh,
        in_specs=placed,
        out_specs=(P("pipe", "seq", None), P("pipe", "seq", None), P("pipe", "seq", None)),
        check_vma=False,
    )
```

```python
import jax
import jax.numpy as jnp
from jax import lax
from jax.experimental import pallas as pl
from jax.sharding import PartitionSpec as P

HEADS = 32
KV_HEADS = 16
HEAD_DIM = 128
WINDOW = 1024
MBLK = 128


SCORE_SCALE = 168.0 ** (-0.5)
MASKED_SCORE = -1e30


def passed_along(value, axis, steps):
    count = lax.axis_size(axis)
    pairs = [(source, (source + steps) % count) for source in range(count)]
    return lax.ppermute(value, axis, pairs)


def moved(value, pairs):
    return lax.ppermute(value, "seq", pairs)


def reverse(pairs):
    return [(t, s) for (s, t) in pairs]


class Routes:
    def __init__(self, count, reach):
        self.reach = reach
        self.chips = reach // 2
        group_chip = lambda i: (i % reach) // 2
        self.hop = [(i, i + reach) for i in range(count - reach)]
        self.up = []
        self.down = []
        for e in range(1, self.chips):
            self.up.append([(i, i + 2 * e) for i in range(count) if group_chip(i) + e < self.chips])
            self.down.append(
                [(i, i + 2 * e - reach) for i in range(count) if group_chip(i) + e >= self.chips]
            )
        self.sibling = [(i, i ^ 1) for i in range(count)]


def gather_window(own, routes, chip_in_group, core):
    prev = moved(own, routes.hop)
    direct = [own]
    for e in range(1, routes.chips):
        up = moved(own, routes.up[e - 1])
        down = moved(prev, routes.down[e - 1])
        direct.append(jnp.where(chip_in_group >= e, up, down))
    later = direct[1:] + [prev]
    sent = jnp.where(core == 0, jnp.stack(direct), jnp.stack(later))
    sib = moved(sent, routes.sibling)
    return prev, direct, sib


def scatter_window(prev, direct, sib, routes, chip_in_group, core):
    chips = routes.chips
    link = jnp.bfloat16
    back = moved(sib, routes.sibling).astype(jnp.float32)
    is_even = core == 0
    own = direct[0] + jnp.where(is_even, back[0], 0.0)
    prev = prev + jnp.where(is_even, 0.0, back[chips - 1])
    sums = [direct[e] + jnp.where(is_even, back[e], back[e - 1]) for e in range(1, chips)]
    for e in range(1, chips):
        sent = sums[e - 1].astype(link)
        got = moved(sent, reverse(routes.up[e - 1] + routes.down[e - 1])).astype(jnp.float32)
        upward = chip_in_group + e < chips
        own = own + jnp.where(upward, got, 0.0)
        prev = prev + jnp.where(upward, 0.0, got)
    own = own + moved(prev.astype(link), reverse(routes.hop)).astype(jnp.float32)
    return own


def attention_kernel(chips, heads, bias_ref, q_ref, do_ref, prev_ref, *refs):
    direct_refs = refs[:chips]
    sib_ref = refs[chips]
    dq_ref, dprev_ref = refs[chips + 1], refs[chips + 2]
    ddirect_refs = refs[chips + 3 : 2 * chips + 3]
    dsib_ref = refs[2 * chips + 3]
    tokens = q_ref.shape[0]
    blocks = [prev_ref]
    outs = [dprev_ref]
    for k in range(chips - 1, -1, -1):
        blocks += [sib_ref.at[k], direct_refs[k]]
        outs += [dsib_ref.at[k], ddirect_refs[k]]
    bias = bias_ref[...]
    contract_last = (((1,), (1,)), ((), ()))
    contract_first = (((0,), (0,)), ((), ()))
    for h in range(heads):
        cols = slice(h * HEAD_DIM, (h + 1) * HEAD_DIM)
        pair = slice(2 * h * HEAD_DIM, (2 * h + 1) * HEAD_DIM)
        pair2 = slice((2 * h + 1) * HEAD_DIM, (2 * h + 2) * HEAD_DIM)
        k = jnp.concatenate([b[0, :, cols] for b in blocks], axis=0)
        v = jnp.concatenate([b[1, :, cols] for b in blocks], axis=0)
        qs = jnp.concatenate([q_ref[:, pair], q_ref[:, pair2]], axis=0)
        dos = jnp.concatenate([do_ref[:, pair], do_ref[:, pair2]], axis=0)
        scores = lax.dot_general(qs, k, contract_last, preferred_element_type=jnp.float32)
        scores = scores * SCORE_SCALE + bias
        largest = jnp.max(scores, axis=1, keepdims=True)
        unscaled = jnp.exp(scores - largest)
        attn = unscaled * (1.0 / jnp.sum(unscaled, axis=1, keepdims=True))
        dattn = lax.dot_general(dos, v, contract_last, preferred_element_type=jnp.float32)
        row_delta = jnp.sum(attn * dattn, axis=1, keepdims=True)
        dscores = (attn * (dattn - row_delta)).astype(jnp.bfloat16)
        grad_q = jnp.dot(dscores, k, preferred_element_type=jnp.float32) * SCORE_SCALE
        dq_ref[:, pair] = grad_q[:tokens].astype(dq_ref.dtype)
        dq_ref[:, pair2] = grad_q[tokens:].astype(dq_ref.dtype)
        grad_k = (
            lax.dot_general(dscores, qs, contract_first, preferred_element_type=jnp.float32)
            * SCORE_SCALE
        )
        grad_v = lax.dot_general(
            attn.astype(jnp.bfloat16), dos, contract_first, preferred_element_type=jnp.float32
        )
        for j, out in enumerate(outs):
            rows = slice(j * tokens, (j + 1) * tokens)
            out[0, :, cols] = grad_k[rows].astype(out.dtype)
            out[1, :, cols] = grad_v[rows].astype(out.dtype)


def attention_grads(bias, queries, grad_out, prev, direct, sib, per_step=2):
    tokens = queries.shape[0]
    chips = len(direct)
    key_count = bias.shape[1]
    width = prev.shape[2]
    heads = width // HEAD_DIM
    cols = per_step * HEAD_DIM
    block = pl.BlockSpec((2, tokens, cols), lambda g: (0, 0, g))
    sib_block = pl.BlockSpec((chips, 2, tokens, cols), lambda g: (0, 0, 0, g))
    pair_block = pl.BlockSpec((tokens, 2 * cols), lambda g: (0, g))
    part = jax.ShapeDtypeStruct(prev.shape, jnp.float32)
    flops = 2 * 5 * (2 * tokens) * key_count * HEAD_DIM * heads
    moved_bytes = 2 * 3 * queries.size + 2 * 2 * key_count * width * 3 + bias.size * 4
    return pl.pallas_call(
        lambda *refs: attention_kernel(chips, per_step, *refs),
        grid=(heads // per_step,),
        in_specs=[pl.BlockSpec(bias.shape, lambda g: (0, 0)), pair_block, pair_block]
        + [block] * (chips + 1)
        + [sib_block],
        out_specs=[pair_block] + [block] * (chips + 1) + [sib_block],
        out_shape=[jax.ShapeDtypeStruct(queries.shape, jnp.bfloat16)]
        + [part] * (chips + 1)
        + [jax.ShapeDtypeStruct(sib.shape, jnp.bfloat16)],
        cost_estimate=pl.CostEstimate(
            flops=flops, transcendentals=2 * tokens * key_count * heads, bytes_accessed=moved_bytes
        ),
    )(bias, queries, grad_out, prev, *direct, sib)


def local(queries, key_rows, value_rows, arriving_grad, doc_blocks):
    tokens = queries.shape[1]
    count = lax.axis_size("seq")
    if lax.axis_size("pipe") > 1:
        arriving_grad = passed_along(arriving_grad, "pipe", -1)
    grad_out = arriving_grad[0]
    position = lax.axis_index("seq")
    reach_back = (WINDOW - 1) // tokens + 1
    assert reach_back % 2 == 0 and count % reach_back == 0 and WINDOW % tokens == 0
    routes = Routes(count, reach_back)
    chip_in_group = (position % reach_back) // 2
    core = position % 2
    key_count = (reach_back + 1) * tokens
    token_doc = jnp.repeat(doc_blocks[0], MBLK)
    doc_pad = jnp.concatenate([jnp.full((reach_back * tokens,), -1, jnp.int32), token_doc])
    key_doc = lax.dynamic_slice_in_dim(doc_pad, position * tokens, key_count, 0)
    key_pos = (position - reach_back) * tokens + jnp.arange(key_count, dtype=jnp.int32)
    query_pos = position * tokens + jnp.arange(tokens, dtype=jnp.int32)
    query_doc = lax.dynamic_slice_in_dim(token_doc, position * tokens, tokens, 0)
    distance = query_pos[:, None] - key_pos[None, :]
    allowed = (distance >= 0) & (distance < WINDOW) & (query_doc[:, None] == key_doc[None, :])
    bias = jnp.where(allowed, 0.0, MASKED_SCORE).astype(jnp.float32)
    bias = jnp.concatenate([bias, bias], axis=0)
    packed = jnp.stack([key_rows[0], value_rows[0]])
    prev, direct, sib = gather_window(packed, routes, chip_in_group, core)
    outs = attention_grads(bias, queries[0], grad_out, prev, direct, sib)
    grad_query, dprev, ddirect, dsib = outs[0], outs[1], outs[2 : 2 + routes.chips], outs[-1]
    summed = scatter_window(dprev, ddirect, dsib, routes, chip_in_group, core)
    return (
        grad_query[None],
        summed[0].astype(jnp.bfloat16)[None],
        summed[1].astype(jnp.bfloat16)[None],
    )


def solution(mesh):
    placed = (
        P("pipe", "seq", None),
        P("pipe", "seq", None),
        P("pipe", "seq", None),
        P("pipe", "seq", None),
        P("pipe", None),
    )
    return jax.shard_map(
        local,
        mesh=mesh,
        in_specs=placed,
        out_specs=(P("pipe", "seq", None), P("pipe", "seq", None), P("pipe", "seq", None)),
        check_vma=False,
    )
```

```python
import jax
import jax.numpy as jnp
from jax import lax
from jax.experimental import pallas as pl
from jax.sharding import PartitionSpec as P

HEADS = 32
KV_HEADS = 16
HEAD_DIM = 128
WINDOW = 1024
MBLK = 128


SCORE_SCALE = 168.0 ** (-0.5)
MASKED_SCORE = -1e30


def passed_along(value, axis, steps):
    count = lax.axis_size(axis)
    pairs = [(source, (source + steps) % count) for source in range(count)]
    return lax.ppermute(value, axis, pairs)


def moved(value, pairs):
    return lax.ppermute(value, "seq", pairs)


def reverse(pairs):
    return [(t, s) for (s, t) in pairs]


class Routes:
    def __init__(self, count, reach):
        self.reach = reach
        self.chips = reach // 2
        group_chip = lambda i: (i % reach) // 2
        self.hop = [(i, i + reach) for i in range(count - reach)]
        self.up = []
        self.down = []
        for e in range(1, self.chips):
            self.up.append([(i, i + 2 * e) for i in range(count) if group_chip(i) + e < self.chips])
            self.down.append(
                [(i, i + 2 * e - reach) for i in range(count) if group_chip(i) + e >= self.chips]
            )
        self.sibling = [(i, i ^ 1) for i in range(count)]


def halves(value):
    width = value.shape[-1] // 2
    return [value[..., :width], value[..., width:]]


def gather_window(own, routes, chip_in_group, core):
    prev_parts = [moved(part, routes.hop) for part in halves(own)]
    direct = [own]
    for e in range(1, routes.chips):
        up = moved(own, routes.up[e - 1])
        down = jnp.concatenate(
            [moved(part, routes.down[e - 1]) for part in prev_parts], axis=-1
        )
        direct.append(jnp.where(chip_in_group >= e, up, down))
    prev = jnp.concatenate(prev_parts, axis=-1)
    later = direct[1:] + [prev]
    sent = jnp.where(core == 0, jnp.stack(direct), jnp.stack(later))
    sib = moved(sent, routes.sibling)
    return prev, direct, sib


def scatter_window(prev, direct, sib, routes, chip_in_group, core):
    chips = routes.chips
    link = jnp.bfloat16
    back = moved(sib, routes.sibling).astype(jnp.float32)
    is_even = core == 0
    own = direct[0] + jnp.where(is_even, back[0], 0.0)
    prev = prev + jnp.where(is_even, 0.0, back[chips - 1])
    sums = [direct[e] + jnp.where(is_even, back[e], back[e - 1]) for e in range(1, chips)]
    sent = [total.astype(link) for total in sums]
    prev_parts = halves(prev)
    for e in range(1, chips):
        for x, part in enumerate(halves(sent[e - 1])):
            got = moved(part, reverse(routes.down[e - 1]))
            prev_parts[x] = prev_parts[x] + got.astype(jnp.float32)
    for e in range(1, chips):
        own = own + moved(sent[e - 1], reverse(routes.up[e - 1])).astype(jnp.float32)
    hopped = [moved(part.astype(link), reverse(routes.hop)) for part in prev_parts]
    return own + jnp.concatenate(hopped, axis=-1).astype(jnp.float32)


def attention_kernel(chips, heads, bias_ref, q_ref, do_ref, prev_ref, *refs):
    direct_refs = refs[:chips]
    sib_ref = refs[chips]
    dq_ref, dprev_ref = refs[chips + 1], refs[chips + 2]
    ddirect_refs = refs[chips + 3 : 2 * chips + 3]
    dsib_ref = refs[2 * chips + 3]
    tokens = q_ref.shape[0]
    blocks = [prev_ref]
    outs = [dprev_ref]
    for k in range(chips - 1, -1, -1):
        blocks += [sib_ref.at[k], direct_refs[k]]
        outs += [dsib_ref.at[k], ddirect_refs[k]]
    bias = bias_ref[...]
    contract_last = (((1,), (1,)), ((), ()))
    contract_first = (((0,), (0,)), ((), ()))
    for h in range(heads):
        cols = slice(h * HEAD_DIM, (h + 1) * HEAD_DIM)
        pair = slice(2 * h * HEAD_DIM, (2 * h + 1) * HEAD_DIM)
        pair2 = slice((2 * h + 1) * HEAD_DIM, (2 * h + 2) * HEAD_DIM)
        k = jnp.concatenate([b[0, :, cols] for b in blocks], axis=0)
        v = jnp.concatenate([b[1, :, cols] for b in blocks], axis=0)
        qs = jnp.concatenate([q_ref[:, pair], q_ref[:, pair2]], axis=0)
        dos = jnp.concatenate([do_ref[:, pair], do_ref[:, pair2]], axis=0)
        scores = lax.dot_general(qs, k, contract_last, preferred_element_type=jnp.float32)
        scores = scores * SCORE_SCALE + bias
        largest = jnp.max(scores, axis=1, keepdims=True)
        unscaled = jnp.exp(scores - largest)
        attn = unscaled * (1.0 / jnp.sum(unscaled, axis=1, keepdims=True))
        dattn = lax.dot_general(dos, v, contract_last, preferred_element_type=jnp.float32)
        row_delta = jnp.sum(attn * dattn, axis=1, keepdims=True)
        dscores = (attn * (dattn - row_delta)).astype(jnp.bfloat16)
        grad_q = jnp.dot(dscores, k, preferred_element_type=jnp.float32) * SCORE_SCALE
        dq_ref[:, pair] = grad_q[:tokens].astype(dq_ref.dtype)
        dq_ref[:, pair2] = grad_q[tokens:].astype(dq_ref.dtype)
        grad_k = (
            lax.dot_general(dscores, qs, contract_first, preferred_element_type=jnp.float32)
            * SCORE_SCALE
        )
        grad_v = lax.dot_general(
            attn.astype(jnp.bfloat16), dos, contract_first, preferred_element_type=jnp.float32
        )
        for j, out in enumerate(outs):
            rows = slice(j * tokens, (j + 1) * tokens)
            out[0, :, cols] = grad_k[rows].astype(out.dtype)
            out[1, :, cols] = grad_v[rows].astype(out.dtype)


def attention_grads(bias, queries, grad_out, prev, direct, sib, per_step=2):
    tokens = queries.shape[0]
    chips = len(direct)
    key_count = bias.shape[1]
    width = prev.shape[2]
    heads = width // HEAD_DIM
    cols = per_step * HEAD_DIM
    block = pl.BlockSpec((2, tokens, cols), lambda g: (0, 0, g))
    sib_block = pl.BlockSpec((chips, 2, tokens, cols), lambda g: (0, 0, 0, g))
    pair_block = pl.BlockSpec((tokens, 2 * cols), lambda g: (0, g))
    part = jax.ShapeDtypeStruct(prev.shape, jnp.float32)
    flops = 2 * 5 * (2 * tokens) * key_count * HEAD_DIM * heads
    moved_bytes = 2 * 3 * queries.size + 2 * 2 * key_count * width * 3 + bias.size * 4
    return pl.pallas_call(
        lambda *refs: attention_kernel(chips, per_step, *refs),
        grid=(heads // per_step,),
        in_specs=[pl.BlockSpec(bias.shape, lambda g: (0, 0)), pair_block, pair_block]
        + [block] * (chips + 1)
        + [sib_block],
        out_specs=[pair_block] + [block] * (chips + 1) + [sib_block],
        out_shape=[jax.ShapeDtypeStruct(queries.shape, jnp.bfloat16)]
        + [part] * (chips + 1)
        + [jax.ShapeDtypeStruct(sib.shape, jnp.bfloat16)],
        cost_estimate=pl.CostEstimate(
            flops=flops, transcendentals=2 * tokens * key_count * heads, bytes_accessed=moved_bytes
        ),
    )(bias, queries, grad_out, prev, *direct, sib)


def local(queries, key_rows, value_rows, arriving_grad, doc_blocks):
    tokens = queries.shape[1]
    count = lax.axis_size("seq")
    if lax.axis_size("pipe") > 1:
        arriving_grad = passed_along(arriving_grad, "pipe", -1)
    grad_out = arriving_grad[0]
    position = lax.axis_index("seq")
    reach_back = (WINDOW - 1) // tokens + 1
    assert reach_back % 2 == 0 and count % reach_back == 0 and WINDOW % tokens == 0
    routes = Routes(count, reach_back)
    chip_in_group = (position % reach_back) // 2
    core = position % 2
    key_count = (reach_back + 1) * tokens
    token_doc = jnp.repeat(doc_blocks[0], MBLK)
    doc_pad = jnp.concatenate([jnp.full((reach_back * tokens,), -1, jnp.int32), token_doc])
    key_doc = lax.dynamic_slice_in_dim(doc_pad, position * tokens, key_count, 0)
    key_pos = (position - reach_back) * tokens + jnp.arange(key_count, dtype=jnp.int32)
    query_pos = position * tokens + jnp.arange(tokens, dtype=jnp.int32)
    query_doc = lax.dynamic_slice_in_dim(token_doc, position * tokens, tokens, 0)
    distance = query_pos[:, None] - key_pos[None, :]
    allowed = (distance >= 0) & (distance < WINDOW) & (query_doc[:, None] == key_doc[None, :])
    bias = jnp.where(allowed, 0.0, MASKED_SCORE).astype(jnp.float32)
    bias = jnp.concatenate([bias, bias], axis=0)
    packed = jnp.stack([key_rows[0], value_rows[0]])
    prev, direct, sib = gather_window(packed, routes, chip_in_group, core)
    outs = attention_grads(bias, queries[0], grad_out, prev, direct, sib)
    grad_query, dprev, ddirect, dsib = outs[0], outs[1], outs[2 : 2 + routes.chips], outs[-1]
    summed = scatter_window(dprev, ddirect, dsib, routes, chip_in_group, core)
    return (
        grad_query[None],
        summed[0].astype(jnp.bfloat16)[None],
        summed[1].astype(jnp.bfloat16)[None],
    )


def solution(mesh):
    placed = (
        P("pipe", "seq", None),
        P("pipe", "seq", None),
        P("pipe", "seq", None),
        P("pipe", "seq", None),
        P("pipe", None),
    )
    return jax.shard_map(
        local,
        mesh=mesh,
        in_specs=placed,
        out_specs=(P("pipe", "seq", None), P("pipe", "seq", None), P("pipe", "seq", None)),
        check_vma=False,
    )
```

```python
import jax
import jax.numpy as jnp
from jax import lax
from jax.experimental import pallas as pl
from jax.experimental.pallas import tpu as pltpu
from jax.sharding import PartitionSpec as P

HEADS = 32
KV_HEADS = 16
HEAD_DIM = 128
WINDOW = 1024
MBLK = 128


SCORE_SCALE = 168.0 ** (-0.5)
MASKED_SCORE = -1e30


def passed_along(value, axis, steps):
    count = lax.axis_size(axis)
    pairs = [(source, (source + steps) % count) for source in range(count)]
    return lax.ppermute(value, axis, pairs)


def moved(value, pairs):
    return lax.ppermute(value, "seq", pairs)


def reverse(pairs):
    return [(t, s) for (s, t) in pairs]


class Routes:
    def __init__(self, count, reach):
        self.reach = reach
        self.chips = reach // 2
        group_chip = lambda i: (i % reach) // 2
        self.hop = [(i, i + reach) for i in range(count - reach)]
        self.up = []
        self.down = []
        for e in range(1, self.chips):
            self.up.append([(i, i + 2 * e) for i in range(count) if group_chip(i) + e < self.chips])
            self.down.append(
                [(i, i + 2 * e - reach) for i in range(count) if group_chip(i) + e >= self.chips]
            )
        self.sibling = [(i, i ^ 1) for i in range(count)]


def gather_window(own, routes, chip_in_group):
    prev = moved(own, routes.hop)
    recv = []
    for e in range(1, routes.chips):
        up = moved(own, routes.up[e - 1])
        down = moved(prev, routes.down[e - 1])
        recv.append(jnp.where(chip_in_group >= e, up, down))
    return [prev] + recv[::-1] + [own]


def scatter_window(parts, routes):
    link = jnp.bfloat16
    chips = routes.chips
    prev, own = parts[0], parts[-1]
    recv = parts[1:-1][::-1]
    sent = [r.astype(link) for r in recv]
    for e in range(1, chips):
        prev = prev + moved(sent[e - 1], reverse(routes.down[e - 1])).astype(jnp.float32)
    for e in range(1, chips):
        own = own + moved(sent[e - 1], reverse(routes.up[e - 1])).astype(jnp.float32)
    return own + moved(prev.astype(link), reverse(routes.hop)).astype(jnp.float32)


def attention_kernel(chips, core_ref, bias_ref, qm_ref, qs_ref, dm_ref, ds_ref, *refs):
    del core_ref
    kv_refs = refs[:chips]
    dqm_ref, dqs_ref = refs[chips], refs[chips + 1]
    part_refs = refs[chips + 2 :]
    tokens = qm_ref.shape[0]
    d = HEAD_DIM
    k = jnp.concatenate([r[0, s] for r in kv_refs for s in range(2)], axis=0)
    v = jnp.concatenate([r[1, s] for r in kv_refs for s in range(2)], axis=0)
    qs = jnp.concatenate([qm_ref[:, :d], qs_ref[:, :d], qm_ref[:, d:], qs_ref[:, d:]], axis=0)
    dos = jnp.concatenate([dm_ref[:, :d], ds_ref[:, :d], dm_ref[:, d:], ds_ref[:, d:]], axis=0)
    contract_last = (((1,), (1,)), ((), ()))
    contract_first = (((0,), (0,)), ((), ()))
    scores = lax.dot_general(qs, k, contract_last, preferred_element_type=jnp.float32)
    scores = scores * SCORE_SCALE + bias_ref[...]
    largest = jnp.max(scores, axis=1, keepdims=True)
    unscaled = jnp.exp(scores - largest)
    attn = unscaled * (1.0 / jnp.sum(unscaled, axis=1, keepdims=True))
    dattn = lax.dot_general(dos, v, contract_last, preferred_element_type=jnp.float32)
    row_delta = jnp.sum(attn * dattn, axis=1, keepdims=True)
    dscores = (attn * (dattn - row_delta)).astype(jnp.bfloat16)
    grad_q = jnp.dot(dscores, k, preferred_element_type=jnp.float32) * SCORE_SCALE
    rows = lambda j: slice(j * tokens, (j + 1) * tokens)
    dqm_ref[:, :d] = grad_q[rows(0)].astype(dqm_ref.dtype)
    dqs_ref[:, :d] = grad_q[rows(1)].astype(dqs_ref.dtype)
    dqm_ref[:, d:] = grad_q[rows(2)].astype(dqm_ref.dtype)
    dqs_ref[:, d:] = grad_q[rows(3)].astype(dqs_ref.dtype)
    grad_k = (
        lax.dot_general(dscores, qs, contract_first, preferred_element_type=jnp.float32)
        * SCORE_SCALE
    )
    grad_v = lax.dot_general(
        attn.astype(jnp.bfloat16), dos, contract_first, preferred_element_type=jnp.float32
    )
    for j, out in enumerate(part_refs):
        for s in range(2):
            out[0, s] = grad_k[rows(2 * j + s)]
            out[1, s] = grad_v[rows(2 * j + s)]


def attention_grads(core, bias, queries, query_sib, grad_out, grad_sib, payloads):
    tokens = queries.shape[0]
    chips = len(payloads)
    key_count = bias.shape[1]
    half = payloads[0].shape[3]
    heads = half // HEAD_DIM
    pair = 2 * HEAD_DIM
    mine = pl.BlockSpec((tokens, pair), lambda g, c: (0, c[0] * heads + g))
    other = pl.BlockSpec((tokens, pair), lambda g, c: (0, g))
    chip = pl.BlockSpec((2, 2, tokens, HEAD_DIM), lambda g, c: (0, 0, 0, g))
    part = jax.ShapeDtypeStruct(payloads[0].shape, jnp.float32)
    rows = 4 * tokens
    flops = 2 * 5 * rows * key_count * HEAD_DIM * heads
    moved_bytes = 2 * 6 * tokens * half * 2 + 2 * 2 * key_count * half * 3 + bias.size * 4
    grid_spec = pltpu.PrefetchScalarGridSpec(
        num_scalar_prefetch=1,
        grid=(heads,),
        in_specs=[pl.BlockSpec(bias.shape, lambda g, c: (0, 0)), mine, other, mine, other]
        + [chip] * chips,
        out_specs=[other, other] + [chip] * chips,
    )
    return pl.pallas_call(
        lambda *refs: attention_kernel(chips, *refs),
        grid_spec=grid_spec,
        out_shape=[jax.ShapeDtypeStruct(query_sib.shape, jnp.bfloat16)] * 2 + [part] * chips,
        cost_estimate=pl.CostEstimate(
            flops=flops, transcendentals=rows * key_count * heads, bytes_accessed=moved_bytes
        ),
    )(core, bias, queries, query_sib, grad_out, grad_sib, *payloads)


def in_core_order(core, mine, theirs):
    return jnp.where(core == 0, jnp.concatenate([mine, theirs], -1), jnp.concatenate([theirs, mine], -1))


def local(queries, key_rows, value_rows, arriving_grad, doc_blocks):
    tokens = queries.shape[1]
    count = lax.axis_size("seq")
    if lax.axis_size("pipe") > 1:
        arriving_grad = passed_along(arriving_grad, "pipe", -1)
    grad_out = arriving_grad[0]
    position = lax.axis_index("seq")
    reach_back = (WINDOW - 1) // tokens + 1
    assert reach_back % 2 == 0 and count % reach_back == 0 and WINDOW % tokens == 0
    routes = Routes(count, reach_back)
    chips = routes.chips
    chip_in_group = (position % reach_back) // 2
    core = position % 2
    other = 1 - core
    key_width = key_rows.shape[2] // 2
    query_width = queries.shape[2] // 2
    keys, values = key_rows[0], value_rows[0]
    kv_sent = jnp.stack(
        [lax.dynamic_slice_in_dim(keys, other * key_width, key_width, 1),
         lax.dynamic_slice_in_dim(values, other * key_width, key_width, 1)]
    )
    kv_sib = moved(kv_sent, routes.sibling)
    kv_mine = jnp.stack(
        [lax.dynamic_slice_in_dim(keys, core * key_width, key_width, 1),
         lax.dynamic_slice_in_dim(values, core * key_width, key_width, 1)]
    )
    own = jnp.stack([kv_mine, kv_sib], axis=1)
    qd_sent = jnp.stack(
        [lax.dynamic_slice_in_dim(queries[0], other * query_width, query_width, 1),
         lax.dynamic_slice_in_dim(grad_out, other * query_width, query_width, 1)]
    )
    qd_sib = moved(qd_sent, routes.sibling)
    payloads = gather_window(own, routes, chip_in_group)

    chip = position // 2
    block_of = lambda m, s: 2 * m + jnp.where(s == 0, core, other)
    key_blocks = [block_of(chip - chips + j, s) for j in range(chips + 1) for s in range(2)]
    token_doc = jnp.repeat(doc_blocks[0], MBLK)
    pad = (reach_back + 2) * tokens
    doc_pad = jnp.concatenate([jnp.full((pad,), -1, jnp.int32), token_doc])
    key_doc = jnp.concatenate(
        [lax.dynamic_slice_in_dim(doc_pad, b * tokens + pad, tokens, 0) for b in key_blocks]
    )
    offsets = jnp.arange(tokens, dtype=jnp.int32)
    key_pos = jnp.concatenate([b * tokens + offsets for b in key_blocks])
    masks = []
    for block in (position, position ^ 1):
        query_pos = block * tokens + offsets
        query_doc = lax.dynamic_slice_in_dim(token_doc, block * tokens, tokens, 0)
        distance = query_pos[:, None] - key_pos[None, :]
        allowed = (distance >= 0) & (distance < WINDOW) & (query_doc[:, None] == key_doc[None, :])
        masks.append(jnp.where(allowed, 0.0, MASKED_SCORE).astype(jnp.float32))
    bias = jnp.concatenate(masks + masks, axis=0)

    outs = attention_grads(
        core[None].astype(jnp.int32), bias, queries[0], qd_sib[0], grad_out, qd_sib[1], payloads
    )
    dq_mine, dq_sib, parts = outs[0], outs[1], outs[2:]
    summed = scatter_window(parts, routes)
    sent = jnp.concatenate(
        [summed[0, 1].astype(jnp.bfloat16), summed[1, 1].astype(jnp.bfloat16), dq_sib], axis=-1
    )
    got = moved(sent, routes.sibling)
    grad_key = in_core_order(core, summed[0, 0].astype(jnp.bfloat16), got[:, :key_width])
    grad_value = in_core_order(
        core, summed[1, 0].astype(jnp.bfloat16), got[:, key_width : 2 * key_width]
    )
    grad_query = in_core_order(core, dq_mine, got[:, 2 * key_width :])
    return (grad_query[None], grad_key[None], grad_value[None])


def solution(mesh):
    placed = (
        P("pipe", "seq", None),
        P("pipe", "seq", None),
        P("pipe", "seq", None),
        P("pipe", "seq", None),
        P("pipe", None),
    )
    return jax.shard_map(
        local,
        mesh=mesh,
        in_specs=placed,
        out_specs=(P("pipe", "seq", None), P("pipe", "seq", None), P("pipe", "seq", None)),
        check_vma=False,
    )
```

```python
import jax
import jax.numpy as jnp
from jax import lax
from jax.experimental import pallas as pl
from jax.experimental.pallas import tpu as pltpu
from jax.sharding import PartitionSpec as P

HEADS = 32
KV_HEADS = 16
HEAD_DIM = 128
WINDOW = 1024
MBLK = 128


SCORE_SCALE = 168.0 ** (-0.5)
MASKED_SCORE = -1e30


def passed_along(value, axis, steps):
    count = lax.axis_size(axis)
    pairs = [(source, (source + steps) % count) for source in range(count)]
    return lax.ppermute(value, axis, pairs)


def moved(value, pairs):
    return lax.ppermute(value, "seq", pairs)


def reverse(pairs):
    return [(t, s) for (s, t) in pairs]


class Routes:
    def __init__(self, count, reach):
        self.reach = reach
        self.chips = reach // 2
        group_chip = lambda i: (i % reach) // 2
        self.hop = [(i, i + reach) for i in range(count - reach)]
        self.hop_cross = [(i, (i + reach) ^ 1) for i in range(count - reach)]
        self.up = []
        self.down = []
        for e in range(1, self.chips):
            self.up.append([(i, i + 2 * e) for i in range(count) if group_chip(i) + e < self.chips])
            self.down.append(
                [(i, i + 2 * e - reach) for i in range(count) if group_chip(i) + e >= self.chips]
            )
        self.sibling = [(i, i ^ 1) for i in range(count)]


def gather_window(own, mine, theirs, routes, chip_in_group):
    prev = jnp.stack([moved(mine, routes.hop), moved(theirs, routes.hop_cross)], axis=1)
    recv = []
    for e in range(1, routes.chips):
        up = moved(own, routes.up[e - 1])
        down = moved(prev, routes.down[e - 1])
        recv.append(jnp.where(chip_in_group >= e, up, down))
    return [prev] + recv[::-1] + [own]


def scatter_window(parts, routes):
    link = jnp.bfloat16
    chips = routes.chips
    prev, own = parts[0], parts[-1]
    recv = parts[1:-1][::-1]
    sent = [r.astype(link) for r in recv]
    for e in range(1, chips):
        prev = prev + moved(sent[e - 1], reverse(routes.down[e - 1])).astype(jnp.float32)
    for e in range(1, chips):
        own = own + moved(sent[e - 1], reverse(routes.up[e - 1])).astype(jnp.float32)
    return own + moved(prev.astype(link), reverse(routes.hop)).astype(jnp.float32)


def attention_kernel(chips, core_ref, bias_ref, qm_ref, qs_ref, dm_ref, ds_ref, *refs):
    del core_ref
    kv_refs = refs[:chips]
    dqm_ref, dqs_ref = refs[chips], refs[chips + 1]
    part_refs = refs[chips + 2 :]
    tokens = qm_ref.shape[0]
    d = HEAD_DIM
    k = jnp.concatenate([r[0, s] for r in kv_refs for s in range(2)], axis=0)
    v = jnp.concatenate([r[1, s] for r in kv_refs for s in range(2)], axis=0)
    qs = jnp.concatenate([qm_ref[:, :d], qs_ref[:, :d], qm_ref[:, d:], qs_ref[:, d:]], axis=0)
    dos = jnp.concatenate([dm_ref[:, :d], ds_ref[:, :d], dm_ref[:, d:], ds_ref[:, d:]], axis=0)
    contract_last = (((1,), (1,)), ((), ()))
    contract_first = (((0,), (0,)), ((), ()))
    scores = lax.dot_general(qs, k, contract_last, preferred_element_type=jnp.float32)
    scores = scores * SCORE_SCALE + bias_ref[...]
    largest = jnp.max(scores, axis=1, keepdims=True)
    unscaled = jnp.exp(scores - largest)
    attn = unscaled * (1.0 / jnp.sum(unscaled, axis=1, keepdims=True))
    dattn = lax.dot_general(dos, v, contract_last, preferred_element_type=jnp.float32)
    row_delta = jnp.sum(attn * dattn, axis=1, keepdims=True)
    dscores = (attn * (dattn - row_delta)).astype(jnp.bfloat16)
    grad_q = jnp.dot(dscores, k, preferred_element_type=jnp.float32) * SCORE_SCALE
    rows = lambda j: slice(j * tokens, (j + 1) * tokens)
    dqm_ref[:, :d] = grad_q[rows(0)].astype(dqm_ref.dtype)
    dqs_ref[:, :d] = grad_q[rows(1)].astype(dqs_ref.dtype)
    dqm_ref[:, d:] = grad_q[rows(2)].astype(dqm_ref.dtype)
    dqs_ref[:, d:] = grad_q[rows(3)].astype(dqs_ref.dtype)
    grad_k = (
        lax.dot_general(dscores, qs, contract_first, preferred_element_type=jnp.float32)
        * SCORE_SCALE
    )
    grad_v = lax.dot_general(
        attn.astype(jnp.bfloat16), dos, contract_first, preferred_element_type=jnp.float32
    )
    for j, out in enumerate(part_refs):
        for s in range(2):
            out[0, s] = grad_k[rows(2 * j + s)]
            out[1, s] = grad_v[rows(2 * j + s)]


def attention_grads(core, bias, queries, query_sib, grad_out, grad_sib, payloads):
    tokens = queries.shape[0]
    chips = len(payloads)
    key_count = bias.shape[1]
    half = payloads[0].shape[3]
    heads = half // HEAD_DIM
    pair = 2 * HEAD_DIM
    mine = pl.BlockSpec((tokens, pair), lambda g, c: (0, c[0] * heads + g))
    other = pl.BlockSpec((tokens, pair), lambda g, c: (0, g))
    chip = pl.BlockSpec((2, 2, tokens, HEAD_DIM), lambda g, c: (0, 0, 0, g))
    part = jax.ShapeDtypeStruct(payloads[0].shape, jnp.float32)
    rows = 4 * tokens
    flops = 2 * 5 * rows * key_count * HEAD_DIM * heads
    moved_bytes = 2 * 6 * tokens * half * 2 + 2 * 2 * key_count * half * 3 + bias.size * 4
    grid_spec = pltpu.PrefetchScalarGridSpec(
        num_scalar_prefetch=1,
        grid=(heads,),
        in_specs=[pl.BlockSpec(bias.shape, lambda g, c: (0, 0)), mine, other, mine, other]
        + [chip] * chips,
        out_specs=[other, other] + [chip] * chips,
    )
    return pl.pallas_call(
        lambda *refs: attention_kernel(chips, *refs),
        grid_spec=grid_spec,
        out_shape=[jax.ShapeDtypeStruct(query_sib.shape, jnp.bfloat16)] * 2 + [part] * chips,
        cost_estimate=pl.CostEstimate(
            flops=flops, transcendentals=rows * key_count * heads, bytes_accessed=moved_bytes
        ),
    )(core, bias, queries, query_sib, grad_out, grad_sib, *payloads)


def in_core_order(core, mine, theirs):
    return jnp.where(core == 0, jnp.concatenate([mine, theirs], -1), jnp.concatenate([theirs, mine], -1))


def local(queries, key_rows, value_rows, arriving_grad, doc_blocks):
    tokens = queries.shape[1]
    count = lax.axis_size("seq")
    if lax.axis_size("pipe") > 1:
        arriving_grad = passed_along(arriving_grad, "pipe", -1)
    grad_out = arriving_grad[0]
    position = lax.axis_index("seq")
    reach_back = (WINDOW - 1) // tokens + 1
    assert reach_back % 2 == 0 and count % reach_back == 0 and WINDOW % tokens == 0
    routes = Routes(count, reach_back)
    chips = routes.chips
    chip_in_group = (position % reach_back) // 2
    core = position % 2
    other = 1 - core
    key_width = key_rows.shape[2] // 2
    query_width = queries.shape[2] // 2
    keys, values = key_rows[0], value_rows[0]
    kv_sent = jnp.stack(
        [lax.dynamic_slice_in_dim(keys, other * key_width, key_width, 1),
         lax.dynamic_slice_in_dim(values, other * key_width, key_width, 1)]
    )
    kv_sib = moved(kv_sent, routes.sibling)
    kv_mine = jnp.stack(
        [lax.dynamic_slice_in_dim(keys, core * key_width, key_width, 1),
         lax.dynamic_slice_in_dim(values, core * key_width, key_width, 1)]
    )
    own = jnp.stack([kv_mine, kv_sib], axis=1)
    qd_sent = jnp.stack(
        [lax.dynamic_slice_in_dim(queries[0], other * query_width, query_width, 1),
         lax.dynamic_slice_in_dim(grad_out, other * query_width, query_width, 1)]
    )
    qd_sib = moved(qd_sent, routes.sibling)
    payloads = gather_window(own, kv_mine, kv_sent, routes, chip_in_group)

    chip = position // 2
    block_of = lambda m, s: 2 * m + jnp.where(s == 0, core, other)
    key_blocks = [block_of(chip - chips + j, s) for j in range(chips + 1) for s in range(2)]
    token_doc = jnp.repeat(doc_blocks[0], MBLK)
    pad = (reach_back + 2) * tokens
    doc_pad = jnp.concatenate([jnp.full((pad,), -1, jnp.int32), token_doc])
    key_doc = jnp.concatenate(
        [lax.dynamic_slice_in_dim(doc_pad, b * tokens + pad, tokens, 0) for b in key_blocks]
    )
    offsets = jnp.arange(tokens, dtype=jnp.int32)
    key_pos = jnp.concatenate([b * tokens + offsets for b in key_blocks])
    masks = []
    for block in (position, position ^ 1):
        query_pos = block * tokens + offsets
        query_doc = lax.dynamic_slice_in_dim(token_doc, block * tokens, tokens, 0)
        distance = query_pos[:, None] - key_pos[None, :]
        allowed = (distance >= 0) & (distance < WINDOW) & (query_doc[:, None] == key_doc[None, :])
        masks.append(jnp.where(allowed, 0.0, MASKED_SCORE).astype(jnp.float32))
    bias = jnp.concatenate(masks + masks, axis=0)

    outs = attention_grads(
        core[None].astype(jnp.int32), bias, queries[0], qd_sib[0], grad_out, qd_sib[1], payloads
    )
    dq_mine, dq_sib, parts = outs[0], outs[1], outs[2:]
    grad_query = in_core_order(core, dq_mine, moved(dq_sib, routes.sibling))
    summed = scatter_window(parts, routes)
    got = moved(summed[:, 1].astype(jnp.bfloat16), routes.sibling)
    grad_key = in_core_order(core, summed[0, 0].astype(jnp.bfloat16), got[0])
    grad_value = in_core_order(core, summed[1, 0].astype(jnp.bfloat16), got[1])
    return (grad_query[None], grad_key[None], grad_value[None])


def solution(mesh):
    placed = (
        P("pipe", "seq", None),
        P("pipe", "seq", None),
        P("pipe", "seq", None),
        P("pipe", "seq", None),
        P("pipe", None),
    )
    return jax.shard_map(
        local,
        mesh=mesh,
        in_specs=placed,
        out_specs=(P("pipe", "seq", None), P("pipe", "seq", None), P("pipe", "seq", None)),
        check_vma=False,
    )
```

```python
import jax
import jax.numpy as jnp
from jax import lax
from jax.experimental import pallas as pl
from jax.experimental.pallas import tpu as pltpu
from jax.sharding import PartitionSpec as P

HEADS = 32
KV_HEADS = 16
HEAD_DIM = 128
WINDOW = 1024
MBLK = 128


SCORE_SCALE = 168.0 ** (-0.5)
MASKED_SCORE = -1e30


def passed_along(value, axis, steps):
    count = lax.axis_size(axis)
    pairs = [(source, (source + steps) % count) for source in range(count)]
    return lax.ppermute(value, axis, pairs)


def moved(value, pairs):
    return lax.ppermute(value, "seq", pairs)


def reverse(pairs):
    return [(t, s) for (s, t) in pairs]


class Routes:
    def __init__(self, count, reach):
        self.reach = reach
        self.chips = reach // 2
        group_chip = lambda i: (i % reach) // 2
        self.hop = [(i, i + reach) for i in range(count - reach)]
        self.up = []
        self.down = []
        for e in range(1, self.chips):
            self.up.append([(i, i + 2 * e) for i in range(count) if group_chip(i) + e < self.chips])
            self.down.append(
                [(i, i + 2 * e - reach) for i in range(count) if group_chip(i) + e >= self.chips]
            )
        self.sibling = [(i, i ^ 1) for i in range(count)]


def gather_window(own, routes, chip_in_group):
    prev = moved(own, routes.hop)
    recv = []
    for e in range(1, routes.chips):
        sent = jnp.where(chip_in_group + e < routes.chips, own, prev)
        recv.append(moved(sent, routes.up[e - 1] + routes.down[e - 1]))
    return [prev] + recv[::-1] + [own]


def scatter_window(parts, routes):
    link = jnp.bfloat16
    chips = routes.chips
    prev, own = parts[0], parts[-1]
    recv = parts[1:-1][::-1]
    sent = [r.astype(link) for r in recv]
    for e in range(1, chips):
        prev = prev + moved(sent[e - 1], reverse(routes.down[e - 1])).astype(jnp.float32)
    for e in range(1, chips):
        own = own + moved(sent[e - 1], reverse(routes.up[e - 1])).astype(jnp.float32)
    return own + moved(prev.astype(link), reverse(routes.hop)).astype(jnp.float32)


def attention_kernel(chips, core_ref, bias_ref, qm_ref, qs_ref, dm_ref, ds_ref, *refs):
    del core_ref
    kv_refs = refs[:chips]
    dqm_ref, dqs_ref = refs[chips], refs[chips + 1]
    part_refs = refs[chips + 2 :]
    tokens = qm_ref.shape[0]
    d = HEAD_DIM
    k = jnp.concatenate([r[0, s] for r in kv_refs for s in range(2)], axis=0)
    v = jnp.concatenate([r[1, s] for r in kv_refs for s in range(2)], axis=0)
    qs = jnp.concatenate([qm_ref[:, :d], qs_ref[:, :d], qm_ref[:, d:], qs_ref[:, d:]], axis=0)
    dos = jnp.concatenate([dm_ref[:, :d], ds_ref[:, :d], dm_ref[:, d:], ds_ref[:, d:]], axis=0)
    contract_last = (((1,), (1,)), ((), ()))
    contract_first = (((0,), (0,)), ((), ()))
    scores = lax.dot_general(qs, k, contract_last, preferred_element_type=jnp.float32)
    scores = scores * SCORE_SCALE + bias_ref[...]
    largest = jnp.max(scores, axis=1, keepdims=True)
    unscaled = jnp.exp(scores - largest)
    attn = unscaled * (1.0 / jnp.sum(unscaled, axis=1, keepdims=True))
    dattn = lax.dot_general(dos, v, contract_last, preferred_element_type=jnp.float32)
    row_delta = jnp.sum(attn * dattn, axis=1, keepdims=True)
    dscores = (attn * (dattn - row_delta)).astype(jnp.bfloat16)
    grad_q = jnp.dot(dscores, k, preferred_element_type=jnp.float32) * SCORE_SCALE
    rows = lambda j: slice(j * tokens, (j + 1) * tokens)
    dqm_ref[:, :d] = grad_q[rows(0)].astype(dqm_ref.dtype)
    dqs_ref[:, :d] = grad_q[rows(1)].astype(dqs_ref.dtype)
    dqm_ref[:, d:] = grad_q[rows(2)].astype(dqm_ref.dtype)
    dqs_ref[:, d:] = grad_q[rows(3)].astype(dqs_ref.dtype)
    grad_k = (
        lax.dot_general(dscores, qs, contract_first, preferred_element_type=jnp.float32)
        * SCORE_SCALE
    )
    grad_v = lax.dot_general(
        attn.astype(jnp.bfloat16), dos, contract_first, preferred_element_type=jnp.float32
    )
    for j, out in enumerate(part_refs):
        for s in range(2):
            out[0, s] = grad_k[rows(2 * j + s)]
            out[1, s] = grad_v[rows(2 * j + s)]


def attention_grads(core, bias, queries, query_sib, grad_out, grad_sib, payloads):
    tokens = queries.shape[0]
    chips = len(payloads)
    key_count = bias.shape[1]
    half = payloads[0].shape[3]
    heads = half // HEAD_DIM
    pair = 2 * HEAD_DIM
    mine = pl.BlockSpec((tokens, pair), lambda g, c: (0, c[0] * heads + g))
    other = pl.BlockSpec((tokens, pair), lambda g, c: (0, g))
    chip = pl.BlockSpec((2, 2, tokens, HEAD_DIM), lambda g, c: (0, 0, 0, g))
    part = jax.ShapeDtypeStruct(payloads[0].shape, jnp.float32)
    rows = 4 * tokens
    flops = 2 * 5 * rows * key_count * HEAD_DIM * heads
    moved_bytes = 2 * 6 * tokens * half * 2 + 2 * 2 * key_count * half * 3 + bias.size * 4
    grid_spec = pltpu.PrefetchScalarGridSpec(
        num_scalar_prefetch=1,
        grid=(heads,),
        in_specs=[pl.BlockSpec(bias.shape, lambda g, c: (0, 0)), mine, other, mine, other]
        + [chip] * chips,
        out_specs=[other, other] + [chip] * chips,
    )
    return pl.pallas_call(
        lambda *refs: attention_kernel(chips, *refs),
        grid_spec=grid_spec,
        out_shape=[jax.ShapeDtypeStruct(query_sib.shape, jnp.bfloat16)] * 2 + [part] * chips,
        cost_estimate=pl.CostEstimate(
            flops=flops, transcendentals=rows * key_count * heads, bytes_accessed=moved_bytes
        ),
    )(core, bias, queries, query_sib, grad_out, grad_sib, *payloads)


def in_core_order(core, mine, theirs):
    return jnp.where(core == 0, jnp.concatenate([mine, theirs], -1), jnp.concatenate([theirs, mine], -1))


def local(queries, key_rows, value_rows, arriving_grad, doc_blocks):
    tokens = queries.shape[1]
    count = lax.axis_size("seq")
    if lax.axis_size("pipe") > 1:
        arriving_grad = passed_along(arriving_grad, "pipe", -1)
    grad_out = arriving_grad[0]
    position = lax.axis_index("seq")
    reach_back = (WINDOW - 1) // tokens + 1
    assert reach_back % 2 == 0 and count % reach_back == 0 and WINDOW % tokens == 0
    routes = Routes(count, reach_back)
    chips = routes.chips
    chip_in_group = (position % reach_back) // 2
    core = position % 2
    other = 1 - core
    key_width = key_rows.shape[2] // 2
    query_width = queries.shape[2] // 2
    keys, values = key_rows[0], value_rows[0]
    kv_sent = jnp.stack(
        [lax.dynamic_slice_in_dim(keys, other * key_width, key_width, 1),
         lax.dynamic_slice_in_dim(values, other * key_width, key_width, 1)]
    )
    kv_sib = moved(kv_sent, routes.sibling)
    kv_mine = jnp.stack(
        [lax.dynamic_slice_in_dim(keys, core * key_width, key_width, 1),
         lax.dynamic_slice_in_dim(values, core * key_width, key_width, 1)]
    )
    own = jnp.stack([kv_mine, kv_sib], axis=1)
    qd_sent = jnp.stack(
        [lax.dynamic_slice_in_dim(queries[0], other * query_width, query_width, 1),
         lax.dynamic_slice_in_dim(grad_out, other * query_width, query_width, 1)]
    )
    qd_sib = moved(qd_sent, routes.sibling)
    payloads = gather_window(own, routes, chip_in_group)

    chip = position // 2
    block_of = lambda m, s: 2 * m + jnp.where(s == 0, core, other)
    key_blocks = [block_of(chip - chips + j, s) for j in range(chips + 1) for s in range(2)]
    token_doc = jnp.repeat(doc_blocks[0], MBLK)
    pad = (reach_back + 2) * tokens
    doc_pad = jnp.concatenate([jnp.full((pad,), -1, jnp.int32), token_doc])
    key_doc = jnp.concatenate(
        [lax.dynamic_slice_in_dim(doc_pad, b * tokens + pad, tokens, 0) for b in key_blocks]
    )
    offsets = jnp.arange(tokens, dtype=jnp.int32)
    key_pos = jnp.concatenate([b * tokens + offsets for b in key_blocks])
    masks = []
    for block in (position, position ^ 1):
        query_pos = block * tokens + offsets
        query_doc = lax.dynamic_slice_in_dim(token_doc, block * tokens, tokens, 0)
        distance = query_pos[:, None] - key_pos[None, :]
        allowed = (distance >= 0) & (distance < WINDOW) & (query_doc[:, None] == key_doc[None, :])
        masks.append(jnp.where(allowed, 0.0, MASKED_SCORE).astype(jnp.float32))
    bias = jnp.concatenate(masks + masks, axis=0)

    outs = attention_grads(
        core[None].astype(jnp.int32), bias, queries[0], qd_sib[0], grad_out, qd_sib[1], payloads
    )
    dq_mine, dq_sib, parts = outs[0], outs[1], outs[2:]
    summed = scatter_window(parts, routes)
    sent = jnp.concatenate(
        [summed[0, 1].astype(jnp.bfloat16), summed[1, 1].astype(jnp.bfloat16), dq_sib], axis=-1
    )
    got = moved(sent, routes.sibling)
    grad_key = in_core_order(core, summed[0, 0].astype(jnp.bfloat16), got[:, :key_width])
    grad_value = in_core_order(
        core, summed[1, 0].astype(jnp.bfloat16), got[:, key_width : 2 * key_width]
    )
    grad_query = in_core_order(core, dq_mine, got[:, 2 * key_width :])
    return (grad_query[None], grad_key[None], grad_value[None])


def solution(mesh):
    placed = (
        P("pipe", "seq", None),
        P("pipe", "seq", None),
        P("pipe", "seq", None),
        P("pipe", "seq", None),
        P("pipe", None),
    )
    return jax.shard_map(
        local,
        mesh=mesh,
        in_specs=placed,
        out_specs=(P("pipe", "seq", None), P("pipe", "seq", None), P("pipe", "seq", None)),
        check_vma=False,
    )
```

```python
import jax
import jax.numpy as jnp
from jax import lax
from jax.experimental import pallas as pl
from jax.experimental.pallas import tpu as pltpu
from jax.sharding import PartitionSpec as P

HEADS = 32
KV_HEADS = 16
HEAD_DIM = 128
WINDOW = 1024
MBLK = 128


SCORE_SCALE = 168.0 ** (-0.5)
MASKED_SCORE = -1e30


def passed_along(value, axis, steps):
    count = lax.axis_size(axis)
    pairs = [(source, (source + steps) % count) for source in range(count)]
    return lax.ppermute(value, axis, pairs)


def moved(value, pairs):
    return lax.ppermute(value, "seq", pairs)


def reverse(pairs):
    return [(t, s) for (s, t) in pairs]


class Routes:
    def __init__(self, count, reach):
        self.reach = reach
        self.chips = reach // 2
        group_chip = lambda i: (i % reach) // 2
        self.hop = [(i, i + reach) for i in range(count - reach)]
        self.up = []
        self.down = []
        for e in range(1, self.chips):
            self.up.append([(i, i + 2 * e) for i in range(count) if group_chip(i) + e < self.chips])
            self.down.append(
                [(i, i + 2 * e - reach) for i in range(count) if group_chip(i) + e >= self.chips]
            )
        self.sibling = [(i, i ^ 1) for i in range(count)]


def gather_window(own, routes, chip_in_group):
    prev = moved(own, routes.hop)
    recv = []
    for e in range(1, routes.chips):
        sent = jnp.where(chip_in_group + e < routes.chips, own, prev)
        recv.append(moved(sent, routes.up[e - 1] + routes.down[e - 1]))
    return [prev] + recv[::-1] + [own]


def scatter_window(parts, routes, chip_in_group):
    link = jnp.bfloat16
    chips = routes.chips
    prev, own = parts[0], parts[-1]
    recv = parts[1:-1][::-1]
    for e in range(1, chips):
        pairs = reverse(routes.up[e - 1] + routes.down[e - 1])
        got = moved(recv[e - 1].astype(link), pairs).astype(jnp.float32)
        upward = chip_in_group + e < chips
        own = own + jnp.where(upward, got, 0.0)
        prev = prev + jnp.where(upward, 0.0, got)
    return own + moved(prev.astype(link), reverse(routes.hop)).astype(jnp.float32)


def attention_kernel(chips, core_ref, bias_ref, qm_ref, qs_ref, dm_ref, ds_ref, *refs):
    del core_ref
    kv_refs = refs[:chips]
    dqm_ref, dqs_ref = refs[chips], refs[chips + 1]
    part_refs = refs[chips + 2 :]
    tokens = qm_ref.shape[0]
    d = HEAD_DIM
    k = jnp.concatenate([r[0, s] for r in kv_refs for s in range(2)], axis=0)
    v = jnp.concatenate([r[1, s] for r in kv_refs for s in range(2)], axis=0)
    qs = jnp.concatenate([qm_ref[:, :d], qs_ref[:, :d], qm_ref[:, d:], qs_ref[:, d:]], axis=0)
    dos = jnp.concatenate([dm_ref[:, :d], ds_ref[:, :d], dm_ref[:, d:], ds_ref[:, d:]], axis=0)
    contract_last = (((1,), (1,)), ((), ()))
    contract_first = (((0,), (0,)), ((), ()))
    scores = lax.dot_general(qs, k, contract_last, preferred_element_type=jnp.float32)
    scores = scores * SCORE_SCALE + bias_ref[...]
    largest = jnp.max(scores, axis=1, keepdims=True)
    unscaled = jnp.exp(scores - largest)
    attn = unscaled * (1.0 / jnp.sum(unscaled, axis=1, keepdims=True))
    dattn = lax.dot_general(dos, v, contract_last, preferred_element_type=jnp.float32)
    row_delta = jnp.sum(attn * dattn, axis=1, keepdims=True)
    dscores = (attn * (dattn - row_delta)).astype(jnp.bfloat16)
    grad_q = jnp.dot(dscores, k, preferred_element_type=jnp.float32) * SCORE_SCALE
    rows = lambda j: slice(j * tokens, (j + 1) * tokens)
    dqm_ref[:, :d] = grad_q[rows(0)].astype(dqm_ref.dtype)
    dqs_ref[:, :d] = grad_q[rows(1)].astype(dqs_ref.dtype)
    dqm_ref[:, d:] = grad_q[rows(2)].astype(dqm_ref.dtype)
    dqs_ref[:, d:] = grad_q[rows(3)].astype(dqs_ref.dtype)
    grad_k = (
        lax.dot_general(dscores, qs, contract_first, preferred_element_type=jnp.float32)
        * SCORE_SCALE
    )
    grad_v = lax.dot_general(
        attn.astype(jnp.bfloat16), dos, contract_first, preferred_element_type=jnp.float32
    )
    for j, out in enumerate(part_refs):
        for s in range(2):
            out[0, s] = grad_k[rows(2 * j + s)]
            out[1, s] = grad_v[rows(2 * j + s)]


def attention_grads(core, bias, queries, query_sib, grad_out, grad_sib, payloads):
    tokens = queries.shape[0]
    chips = len(payloads)
    key_count = bias.shape[1]
    half = payloads[0].shape[3]
    heads = half // HEAD_DIM
    pair = 2 * HEAD_DIM
    mine = pl.BlockSpec((tokens, pair), lambda g, c: (0, c[0] * heads + g))
    other = pl.BlockSpec((tokens, pair), lambda g, c: (0, g))
    chip = pl.BlockSpec((2, 2, tokens, HEAD_DIM), lambda g, c: (0, 0, 0, g))
    part = jax.ShapeDtypeStruct(payloads[0].shape, jnp.float32)
    rows = 4 * tokens
    flops = 2 * 5 * rows * key_count * HEAD_DIM * heads
    moved_bytes = 2 * 6 * tokens * half * 2 + 2 * 2 * key_count * half * 3 + bias.size * 4
    grid_spec = pltpu.PrefetchScalarGridSpec(
        num_scalar_prefetch=1,
        grid=(heads,),
        in_specs=[pl.BlockSpec(bias.shape, lambda g, c: (0, 0)), mine, other, mine, other]
        + [chip] * chips,
        out_specs=[other, other] + [chip] * chips,
    )
    return pl.pallas_call(
        lambda *refs: attention_kernel(chips, *refs),
        grid_spec=grid_spec,
        out_shape=[jax.ShapeDtypeStruct(query_sib.shape, jnp.bfloat16)] * 2 + [part] * chips,
        cost_estimate=pl.CostEstimate(
            flops=flops, transcendentals=rows * key_count * heads, bytes_accessed=moved_bytes
        ),
    )(core, bias, queries, query_sib, grad_out, grad_sib, *payloads)


def in_core_order(core, mine, theirs):
    return jnp.where(core == 0, jnp.concatenate([mine, theirs], -1), jnp.concatenate([theirs, mine], -1))


def local(queries, key_rows, value_rows, arriving_grad, doc_blocks):
    tokens = queries.shape[1]
    count = lax.axis_size("seq")
    if lax.axis_size("pipe") > 1:
        arriving_grad = passed_along(arriving_grad, "pipe", -1)
    grad_out = arriving_grad[0]
    position = lax.axis_index("seq")
    reach_back = (WINDOW - 1) // tokens + 1
    assert reach_back % 2 == 0 and count % reach_back == 0 and WINDOW % tokens == 0
    routes = Routes(count, reach_back)
    chips = routes.chips
    chip_in_group = (position % reach_back) // 2
    core = position % 2
    other = 1 - core
    key_width = key_rows.shape[2] // 2
    query_width = queries.shape[2] // 2
    keys, values = key_rows[0], value_rows[0]
    kv_sent = jnp.stack(
        [lax.dynamic_slice_in_dim(keys, other * key_width, key_width, 1),
         lax.dynamic_slice_in_dim(values, other * key_width, key_width, 1)]
    )
    kv_sib = moved(kv_sent, routes.sibling)
    kv_mine = jnp.stack(
        [lax.dynamic_slice_in_dim(keys, core * key_width, key_width, 1),
         lax.dynamic_slice_in_dim(values, core * key_width, key_width, 1)]
    )
    own = jnp.stack([kv_mine, kv_sib], axis=1)
    qd_sent = jnp.stack(
        [lax.dynamic_slice_in_dim(queries[0], other * query_width, query_width, 1),
         lax.dynamic_slice_in_dim(grad_out, other * query_width, query_width, 1)]
    )
    qd_sib = moved(qd_sent, routes.sibling)
    payloads = gather_window(own, routes, chip_in_group)

    chip = position // 2
    block_of = lambda m, s: 2 * m + jnp.where(s == 0, core, other)
    key_blocks = [block_of(chip - chips + j, s) for j in range(chips + 1) for s in range(2)]
    token_doc = jnp.repeat(doc_blocks[0], MBLK)
    pad = (reach_back + 2) * tokens
    doc_pad = jnp.concatenate([jnp.full((pad,), -1, jnp.int32), token_doc])
    key_doc = jnp.concatenate(
        [lax.dynamic_slice_in_dim(doc_pad, b * tokens + pad, tokens, 0) for b in key_blocks]
    )
    offsets = jnp.arange(tokens, dtype=jnp.int32)
    key_pos = jnp.concatenate([b * tokens + offsets for b in key_blocks])
    masks = []
    for block in (position, position ^ 1):
        query_pos = block * tokens + offsets
        query_doc = lax.dynamic_slice_in_dim(token_doc, block * tokens, tokens, 0)
        distance = query_pos[:, None] - key_pos[None, :]
        allowed = (distance >= 0) & (distance < WINDOW) & (query_doc[:, None] == key_doc[None, :])
        masks.append(jnp.where(allowed, 0.0, MASKED_SCORE).astype(jnp.float32))
    bias = jnp.concatenate(masks + masks, axis=0)

    outs = attention_grads(
        core[None].astype(jnp.int32), bias, queries[0], qd_sib[0], grad_out, qd_sib[1], payloads
    )
    dq_mine, dq_sib, parts = outs[0], outs[1], outs[2:]
    summed = scatter_window(parts, routes, chip_in_group)
    sent = jnp.concatenate(
        [summed[0, 1].astype(jnp.bfloat16), summed[1, 1].astype(jnp.bfloat16), dq_sib], axis=-1
    )
    got = moved(sent, routes.sibling)
    grad_key = in_core_order(core, summed[0, 0].astype(jnp.bfloat16), got[:, :key_width])
    grad_value = in_core_order(
        core, summed[1, 0].astype(jnp.bfloat16), got[:, key_width : 2 * key_width]
    )
    grad_query = in_core_order(core, dq_mine, got[:, 2 * key_width :])
    return (grad_query[None], grad_key[None], grad_value[None])


def solution(mesh):
    placed = (
        P("pipe", "seq", None),
        P("pipe", "seq", None),
        P("pipe", "seq", None),
        P("pipe", "seq", None),
        P("pipe", None),
    )
    return jax.shard_map(
        local,
        mesh=mesh,
        in_specs=placed,
        out_specs=(P("pipe", "seq", None), P("pipe", "seq", None), P("pipe", "seq", None)),
        check_vma=False,
    )
```

```python
import jax
import jax.numpy as jnp
from jax import lax
from jax.experimental import pallas as pl
from jax.experimental.pallas import tpu as pltpu
from jax.sharding import PartitionSpec as P

HEADS = 32
KV_HEADS = 16
HEAD_DIM = 128
WINDOW = 1024
MBLK = 128


SCORE_SCALE = 168.0 ** (-0.5)
MASKED_SCORE = -1e30


def passed_along(value, axis, steps):
    count = lax.axis_size(axis)
    pairs = [(source, (source + steps) % count) for source in range(count)]
    return lax.ppermute(value, axis, pairs)


def moved(value, pairs):
    return lax.ppermute(value, "seq", pairs)


def reverse(pairs):
    return [(t, s) for (s, t) in pairs]


class Routes:
    def __init__(self, count, reach):
        self.reach = reach
        self.chips = reach // 2
        group_chip = lambda i: (i % reach) // 2
        self.hop = [(i, i + reach) for i in range(count - reach)]
        self.up = []
        self.down = []
        for e in range(1, self.chips):
            self.up.append([(i, i + 2 * e) for i in range(count) if group_chip(i) + e < self.chips])
            self.down.append(
                [(i, i + 2 * e - reach) for i in range(count) if group_chip(i) + e >= self.chips]
            )
        self.sibling = [(i, i ^ 1) for i in range(count)]


def gather_window(own, routes, chip_in_group):
    prev = moved(own, routes.hop)
    recv = []
    for e in range(1, routes.chips):
        sent = jnp.where(chip_in_group + e < routes.chips, own, prev)
        recv.append(moved(sent, routes.up[e - 1] + routes.down[e - 1]))
    return [prev] + recv[::-1] + [own]


def scatter_window(parts, routes, chip_in_group):
    link = jnp.bfloat16
    chips = routes.chips
    prev, own = parts[0], parts[-1]
    recv = parts[1:-1][::-1]
    for e in range(1, chips):
        pairs = reverse(routes.up[e - 1] + routes.down[e - 1])
        got = moved(recv[e - 1].astype(link), pairs).astype(jnp.float32)
        upward = chip_in_group + e < chips
        own = own + jnp.where(upward, got, 0.0)
        prev = prev + jnp.where(upward, 0.0, got)
    return own + moved(prev.astype(link), reverse(routes.hop)).astype(jnp.float32)


def attention_kernel(chips, core_ref, bias_ref, qm_ref, qs_ref, dm_ref, ds_ref, *refs):
    del core_ref
    kv_refs = refs[:chips]
    dqm_ref, dqs_ref = refs[chips], refs[chips + 1]
    part_refs = refs[chips + 2 :]
    tokens = qm_ref.shape[0]
    d = HEAD_DIM
    k = jnp.concatenate([r[0, s] for r in kv_refs for s in range(2)], axis=0)
    v = jnp.concatenate([r[1, s] for r in kv_refs for s in range(2)], axis=0)
    qs = jnp.concatenate([qm_ref[:, :d], qs_ref[:, :d], qm_ref[:, d:], qs_ref[:, d:]], axis=0)
    dos = jnp.concatenate([dm_ref[:, :d], ds_ref[:, :d], dm_ref[:, d:], ds_ref[:, d:]], axis=0)
    contract_last = (((1,), (1,)), ((), ()))
    contract_first = (((0,), (0,)), ((), ()))
    scores = lax.dot_general(qs, k, contract_last, preferred_element_type=jnp.float32)
    scores = scores * SCORE_SCALE + bias_ref[...]
    largest = jnp.max(scores, axis=1, keepdims=True)
    unscaled = jnp.exp(scores - largest)
    attn = unscaled * (1.0 / jnp.sum(unscaled, axis=1, keepdims=True))
    dattn = lax.dot_general(dos, v, contract_last, preferred_element_type=jnp.float32)
    row_delta = jnp.sum(attn * dattn, axis=1, keepdims=True)
    dscores = (attn * (dattn - row_delta)).astype(jnp.bfloat16)
    grad_q = jnp.dot(dscores, k, preferred_element_type=jnp.float32) * SCORE_SCALE
    rows = lambda j: slice(j * tokens, (j + 1) * tokens)
    dqm_ref[:, :d] = grad_q[rows(0)].astype(dqm_ref.dtype)
    dqs_ref[:, :d] = grad_q[rows(1)].astype(dqs_ref.dtype)
    dqm_ref[:, d:] = grad_q[rows(2)].astype(dqm_ref.dtype)
    dqs_ref[:, d:] = grad_q[rows(3)].astype(dqs_ref.dtype)
    grad_k = (
        lax.dot_general(dscores, qs, contract_first, preferred_element_type=jnp.float32)
        * SCORE_SCALE
    )
    grad_v = lax.dot_general(
        attn.astype(jnp.bfloat16), dos, contract_first, preferred_element_type=jnp.float32
    )
    for j, out in enumerate(part_refs):
        for s in range(2):
            out[0, s] = grad_k[rows(2 * j + s)]
            out[1, s] = grad_v[rows(2 * j + s)]


def attention_grads(core, bias, queries, query_sib, grad_out, grad_sib, payloads):
    tokens = queries.shape[0]
    chips = len(payloads)
    key_count = bias.shape[1]
    half = payloads[0].shape[3]
    heads = half // HEAD_DIM
    pair = 2 * HEAD_DIM
    mine = pl.BlockSpec((tokens, pair), lambda g, c: (0, c[0] * heads + g))
    other = pl.BlockSpec((tokens, pair), lambda g, c: (0, g))
    chip = pl.BlockSpec((2, 2, tokens, HEAD_DIM), lambda g, c: (0, 0, 0, g))
    part = jax.ShapeDtypeStruct(payloads[0].shape, jnp.float32)
    rows = 4 * tokens
    flops = 2 * 5 * rows * key_count * HEAD_DIM * heads
    moved_bytes = 2 * 6 * tokens * half * 2 + 2 * 2 * key_count * half * 3 + bias.size * 4
    grid_spec = pltpu.PrefetchScalarGridSpec(
        num_scalar_prefetch=1,
        grid=(heads,),
        in_specs=[pl.BlockSpec(bias.shape, lambda g, c: (0, 0)), mine, other, mine, other]
        + [chip] * chips,
        out_specs=[other, other] + [chip] * chips,
    )
    return pl.pallas_call(
        lambda *refs: attention_kernel(chips, *refs),
        grid_spec=grid_spec,
        out_shape=[jax.ShapeDtypeStruct(query_sib.shape, jnp.bfloat16)] * 2 + [part] * chips,
        cost_estimate=pl.CostEstimate(
            flops=flops, transcendentals=rows * key_count * heads, bytes_accessed=moved_bytes
        ),
    )(core, bias, queries, query_sib, grad_out, grad_sib, *payloads)


def in_core_order(core, mine, theirs):
    return jnp.where(core == 0, jnp.concatenate([mine, theirs], -1), jnp.concatenate([theirs, mine], -1))


def local(queries, key_rows, value_rows, arriving_grad, doc_blocks):
    tokens = queries.shape[1]
    count = lax.axis_size("seq")
    if lax.axis_size("pipe") > 1:
        arriving_grad = passed_along(arriving_grad, "pipe", -1)
    grad_out = arriving_grad[0]
    position = lax.axis_index("seq")
    reach_back = (WINDOW - 1) // tokens + 1
    assert reach_back % 2 == 0 and count % reach_back == 0 and WINDOW % tokens == 0
    routes = Routes(count, reach_back)
    chips = routes.chips
    chip_in_group = (position % reach_back) // 2
    core = position % 2
    other = 1 - core
    key_width = key_rows.shape[2] // 2
    query_width = queries.shape[2] // 2
    keys, values = key_rows[0], value_rows[0]
    kv_sent = jnp.stack(
        [lax.dynamic_slice_in_dim(keys, other * key_width, key_width, 1),
         lax.dynamic_slice_in_dim(values, other * key_width, key_width, 1)]
    )
    kv_sib = moved(kv_sent, routes.sibling)
    kv_mine = jnp.stack(
        [lax.dynamic_slice_in_dim(keys, core * key_width, key_width, 1),
         lax.dynamic_slice_in_dim(values, core * key_width, key_width, 1)]
    )
    own = jnp.stack([kv_mine, kv_sib], axis=1)
    payloads = gather_window(own, routes, chip_in_group)
    (query_rows, grad_rows, doc_row), _ = lax.optimization_barrier(
        ((queries[0], grad_out, doc_blocks[0]), payloads[0])
    )
    qd_sent = jnp.stack(
        [lax.dynamic_slice_in_dim(query_rows, other * query_width, query_width, 1),
         lax.dynamic_slice_in_dim(grad_rows, other * query_width, query_width, 1)]
    )
    qd_sib = moved(qd_sent, routes.sibling)

    chip = position // 2
    block_of = lambda m, s: 2 * m + jnp.where(s == 0, core, other)
    key_blocks = [block_of(chip - chips + j, s) for j in range(chips + 1) for s in range(2)]
    token_doc = jnp.repeat(doc_row, MBLK)
    pad = (reach_back + 2) * tokens
    doc_pad = jnp.concatenate([jnp.full((pad,), -1, jnp.int32), token_doc])
    key_doc = jnp.concatenate(
        [lax.dynamic_slice_in_dim(doc_pad, b * tokens + pad, tokens, 0) for b in key_blocks]
    )
    offsets = jnp.arange(tokens, dtype=jnp.int32)
    key_pos = jnp.concatenate([b * tokens + offsets for b in key_blocks])
    masks = []
    for block in (position, position ^ 1):
        query_pos = block * tokens + offsets
        query_doc = lax.dynamic_slice_in_dim(token_doc, block * tokens, tokens, 0)
        distance = query_pos[:, None] - key_pos[None, :]
        allowed = (distance >= 0) & (distance < WINDOW) & (query_doc[:, None] == key_doc[None, :])
        masks.append(jnp.where(allowed, 0.0, MASKED_SCORE).astype(jnp.float32))
    bias = jnp.concatenate(masks + masks, axis=0)

    outs = attention_grads(
        core[None].astype(jnp.int32), bias, queries[0], qd_sib[0], grad_out, qd_sib[1], payloads
    )
    dq_mine, dq_sib, parts = outs[0], outs[1], outs[2:]
    summed = scatter_window(parts, routes, chip_in_group)
    sent = jnp.concatenate(
        [summed[0, 1].astype(jnp.bfloat16), summed[1, 1].astype(jnp.bfloat16), dq_sib], axis=-1
    )
    got = moved(sent, routes.sibling)
    grad_key = in_core_order(core, summed[0, 0].astype(jnp.bfloat16), got[:, :key_width])
    grad_value = in_core_order(
        core, summed[1, 0].astype(jnp.bfloat16), got[:, key_width : 2 * key_width]
    )
    grad_query = in_core_order(core, dq_mine, got[:, 2 * key_width :])
    return (grad_query[None], grad_key[None], grad_value[None])


def solution(mesh):
    placed = (
        P("pipe", "seq", None),
        P("pipe", "seq", None),
        P("pipe", "seq", None),
        P("pipe", "seq", None),
        P("pipe", None),
    )
    return jax.shard_map(
        local,
        mesh=mesh,
        in_specs=placed,
        out_specs=(P("pipe", "seq", None), P("pipe", "seq", None), P("pipe", "seq", None)),
        check_vma=False,
    )
```

```python
import jax
import jax.numpy as jnp
from jax import lax
from jax.experimental import pallas as pl
from jax.experimental.pallas import tpu as pltpu
from jax.sharding import PartitionSpec as P

HEADS = 32
KV_HEADS = 16
HEAD_DIM = 128
WINDOW = 1024
MBLK = 128


SCORE_SCALE = 168.0 ** (-0.5)
MASKED_SCORE = -1e30


def passed_along(value, axis, steps):
    count = lax.axis_size(axis)
    pairs = [(source, (source + steps) % count) for source in range(count)]
    return lax.ppermute(value, axis, pairs)


def moved(value, pairs):
    return lax.ppermute(value, "seq", pairs)


def reverse(pairs):
    return [(t, s) for (s, t) in pairs]


class Routes:
    def __init__(self, count, reach):
        self.reach = reach
        self.chips = reach // 2
        group_chip = lambda i: (i % reach) // 2
        self.hop = [(i, i + reach) for i in range(count - reach)]
        self.up = []
        self.down = []
        for e in range(1, self.chips):
            self.up.append([(i, i + 2 * e) for i in range(count) if group_chip(i) + e < self.chips])
            self.down.append(
                [(i, i + 2 * e - reach) for i in range(count) if group_chip(i) + e >= self.chips]
            )
        self.sibling = [(i, i ^ 1) for i in range(count)]


def gather_window(own, routes, chip_in_group):
    prev = moved(own, routes.hop)
    recv = []
    for e in range(1, routes.chips):
        sent = jnp.where(chip_in_group + e < routes.chips, own, prev)
        recv.append(moved(sent, routes.up[e - 1] + routes.down[e - 1]))
    return [prev] + recv[::-1] + [own]


def scatter_window(parts, routes, chip_in_group):
    link = jnp.bfloat16
    chips = routes.chips
    prev, own = parts[0], parts[-1]
    recv = parts[1:-1][::-1]
    for e in range(1, chips):
        pairs = reverse(routes.up[e - 1] + routes.down[e - 1])
        got = moved(recv[e - 1].astype(link), pairs).astype(jnp.float32)
        upward = chip_in_group + e < chips
        own = own + jnp.where(upward, got, 0.0)
        prev = prev + jnp.where(upward, 0.0, got)
    return own + moved(prev.astype(link), reverse(routes.hop)).astype(jnp.float32)


def attention_kernel(chips, core_ref, bias_ref, qm_ref, qs_ref, dm_ref, ds_ref, *refs):
    del core_ref
    kv_refs = refs[:chips]
    dqm_ref, dqs_ref = refs[chips], refs[chips + 1]
    part_refs = refs[chips + 2 :]
    tokens = qm_ref.shape[0]
    d = HEAD_DIM
    k = jnp.concatenate([r[0, s] for r in kv_refs for s in range(2)], axis=0)
    v = jnp.concatenate([r[1, s] for r in kv_refs for s in range(2)], axis=0)
    qs = jnp.concatenate([qm_ref[:, :d], qs_ref[:, :d], qm_ref[:, d:], qs_ref[:, d:]], axis=0)
    dos = jnp.concatenate([dm_ref[:, :d], ds_ref[:, :d], dm_ref[:, d:], ds_ref[:, d:]], axis=0)
    contract_last = (((1,), (1,)), ((), ()))
    contract_first = (((0,), (0,)), ((), ()))
    scores = lax.dot_general(qs, k, contract_last, preferred_element_type=jnp.float32)
    scores = scores * SCORE_SCALE + bias_ref[...]
    largest = jnp.max(scores, axis=1, keepdims=True)
    unscaled = jnp.exp(scores - largest)
    attn = unscaled * (1.0 / jnp.sum(unscaled, axis=1, keepdims=True))
    dattn = lax.dot_general(dos, v, contract_last, preferred_element_type=jnp.float32)
    row_delta = jnp.sum(attn * dattn, axis=1, keepdims=True)
    dscores = (attn * (dattn - row_delta)).astype(jnp.bfloat16)
    grad_q = jnp.dot(dscores, k, preferred_element_type=jnp.float32) * SCORE_SCALE
    rows = lambda j: slice(j * tokens, (j + 1) * tokens)
    dqm_ref[:, :d] = grad_q[rows(0)].astype(dqm_ref.dtype)
    dqs_ref[:, :d] = grad_q[rows(1)].astype(dqs_ref.dtype)
    dqm_ref[:, d:] = grad_q[rows(2)].astype(dqm_ref.dtype)
    dqs_ref[:, d:] = grad_q[rows(3)].astype(dqs_ref.dtype)
    grad_k = (
        lax.dot_general(dscores, qs, contract_first, preferred_element_type=jnp.float32)
        * SCORE_SCALE
    )
    grad_v = lax.dot_general(
        attn.astype(jnp.bfloat16), dos, contract_first, preferred_element_type=jnp.float32
    )
    for j, out in enumerate(part_refs):
        for s in range(2):
            out[0, s] = grad_k[rows(2 * j + s)].astype(out.dtype)
            out[1, s] = grad_v[rows(2 * j + s)].astype(out.dtype)


def attention_grads(core, bias, queries, query_sib, grad_out, grad_sib, payloads):
    tokens = queries.shape[0]
    chips = len(payloads)
    key_count = bias.shape[1]
    half = payloads[0].shape[3]
    heads = half // HEAD_DIM
    pair = 2 * HEAD_DIM
    mine = pl.BlockSpec((tokens, pair), lambda g, c: (0, c[0] * heads + g))
    other = pl.BlockSpec((tokens, pair), lambda g, c: (0, g))
    chip = pl.BlockSpec((2, 2, tokens, HEAD_DIM), lambda g, c: (0, 0, 0, g))
    part = jax.ShapeDtypeStruct(payloads[0].shape, jnp.float32)
    rows = 4 * tokens
    flops = 2 * 5 * rows * key_count * HEAD_DIM * heads
    moved_bytes = 2 * 6 * tokens * half * 2 + 2 * 2 * key_count * half * 3 + bias.size * 4
    grid_spec = pltpu.PrefetchScalarGridSpec(
        num_scalar_prefetch=1,
        grid=(heads,),
        in_specs=[pl.BlockSpec(bias.shape, lambda g, c: (0, 0)), mine, other, mine, other]
        + [chip] * chips,
        out_specs=[other, other] + [chip] * chips,
    )
    return pl.pallas_call(
        lambda *refs: attention_kernel(chips, *refs),
        grid_spec=grid_spec,
        out_shape=[jax.ShapeDtypeStruct(query_sib.shape, jnp.bfloat16)] * 2
        + [part]
        + [jax.ShapeDtypeStruct(part.shape, jnp.bfloat16)] * (chips - 2)
        + [part],
        cost_estimate=pl.CostEstimate(
            flops=flops, transcendentals=rows * key_count * heads, bytes_accessed=moved_bytes
        ),
    )(core, bias, queries, query_sib, grad_out, grad_sib, *payloads)


def in_core_order(core, mine, theirs):
    return jnp.where(core == 0, jnp.concatenate([mine, theirs], -1), jnp.concatenate([theirs, mine], -1))


def local(queries, key_rows, value_rows, arriving_grad, doc_blocks):
    tokens = queries.shape[1]
    count = lax.axis_size("seq")
    if lax.axis_size("pipe") > 1:
        arriving_grad = passed_along(arriving_grad, "pipe", -1)
    grad_out = arriving_grad[0]
    position = lax.axis_index("seq")
    reach_back = (WINDOW - 1) // tokens + 1
    assert reach_back % 2 == 0 and count % reach_back == 0 and WINDOW % tokens == 0
    routes = Routes(count, reach_back)
    chips = routes.chips
    chip_in_group = (position % reach_back) // 2
    core = position % 2
    other = 1 - core
    key_width = key_rows.shape[2] // 2
    query_width = queries.shape[2] // 2
    keys, values = key_rows[0], value_rows[0]
    kv_sent = jnp.stack(
        [lax.dynamic_slice_in_dim(keys, other * key_width, key_width, 1),
         lax.dynamic_slice_in_dim(values, other * key_width, key_width, 1)]
    )
    kv_sib = moved(kv_sent, routes.sibling)
    kv_mine = jnp.stack(
        [lax.dynamic_slice_in_dim(keys, core * key_width, key_width, 1),
         lax.dynamic_slice_in_dim(values, core * key_width, key_width, 1)]
    )
    own = jnp.stack([kv_mine, kv_sib], axis=1)
    payloads = gather_window(own, routes, chip_in_group)
    (query_rows, grad_rows, doc_row), _ = lax.optimization_barrier(
        ((queries[0], grad_out, doc_blocks[0]), payloads[0])
    )
    qd_sent = jnp.stack(
        [lax.dynamic_slice_in_dim(query_rows, other * query_width, query_width, 1),
         lax.dynamic_slice_in_dim(grad_rows, other * query_width, query_width, 1)]
    )
    qd_sib = moved(qd_sent, routes.sibling)

    chip = position // 2
    block_of = lambda m, s: 2 * m + jnp.where(s == 0, core, other)
    key_blocks = [block_of(chip - chips + j, s) for j in range(chips + 1) for s in range(2)]
    token_doc = jnp.repeat(doc_row, MBLK)
    pad = (reach_back + 2) * tokens
    doc_pad = jnp.concatenate([jnp.full((pad,), -1, jnp.int32), token_doc])
    key_doc = jnp.concatenate(
        [lax.dynamic_slice_in_dim(doc_pad, b * tokens + pad, tokens, 0) for b in key_blocks]
    )
    offsets = jnp.arange(tokens, dtype=jnp.int32)
    key_pos = jnp.concatenate([b * tokens + offsets for b in key_blocks])
    masks = []
    for block in (position, position ^ 1):
        query_pos = block * tokens + offsets
        query_doc = lax.dynamic_slice_in_dim(token_doc, block * tokens, tokens, 0)
        distance = query_pos[:, None] - key_pos[None, :]
        allowed = (distance >= 0) & (distance < WINDOW) & (query_doc[:, None] == key_doc[None, :])
        masks.append(jnp.where(allowed, 0.0, MASKED_SCORE).astype(jnp.float32))
    bias = jnp.concatenate(masks + masks, axis=0)

    outs = attention_grads(
        core[None].astype(jnp.int32), bias, queries[0], qd_sib[0], grad_out, qd_sib[1], payloads
    )
    dq_mine, dq_sib, parts = outs[0], outs[1], outs[2:]
    summed = scatter_window(parts, routes, chip_in_group)
    sent = jnp.concatenate(
        [summed[0, 1].astype(jnp.bfloat16), summed[1, 1].astype(jnp.bfloat16), dq_sib], axis=-1
    )
    got = moved(sent, routes.sibling)
    grad_key = in_core_order(core, summed[0, 0].astype(jnp.bfloat16), got[:, :key_width])
    grad_value = in_core_order(
        core, summed[1, 0].astype(jnp.bfloat16), got[:, key_width : 2 * key_width]
    )
    grad_query = in_core_order(core, dq_mine, got[:, 2 * key_width :])
    return (grad_query[None], grad_key[None], grad_value[None])


def solution(mesh):
    placed = (
        P("pipe", "seq", None),
        P("pipe", "seq", None),
        P("pipe", "seq", None),
        P("pipe", "seq", None),
        P("pipe", None),
    )
    return jax.shard_map(
        local,
        mesh=mesh,
        in_specs=placed,
        out_specs=(P("pipe", "seq", None), P("pipe", "seq", None), P("pipe", "seq", None)),
        check_vma=False,
    )
```

```python
import jax
import jax.numpy as jnp
from jax import lax
from jax.experimental import pallas as pl
from jax.experimental.pallas import tpu as pltpu
from jax.sharding import PartitionSpec as P

HEADS = 32
KV_HEADS = 16
HEAD_DIM = 128
WINDOW = 1024
MBLK = 128


SCORE_SCALE = 168.0 ** (-0.5)
MASKED_SCORE = -1e30


def passed_along(value, axis, steps):
    count = lax.axis_size(axis)
    pairs = [(source, (source + steps) % count) for source in range(count)]
    return lax.ppermute(value, axis, pairs)


def moved(value, pairs):
    return lax.ppermute(value, "seq", pairs)


def reverse(pairs):
    return [(t, s) for (s, t) in pairs]


class Routes:
    def __init__(self, count, reach):
        self.reach = reach
        self.chips = reach // 2
        group_chip = lambda i: (i % reach) // 2
        self.hop = [(i, i + reach) for i in range(count - reach)]
        self.up = []
        self.down = []
        for e in range(1, self.chips):
            self.up.append([(i, i + 2 * e) for i in range(count) if group_chip(i) + e < self.chips])
            self.down.append(
                [(i, i + 2 * e - reach) for i in range(count) if group_chip(i) + e >= self.chips]
            )
        self.sibling = [(i, i ^ 1) for i in range(count)]


def gather_window(own, routes, chip_in_group):
    prev = moved(own, routes.hop)
    recv = []
    for e in range(1, routes.chips):
        sent = jnp.where(chip_in_group + e < routes.chips, own, prev)
        recv.append(moved(sent, routes.up[e - 1] + routes.down[e - 1]))
    return [prev] + recv[::-1] + [own]


def scatter_window(parts, routes, chip_in_group):
    link = jnp.bfloat16
    chips = routes.chips
    prev, own = parts[0], parts[-1]
    recv = parts[1:-1][::-1]
    for e in range(1, chips):
        pairs = reverse(routes.up[e - 1] + routes.down[e - 1])
        got = moved(recv[e - 1].astype(link), pairs).astype(jnp.float32)
        upward = chip_in_group + e < chips
        own = own + jnp.where(upward, got, 0.0)
        prev = prev + jnp.where(upward, 0.0, got)
    return own + moved(prev.astype(link), reverse(routes.hop)).astype(jnp.float32)


def attention_kernel(chips, heads, core_ref, bias_ref, qm_ref, qs_ref, dm_ref, ds_ref, *refs):
    del core_ref
    kv_refs = refs[:chips]
    dqm_ref, dqs_ref = refs[chips], refs[chips + 1]
    part_refs = refs[chips + 2 :]
    tokens = qm_ref.shape[0]
    d = HEAD_DIM
    contract_last = (((1,), (1,)), ((), ()))
    contract_first = (((0,), (0,)), ((), ()))
    rows = lambda j: slice(j * tokens, (j + 1) * tokens)
    for h in range(heads):
        cols = slice(h * d, (h + 1) * d)
        first = slice(2 * h * d, (2 * h + 1) * d)
        second = slice((2 * h + 1) * d, (2 * h + 2) * d)
        k = jnp.concatenate([r[0, s, :, cols] for r in kv_refs for s in range(2)], axis=0)
        v = jnp.concatenate([r[1, s, :, cols] for r in kv_refs for s in range(2)], axis=0)
        qs = jnp.concatenate(
            [qm_ref[:, first], qs_ref[:, first], qm_ref[:, second], qs_ref[:, second]], axis=0
        )
        dos = jnp.concatenate(
            [dm_ref[:, first], ds_ref[:, first], dm_ref[:, second], ds_ref[:, second]], axis=0
        )
        scores = lax.dot_general(qs, k, contract_last, preferred_element_type=jnp.float32)
        scores = scores * SCORE_SCALE + bias_ref[...]
        largest = jnp.max(scores, axis=1, keepdims=True)
        unscaled = jnp.exp(scores - largest)
        attn = unscaled * (1.0 / jnp.sum(unscaled, axis=1, keepdims=True))
        dattn = lax.dot_general(dos, v, contract_last, preferred_element_type=jnp.float32)
        row_delta = jnp.sum(attn * dattn, axis=1, keepdims=True)
        dscores = (attn * (dattn - row_delta)).astype(jnp.bfloat16)
        grad_q = jnp.dot(dscores, k, preferred_element_type=jnp.float32) * SCORE_SCALE
        dqm_ref[:, first] = grad_q[rows(0)].astype(dqm_ref.dtype)
        dqs_ref[:, first] = grad_q[rows(1)].astype(dqs_ref.dtype)
        dqm_ref[:, second] = grad_q[rows(2)].astype(dqm_ref.dtype)
        dqs_ref[:, second] = grad_q[rows(3)].astype(dqs_ref.dtype)
        grad_k = (
            lax.dot_general(dscores, qs, contract_first, preferred_element_type=jnp.float32)
            * SCORE_SCALE
        )
        grad_v = lax.dot_general(
            attn.astype(jnp.bfloat16), dos, contract_first, preferred_element_type=jnp.float32
        )
        for j, out in enumerate(part_refs):
            for s in range(2):
                out[0, s, :, cols] = grad_k[rows(2 * j + s)].astype(out.dtype)
                out[1, s, :, cols] = grad_v[rows(2 * j + s)].astype(out.dtype)


def attention_grads(core, bias, queries, query_sib, grad_out, grad_sib, payloads, per_step=2):
    tokens = queries.shape[0]
    chips = len(payloads)
    key_count = bias.shape[1]
    half = payloads[0].shape[3]
    heads = half // HEAD_DIM
    pair = 2 * HEAD_DIM * per_step
    steps = heads // per_step
    mine = pl.BlockSpec((tokens, pair), lambda g, c: (0, c[0] * steps + g))
    other = pl.BlockSpec((tokens, pair), lambda g, c: (0, g))
    chip = pl.BlockSpec((2, 2, tokens, HEAD_DIM * per_step), lambda g, c: (0, 0, 0, g))
    part = jax.ShapeDtypeStruct(payloads[0].shape, jnp.float32)
    rows = 4 * tokens
    flops = 2 * 5 * rows * key_count * HEAD_DIM * heads
    moved_bytes = 2 * 6 * tokens * half * 2 + 2 * 2 * key_count * half * 3 + bias.size * 4
    grid_spec = pltpu.PrefetchScalarGridSpec(
        num_scalar_prefetch=1,
        grid=(steps,),
        in_specs=[pl.BlockSpec(bias.shape, lambda g, c: (0, 0)), mine, other, mine, other]
        + [chip] * chips,
        out_specs=[other, other] + [chip] * chips,
    )
    return pl.pallas_call(
        lambda *refs: attention_kernel(chips, per_step, *refs),
        grid_spec=grid_spec,
        out_shape=[jax.ShapeDtypeStruct(query_sib.shape, jnp.bfloat16)] * 2
        + [part]
        + [jax.ShapeDtypeStruct(part.shape, jnp.bfloat16)] * (chips - 2)
        + [part],
        cost_estimate=pl.CostEstimate(
            flops=flops, transcendentals=rows * key_count * heads, bytes_accessed=moved_bytes
        ),
    )(core, bias, queries, query_sib, grad_out, grad_sib, *payloads)


def in_core_order(core, mine, theirs):
    return jnp.where(core == 0, jnp.concatenate([mine, theirs], -1), jnp.concatenate([theirs, mine], -1))


def local(queries, key_rows, value_rows, arriving_grad, doc_blocks):
    tokens = queries.shape[1]
    count = lax.axis_size("seq")
    if lax.axis_size("pipe") > 1:
        arriving_grad = passed_along(arriving_grad, "pipe", -1)
    grad_out = arriving_grad[0]
    position = lax.axis_index("seq")
    reach_back = (WINDOW - 1) // tokens + 1
    assert reach_back % 2 == 0 and count % reach_back == 0 and WINDOW % tokens == 0
    routes = Routes(count, reach_back)
    chips = routes.chips
    chip_in_group = (position % reach_back) // 2
    core = position % 2
    other = 1 - core
    key_width = key_rows.shape[2] // 2
    query_width = queries.shape[2] // 2
    keys, values = key_rows[0], value_rows[0]
    kv_sent = jnp.stack(
        [lax.dynamic_slice_in_dim(keys, other * key_width, key_width, 1),
         lax.dynamic_slice_in_dim(values, other * key_width, key_width, 1)]
    )
    kv_sib = moved(kv_sent, routes.sibling)
    kv_mine = jnp.stack(
        [lax.dynamic_slice_in_dim(keys, core * key_width, key_width, 1),
         lax.dynamic_slice_in_dim(values, core * key_width, key_width, 1)]
    )
    own = jnp.stack([kv_mine, kv_sib], axis=1)
    payloads = gather_window(own, routes, chip_in_group)
    (query_rows, grad_rows, doc_row), _ = lax.optimization_barrier(
        ((queries[0], grad_out, doc_blocks[0]), payloads[0])
    )
    qd_sent = jnp.stack(
        [lax.dynamic_slice_in_dim(query_rows, other * query_width, query_width, 1),
         lax.dynamic_slice_in_dim(grad_rows, other * query_width, query_width, 1)]
    )
    qd_sib = moved(qd_sent, routes.sibling)

    chip = position // 2
    block_of = lambda m, s: 2 * m + jnp.where(s == 0, core, other)
    key_blocks = [block_of(chip - chips + j, s) for j in range(chips + 1) for s in range(2)]
    token_doc = jnp.repeat(doc_row, MBLK)
    pad = (reach_back + 2) * tokens
    doc_pad = jnp.concatenate([jnp.full((pad,), -1, jnp.int32), token_doc])
    key_doc = jnp.concatenate(
        [lax.dynamic_slice_in_dim(doc_pad, b * tokens + pad, tokens, 0) for b in key_blocks]
    )
    offsets = jnp.arange(tokens, dtype=jnp.int32)
    key_pos = jnp.concatenate([b * tokens + offsets for b in key_blocks])
    masks = []
    for block in (position, position ^ 1):
        query_pos = block * tokens + offsets
        query_doc = lax.dynamic_slice_in_dim(token_doc, block * tokens, tokens, 0)
        distance = query_pos[:, None] - key_pos[None, :]
        allowed = (distance >= 0) & (distance < WINDOW) & (query_doc[:, None] == key_doc[None, :])
        masks.append(jnp.where(allowed, 0.0, MASKED_SCORE).astype(jnp.float32))
    bias = jnp.concatenate(masks + masks, axis=0)

    outs = attention_grads(
        core[None].astype(jnp.int32), bias, queries[0], qd_sib[0], grad_out, qd_sib[1], payloads
    )
    dq_mine, dq_sib, parts = outs[0], outs[1], outs[2:]
    summed = scatter_window(parts, routes, chip_in_group)
    sent = jnp.concatenate(
        [summed[0, 1].astype(jnp.bfloat16), summed[1, 1].astype(jnp.bfloat16), dq_sib], axis=-1
    )
    got = moved(sent, routes.sibling)
    grad_key = in_core_order(core, summed[0, 0].astype(jnp.bfloat16), got[:, :key_width])
    grad_value = in_core_order(
        core, summed[1, 0].astype(jnp.bfloat16), got[:, key_width : 2 * key_width]
    )
    grad_query = in_core_order(core, dq_mine, got[:, 2 * key_width :])
    return (grad_query[None], grad_key[None], grad_value[None])


def solution(mesh):
    placed = (
        P("pipe", "seq", None),
        P("pipe", "seq", None),
        P("pipe", "seq", None),
        P("pipe", "seq", None),
        P("pipe", None),
    )
    return jax.shard_map(
        local,
        mesh=mesh,
        in_specs=placed,
        out_specs=(P("pipe", "seq", None), P("pipe", "seq", None), P("pipe", "seq", None)),
        check_vma=False,
    )
```

```python
import jax
import jax.numpy as jnp
from jax import lax
from jax.experimental import pallas as pl
from jax.experimental.pallas import tpu as pltpu
from jax.sharding import PartitionSpec as P

HEADS = 32
KV_HEADS = 16
HEAD_DIM = 128
WINDOW = 1024
MBLK = 128


SCORE_SCALE = 168.0 ** (-0.5)
MASKED_SCORE = -1e30


def passed_along(value, axis, steps):
    count = lax.axis_size(axis)
    pairs = [(source, (source + steps) % count) for source in range(count)]
    return lax.ppermute(value, axis, pairs)


def moved(value, pairs):
    return lax.ppermute(value, "seq", pairs)


def reverse(pairs):
    return [(t, s) for (s, t) in pairs]


class Routes:
    def __init__(self, count, reach):
        self.reach = reach
        self.chips = reach // 2
        group_chip = lambda i: (i % reach) // 2
        self.hop = [(i, i + reach) for i in range(count - reach)]
        self.up = []
        self.down = []
        for e in range(1, self.chips):
            self.up.append([(i, i + 2 * e) for i in range(count) if group_chip(i) + e < self.chips])
            self.down.append(
                [(i, i + 2 * e - reach) for i in range(count) if group_chip(i) + e >= self.chips]
            )
        self.sibling = [(i, i ^ 1) for i in range(count)]


def gather_window(own, routes, chip_in_group):
    prev = moved(own, routes.hop)
    recv = []
    for e in range(1, routes.chips):
        sent = jnp.where(chip_in_group + e < routes.chips, own, prev)
        recv.append(moved(sent, routes.up[e - 1] + routes.down[e - 1]))
    return [prev] + recv[::-1] + [own]


def scatter_window(parts, routes, chip_in_group):
    link = jnp.bfloat16
    chips = routes.chips
    prev, own = parts[0], parts[-1]
    recv = parts[1:-1][::-1]
    for e in range(1, chips):
        pairs = reverse(routes.up[e - 1] + routes.down[e - 1])
        got = moved(recv[e - 1].astype(link), pairs).astype(jnp.float32)
        upward = chip_in_group + e < chips
        own = own + jnp.where(upward, got, 0.0)
        prev = prev + jnp.where(upward, 0.0, got)
    return own + moved(prev.astype(link), reverse(routes.hop)).astype(jnp.float32)


def attention_kernel(chips, core_ref, bias_ref, qm_ref, qs_ref, dm_ref, ds_ref, *refs):
    del core_ref
    kv_refs = refs[:chips]
    dqm_ref, dqs_ref = refs[chips], refs[chips + 1]
    part_refs = refs[chips + 2 :]
    tokens = qm_ref.shape[0]
    d = HEAD_DIM
    k = jnp.concatenate([r[0, s] for r in kv_refs for s in range(2)], axis=0)
    v = jnp.concatenate([r[1, s] for r in kv_refs for s in range(2)], axis=0)
    qs = jnp.concatenate([qm_ref[:, :d], qs_ref[:, :d], qm_ref[:, d:], qs_ref[:, d:]], axis=0)
    dos = jnp.concatenate([dm_ref[:, :d], ds_ref[:, :d], dm_ref[:, d:], ds_ref[:, d:]], axis=0)
    contract_last = (((1,), (1,)), ((), ()))
    contract_first = (((0,), (0,)), ((), ()))
    scores = lax.dot_general(qs, k, contract_last, preferred_element_type=jnp.float32)
    scores = scores * SCORE_SCALE + bias_ref[...]
    largest = jnp.max(scores, axis=1, keepdims=True)
    unscaled = jnp.exp(scores - largest)
    attn = unscaled * (1.0 / jnp.sum(unscaled, axis=1, keepdims=True))
    dattn = lax.dot_general(dos, v, contract_last, preferred_element_type=jnp.float32)
    row_delta = jnp.sum(attn * dattn, axis=1, keepdims=True)
    dscores = (attn * (dattn - row_delta)).astype(jnp.bfloat16)
    grad_q = jnp.dot(dscores, k, preferred_element_type=jnp.float32) * SCORE_SCALE
    rows = lambda j: slice(j * tokens, (j + 1) * tokens)
    dqm_ref[:, :d] = grad_q[rows(0)].astype(dqm_ref.dtype)
    dqs_ref[:, :d] = grad_q[rows(1)].astype(dqs_ref.dtype)
    dqm_ref[:, d:] = grad_q[rows(2)].astype(dqm_ref.dtype)
    dqs_ref[:, d:] = grad_q[rows(3)].astype(dqs_ref.dtype)
    grad_k = (
        lax.dot_general(dscores, qs, contract_first, preferred_element_type=jnp.float32)
        * SCORE_SCALE
    )
    grad_v = lax.dot_general(
        attn.astype(jnp.bfloat16), dos, contract_first, preferred_element_type=jnp.float32
    )
    for j, out in enumerate(part_refs):
        for s in range(2):
            out[0, s] = grad_k[rows(2 * j + s)].astype(out.dtype)
            out[1, s] = grad_v[rows(2 * j + s)].astype(out.dtype)


def attention_grads(core, bias, queries, query_sib, grad_out, grad_sib, payloads):
    tokens = queries.shape[0]
    chips = len(payloads)
    key_count = bias.shape[1]
    half = payloads[0].shape[3]
    heads = half // HEAD_DIM
    pair = 2 * HEAD_DIM
    mine = pl.BlockSpec((tokens, pair), lambda g, c: (0, c[0] * heads + g))
    other = pl.BlockSpec((tokens, pair), lambda g, c: (0, g))
    chip = pl.BlockSpec((2, 2, tokens, HEAD_DIM), lambda g, c: (0, 0, 0, g))
    part = jax.ShapeDtypeStruct(payloads[0].shape, jnp.float32)
    rows = 4 * tokens
    flops = 2 * 5 * rows * key_count * HEAD_DIM * heads
    moved_bytes = 2 * 6 * tokens * half * 2 + 2 * 2 * key_count * half * 3 + bias.size * 4
    grid_spec = pltpu.PrefetchScalarGridSpec(
        num_scalar_prefetch=1,
        grid=(heads,),
        in_specs=[pl.BlockSpec(bias.shape, lambda g, c: (0, 0)), mine, other, mine, other]
        + [chip] * chips,
        out_specs=[other, other] + [chip] * chips,
    )
    return pl.pallas_call(
        lambda *refs: attention_kernel(chips, *refs),
        grid_spec=grid_spec,
        out_shape=[jax.ShapeDtypeStruct(query_sib.shape, jnp.bfloat16)] * 2
        + [part]
        + [jax.ShapeDtypeStruct(part.shape, jnp.bfloat16)] * (chips - 2)
        + [part],
        cost_estimate=pl.CostEstimate(
            flops=flops, transcendentals=rows * key_count * heads, bytes_accessed=moved_bytes
        ),
    )(core, bias, queries, query_sib, grad_out, grad_sib, *payloads)


def in_core_order(core, mine, theirs):
    return jnp.where(core == 0, jnp.concatenate([mine, theirs], -1), jnp.concatenate([theirs, mine], -1))


def local(queries, key_rows, value_rows, arriving_grad, doc_blocks):
    tokens = queries.shape[1]
    count = lax.axis_size("seq")
    if lax.axis_size("pipe") > 1:
        arriving_grad = passed_along(arriving_grad, "pipe", -1)
    grad_out = arriving_grad[0]
    position = lax.axis_index("seq")
    reach_back = (WINDOW - 1) // tokens + 1
    assert reach_back % 2 == 0 and count % reach_back == 0 and WINDOW % tokens == 0
    routes = Routes(count, reach_back)
    chips = routes.chips
    chip_in_group = (position % reach_back) // 2
    core = position % 2
    other = 1 - core
    key_width = key_rows.shape[2] // 2
    query_width = queries.shape[2] // 2
    keys, values = key_rows[0], value_rows[0]
    kv_sent = jnp.stack(
        [lax.dynamic_slice_in_dim(keys, other * key_width, key_width, 1),
         lax.dynamic_slice_in_dim(values, other * key_width, key_width, 1)]
    )
    kv_sib = moved(kv_sent, routes.sibling)
    kv_mine = jnp.stack(
        [lax.dynamic_slice_in_dim(keys, core * key_width, key_width, 1),
         lax.dynamic_slice_in_dim(values, core * key_width, key_width, 1)]
    )
    own = jnp.stack([kv_mine, kv_sib], axis=1)
    payloads = gather_window(own, routes, chip_in_group)
    (query_rows, grad_rows, doc_row), _ = lax.optimization_barrier(
        ((queries[0], grad_out, doc_blocks[0]), payloads[0])
    )
    qd_sent = jnp.stack(
        [lax.dynamic_slice_in_dim(query_rows, other * query_width, query_width, 1),
         lax.dynamic_slice_in_dim(grad_rows, other * query_width, query_width, 1)]
    )
    qd_sib = moved(qd_sent, routes.sibling)

    chip = position // 2
    block_of = lambda m, s: 2 * m + jnp.where(s == 0, core, other)
    key_blocks = [block_of(chip - chips + j, s) for j in range(chips + 1) for s in range(2)]
    token_doc = jnp.repeat(doc_row, MBLK)
    pad = (reach_back + 2) * tokens
    doc_pad = jnp.concatenate([jnp.full((pad,), -1, jnp.int32), token_doc])
    key_doc = jnp.concatenate(
        [lax.dynamic_slice_in_dim(doc_pad, b * tokens + pad, tokens, 0) for b in key_blocks]
    )
    offsets = jnp.arange(tokens, dtype=jnp.int32)
    key_pos = jnp.concatenate([b * tokens + offsets for b in key_blocks])
    masks = []
    for block in (position, position ^ 1):
        query_pos = block * tokens + offsets
        query_doc = lax.dynamic_slice_in_dim(token_doc, block * tokens, tokens, 0)
        distance = query_pos[:, None] - key_pos[None, :]
        allowed = (distance >= 0) & (distance < WINDOW) & (query_doc[:, None] == key_doc[None, :])
        masks.append(jnp.where(allowed, 0.0, MASKED_SCORE).astype(jnp.float32))
    bias = jnp.concatenate(masks + masks, axis=0)

    outs = attention_grads(
        core[None].astype(jnp.int32), bias, queries[0], qd_sib[0], grad_out, qd_sib[1], payloads
    )
    dq_mine, dq_sib, parts = outs[0], outs[1], outs[2:]
    grad_query = in_core_order(core, dq_mine, moved(dq_sib, routes.sibling))
    summed = scatter_window(parts, routes, chip_in_group)
    got = moved(summed[:, 1].astype(jnp.bfloat16), routes.sibling)
    grad_key = in_core_order(core, summed[0, 0].astype(jnp.bfloat16), got[0])
    grad_value = in_core_order(core, summed[1, 0].astype(jnp.bfloat16), got[1])
    return (grad_query[None], grad_key[None], grad_value[None])


def solution(mesh):
    placed = (
        P("pipe", "seq", None),
        P("pipe", "seq", None),
        P("pipe", "seq", None),
        P("pipe", "seq", None),
        P("pipe", None),
    )
    return jax.shard_map(
        local,
        mesh=mesh,
        in_specs=placed,
        out_specs=(P("pipe", "seq", None), P("pipe", "seq", None), P("pipe", "seq", None)),
        check_vma=False,
    )
```

```python
import jax
import jax.numpy as jnp
from jax import lax
from jax.experimental import pallas as pl
from jax.experimental.pallas import tpu as pltpu
from jax.sharding import PartitionSpec as P

HEADS = 32
KV_HEADS = 16
HEAD_DIM = 128
WINDOW = 1024
MBLK = 128


SCORE_SCALE = 168.0 ** (-0.5)
MASKED_SCORE = -1e30


def passed_along(value, axis, steps):
    count = lax.axis_size(axis)
    pairs = [(source, (source + steps) % count) for source in range(count)]
    return lax.ppermute(value, axis, pairs)


def moved(value, pairs):
    return lax.ppermute(value, "seq", pairs)


def reverse(pairs):
    return [(t, s) for (s, t) in pairs]


class Routes:
    def __init__(self, count, reach):
        self.reach = reach
        self.chips = reach // 2
        group_chip = lambda i: (i % reach) // 2
        self.hop = [(i, i + reach) for i in range(count - reach)]
        self.hop_cross = [(i, (i + reach) ^ 1) for i in range(count - reach)]
        self.up = []
        self.down = []
        for e in range(1, self.chips):
            self.up.append([(i, i + 2 * e) for i in range(count) if group_chip(i) + e < self.chips])
            self.down.append(
                [(i, i + 2 * e - reach) for i in range(count) if group_chip(i) + e >= self.chips]
            )
        self.sibling = [(i, i ^ 1) for i in range(count)]


def gather_window(own, routes, chip_in_group):
    prev = moved(own, routes.hop)
    recv = []
    for e in range(1, routes.chips):
        sent = jnp.where(chip_in_group + e < routes.chips, own, prev)
        recv.append(moved(sent, routes.up[e - 1] + routes.down[e - 1]))
    return [prev] + recv[::-1] + [own]


def scatter_window(parts, routes, chip_in_group):
    link = jnp.bfloat16
    chips = routes.chips
    prev, own = parts[0], parts[-1]
    recv = parts[1:-1][::-1]
    for e in range(1, chips):
        pairs = reverse(routes.up[e - 1] + routes.down[e - 1])
        got = moved(recv[e - 1].astype(link), pairs).astype(jnp.float32)
        upward = chip_in_group + e < chips
        own = own + jnp.where(upward, got, 0.0)
        prev = prev + jnp.where(upward, 0.0, got)
    return own, prev


def attention_kernel(chips, core_ref, bias_ref, qm_ref, qs_ref, dm_ref, ds_ref, *refs):
    del core_ref
    kv_refs = refs[:chips]
    dqm_ref, dqs_ref = refs[chips], refs[chips + 1]
    part_refs = refs[chips + 2 :]
    tokens = qm_ref.shape[0]
    d = HEAD_DIM
    k = jnp.concatenate([r[0, s] for r in kv_refs for s in range(2)], axis=0)
    v = jnp.concatenate([r[1, s] for r in kv_refs for s in range(2)], axis=0)
    qs = jnp.concatenate([qm_ref[:, :d], qs_ref[:, :d], qm_ref[:, d:], qs_ref[:, d:]], axis=0)
    dos = jnp.concatenate([dm_ref[:, :d], ds_ref[:, :d], dm_ref[:, d:], ds_ref[:, d:]], axis=0)
    contract_last = (((1,), (1,)), ((), ()))
    contract_first = (((0,), (0,)), ((), ()))
    scores = lax.dot_general(qs, k, contract_last, preferred_element_type=jnp.float32)
    scores = scores * SCORE_SCALE + bias_ref[...]
    largest = jnp.max(scores, axis=1, keepdims=True)
    unscaled = jnp.exp(scores - largest)
    attn = unscaled * (1.0 / jnp.sum(unscaled, axis=1, keepdims=True))
    dattn = lax.dot_general(dos, v, contract_last, preferred_element_type=jnp.float32)
    row_delta = jnp.sum(attn * dattn, axis=1, keepdims=True)
    dscores = (attn * (dattn - row_delta)).astype(jnp.bfloat16)
    grad_q = jnp.dot(dscores, k, preferred_element_type=jnp.float32) * SCORE_SCALE
    rows = lambda j: slice(j * tokens, (j + 1) * tokens)
    dqm_ref[:, :d] = grad_q[rows(0)].astype(dqm_ref.dtype)
    dqs_ref[:, :d] = grad_q[rows(1)].astype(dqs_ref.dtype)
    dqm_ref[:, d:] = grad_q[rows(2)].astype(dqm_ref.dtype)
    dqs_ref[:, d:] = grad_q[rows(3)].astype(dqs_ref.dtype)
    grad_k = (
        lax.dot_general(dscores, qs, contract_first, preferred_element_type=jnp.float32)
        * SCORE_SCALE
    )
    grad_v = lax.dot_general(
        attn.astype(jnp.bfloat16), dos, contract_first, preferred_element_type=jnp.float32
    )
    for j, out in enumerate(part_refs):
        for s in range(2):
            out[0, s] = grad_k[rows(2 * j + s)].astype(out.dtype)
            out[1, s] = grad_v[rows(2 * j + s)].astype(out.dtype)


def attention_grads(core, bias, queries, query_sib, grad_out, grad_sib, payloads):
    tokens = queries.shape[0]
    chips = len(payloads)
    key_count = bias.shape[1]
    half = payloads[0].shape[3]
    heads = half // HEAD_DIM
    pair = 2 * HEAD_DIM
    mine = pl.BlockSpec((tokens, pair), lambda g, c: (0, c[0] * heads + g))
    other = pl.BlockSpec((tokens, pair), lambda g, c: (0, g))
    chip = pl.BlockSpec((2, 2, tokens, HEAD_DIM), lambda g, c: (0, 0, 0, g))
    part = jax.ShapeDtypeStruct(payloads[0].shape, jnp.float32)
    rows = 4 * tokens
    flops = 2 * 5 * rows * key_count * HEAD_DIM * heads
    moved_bytes = 2 * 6 * tokens * half * 2 + 2 * 2 * key_count * half * 3 + bias.size * 4
    grid_spec = pltpu.PrefetchScalarGridSpec(
        num_scalar_prefetch=1,
        grid=(heads,),
        in_specs=[pl.BlockSpec(bias.shape, lambda g, c: (0, 0)), mine, other, mine, other]
        + [chip] * chips,
        out_specs=[other, other] + [chip] * chips,
    )
    return pl.pallas_call(
        lambda *refs: attention_kernel(chips, *refs),
        grid_spec=grid_spec,
        out_shape=[jax.ShapeDtypeStruct(query_sib.shape, jnp.bfloat16)] * 2
        + [part]
        + [jax.ShapeDtypeStruct(part.shape, jnp.bfloat16)] * (chips - 2)
        + [part],
        cost_estimate=pl.CostEstimate(
            flops=flops, transcendentals=rows * key_count * heads, bytes_accessed=moved_bytes
        ),
    )(core, bias, queries, query_sib, grad_out, grad_sib, *payloads)


def in_core_order(core, mine, theirs):
    return jnp.where(core == 0, jnp.concatenate([mine, theirs], -1), jnp.concatenate([theirs, mine], -1))


def local(queries, key_rows, value_rows, arriving_grad, doc_blocks):
    tokens = queries.shape[1]
    count = lax.axis_size("seq")
    if lax.axis_size("pipe") > 1:
        arriving_grad = passed_along(arriving_grad, "pipe", -1)
    grad_out = arriving_grad[0]
    position = lax.axis_index("seq")
    reach_back = (WINDOW - 1) // tokens + 1
    assert reach_back % 2 == 0 and count % reach_back == 0 and WINDOW % tokens == 0
    routes = Routes(count, reach_back)
    chips = routes.chips
    chip_in_group = (position % reach_back) // 2
    core = position % 2
    other = 1 - core
    key_width = key_rows.shape[2] // 2
    query_width = queries.shape[2] // 2
    keys, values = key_rows[0], value_rows[0]
    kv_sent = jnp.stack(
        [lax.dynamic_slice_in_dim(keys, other * key_width, key_width, 1),
         lax.dynamic_slice_in_dim(values, other * key_width, key_width, 1)]
    )
    kv_sib = moved(kv_sent, routes.sibling)
    kv_mine = jnp.stack(
        [lax.dynamic_slice_in_dim(keys, core * key_width, key_width, 1),
         lax.dynamic_slice_in_dim(values, core * key_width, key_width, 1)]
    )
    own = jnp.stack([kv_mine, kv_sib], axis=1)
    payloads = gather_window(own, routes, chip_in_group)
    (query_rows, grad_rows, doc_row), _ = lax.optimization_barrier(
        ((queries[0], grad_out, doc_blocks[0]), payloads[0])
    )
    qd_sent = jnp.stack(
        [lax.dynamic_slice_in_dim(query_rows, other * query_width, query_width, 1),
         lax.dynamic_slice_in_dim(grad_rows, other * query_width, query_width, 1)]
    )
    qd_sib = moved(qd_sent, routes.sibling)

    chip = position // 2
    block_of = lambda m, s: 2 * m + jnp.where(s == 0, core, other)
    key_blocks = [block_of(chip - chips + j, s) for j in range(chips + 1) for s in range(2)]
    token_doc = jnp.repeat(doc_row, MBLK)
    pad = (reach_back + 2) * tokens
    doc_pad = jnp.concatenate([jnp.full((pad,), -1, jnp.int32), token_doc])
    key_doc = jnp.concatenate(
        [lax.dynamic_slice_in_dim(doc_pad, b * tokens + pad, tokens, 0) for b in key_blocks]
    )
    offsets = jnp.arange(tokens, dtype=jnp.int32)
    key_pos = jnp.concatenate([b * tokens + offsets for b in key_blocks])
    masks = []
    for block in (position, position ^ 1):
        query_pos = block * tokens + offsets
        query_doc = lax.dynamic_slice_in_dim(token_doc, block * tokens, tokens, 0)
        distance = query_pos[:, None] - key_pos[None, :]
        allowed = (distance >= 0) & (distance < WINDOW) & (query_doc[:, None] == key_doc[None, :])
        masks.append(jnp.where(allowed, 0.0, MASKED_SCORE).astype(jnp.float32))
    bias = jnp.concatenate(masks + masks, axis=0)

    outs = attention_grads(
        core[None].astype(jnp.int32), bias, queries[0], qd_sib[0], grad_out, qd_sib[1], payloads
    )
    dq_mine, dq_sib, parts = outs[0], outs[1], outs[2:]
    summed, prev = scatter_window(parts, routes, chip_in_group)
    link = jnp.bfloat16
    sent = jnp.concatenate(
        [summed[0, 1].astype(link), summed[1, 1].astype(link), dq_sib], axis=-1
    )
    got = moved(sent, routes.sibling)
    back_same = moved(prev[:, 0].astype(link), reverse(routes.hop)).astype(jnp.float32)
    back_cross = moved(prev[:, 1].astype(link), reverse(routes.hop_cross)).astype(jnp.float32)
    mine = summed[:, 0] + back_same
    theirs = jnp.stack([got[:, :key_width], got[:, key_width : 2 * key_width]])
    theirs = theirs.astype(jnp.float32) + back_cross
    grad_key = in_core_order(core, mine[0].astype(link), theirs[0].astype(link))
    grad_value = in_core_order(core, mine[1].astype(link), theirs[1].astype(link))
    grad_query = in_core_order(core, dq_mine, got[:, 2 * key_width :])
    return (grad_query[None], grad_key[None], grad_value[None])


def solution(mesh):
    placed = (
        P("pipe", "seq", None),
        P("pipe", "seq", None),
        P("pipe", "seq", None),
        P("pipe", "seq", None),
        P("pipe", None),
    )
    return jax.shard_map(
        local,
        mesh=mesh,
        in_specs=placed,
        out_specs=(P("pipe", "seq", None), P("pipe", "seq", None), P("pipe", "seq", None)),
        check_vma=False,
    )
```

```python
import jax
import jax.numpy as jnp
from jax import lax
from jax.experimental import pallas as pl
from jax.experimental.pallas import tpu as pltpu
from jax.sharding import PartitionSpec as P

HEADS = 32
KV_HEADS = 16
HEAD_DIM = 128
WINDOW = 1024
MBLK = 128


SCORE_SCALE = 168.0 ** (-0.5)
MASKED_SCORE = -1e30


def passed_along(value, axis, steps):
    count = lax.axis_size(axis)
    pairs = [(source, (source + steps) % count) for source in range(count)]
    return lax.ppermute(value, axis, pairs)


def moved(value, pairs):
    return lax.ppermute(value, "seq", pairs)


def reverse(pairs):
    return [(t, s) for (s, t) in pairs]


class Routes:
    def __init__(self, count, reach):
        self.reach = reach
        self.chips = reach // 2
        group_chip = lambda i: (i % reach) // 2
        self.hop = [(i, i + reach) for i in range(count - reach)]
        self.up = []
        self.down = []
        for e in range(1, self.chips):
            self.up.append([(i, i + 2 * e) for i in range(count) if group_chip(i) + e < self.chips])
            self.down.append(
                [(i, i + 2 * e - reach) for i in range(count) if group_chip(i) + e >= self.chips]
            )
        self.sibling = [(i, i ^ 1) for i in range(count)]


def gather_window(own, routes, chip_in_group):
    prev = moved(own, routes.hop)
    recv = []
    for e in range(1, routes.chips):
        sent = jnp.where(chip_in_group + e < routes.chips, own, prev)
        recv.append(moved(sent, routes.up[e - 1] + routes.down[e - 1]))
    return [prev] + recv[::-1] + [own]


def scatter_window(parts, routes, chip_in_group):
    link = jnp.bfloat16
    chips = routes.chips
    prev, own = parts[0], parts[-1]
    recv = parts[1:-1][::-1]
    for e in range(1, chips):
        pairs = reverse(routes.up[e - 1] + routes.down[e - 1])
        got = moved(recv[e - 1].astype(link), pairs).astype(jnp.float32)
        upward = chip_in_group + e < chips
        own = own + jnp.where(upward, got, 0.0)
        prev = prev + jnp.where(upward, 0.0, got)
    return own + moved(prev.astype(link), reverse(routes.hop)).astype(jnp.float32)


def attention_kernel(chips, core_ref, bias_ref, qm_ref, qs_ref, dm_ref, ds_ref, *refs):
    del core_ref
    kv_refs = refs[:chips]
    dqm_ref, dqs_ref = refs[chips], refs[chips + 1]
    part_refs = refs[chips + 2 :]
    tokens = qm_ref.shape[0]
    d = HEAD_DIM
    k = jnp.concatenate([r[0, s] for r in kv_refs for s in range(2)], axis=0)
    v = jnp.concatenate([r[1, s] for r in kv_refs for s in range(2)], axis=0)
    qs = jnp.concatenate([qm_ref[:, :d], qs_ref[:, :d], qm_ref[:, d:], qs_ref[:, d:]], axis=0)
    dos = jnp.concatenate([dm_ref[:, :d], ds_ref[:, :d], dm_ref[:, d:], ds_ref[:, d:]], axis=0)
    contract_last = (((1,), (1,)), ((), ()))
    contract_first = (((0,), (0,)), ((), ()))
    scores = lax.dot_general(qs, k, contract_last, preferred_element_type=jnp.float32)
    scores = scores * SCORE_SCALE + bias_ref[...]
    largest = jnp.max(scores, axis=1, keepdims=True)
    unscaled = jnp.exp(scores - largest)
    attn = unscaled * (1.0 / jnp.sum(unscaled, axis=1, keepdims=True))
    dattn = lax.dot_general(dos, v, contract_last, preferred_element_type=jnp.float32)
    attn_low = attn.astype(jnp.bfloat16)
    mixed = jnp.dot(attn_low, v, preferred_element_type=jnp.float32)
    row_delta = jnp.sum(dos.astype(jnp.float32) * mixed, axis=1, keepdims=True)
    dscores = (attn * (dattn - row_delta)).astype(jnp.bfloat16)
    grad_q = jnp.dot(dscores, k, preferred_element_type=jnp.float32) * SCORE_SCALE
    rows = lambda j: slice(j * tokens, (j + 1) * tokens)
    dqm_ref[:, :d] = grad_q[rows(0)].astype(dqm_ref.dtype)
    dqs_ref[:, :d] = grad_q[rows(1)].astype(dqs_ref.dtype)
    dqm_ref[:, d:] = grad_q[rows(2)].astype(dqm_ref.dtype)
    dqs_ref[:, d:] = grad_q[rows(3)].astype(dqs_ref.dtype)
    grad_k = (
        lax.dot_general(dscores, qs, contract_first, preferred_element_type=jnp.float32)
        * SCORE_SCALE
    )
    grad_v = lax.dot_general(attn_low, dos, contract_first, preferred_element_type=jnp.float32)
    for j, out in enumerate(part_refs):
        for s in range(2):
            out[0, s] = grad_k[rows(2 * j + s)].astype(out.dtype)
            out[1, s] = grad_v[rows(2 * j + s)].astype(out.dtype)


def attention_grads(core, bias, queries, query_sib, grad_out, grad_sib, payloads):
    tokens = queries.shape[0]
    chips = len(payloads)
    key_count = bias.shape[1]
    half = payloads[0].shape[3]
    heads = half // HEAD_DIM
    pair = 2 * HEAD_DIM
    mine = pl.BlockSpec((tokens, pair), lambda g, c: (0, c[0] * heads + g))
    other = pl.BlockSpec((tokens, pair), lambda g, c: (0, g))
    chip = pl.BlockSpec((2, 2, tokens, HEAD_DIM), lambda g, c: (0, 0, 0, g))
    part = jax.ShapeDtypeStruct(payloads[0].shape, jnp.float32)
    rows = 4 * tokens
    flops = 2 * 5 * rows * key_count * HEAD_DIM * heads
    moved_bytes = 2 * 6 * tokens * half * 2 + 2 * 2 * key_count * half * 3 + bias.size * 4
    grid_spec = pltpu.PrefetchScalarGridSpec(
        num_scalar_prefetch=1,
        grid=(heads,),
        in_specs=[pl.BlockSpec(bias.shape, lambda g, c: (0, 0)), mine, other, mine, other]
        + [chip] * chips,
        out_specs=[other, other] + [chip] * chips,
    )
    return pl.pallas_call(
        lambda *refs: attention_kernel(chips, *refs),
        grid_spec=grid_spec,
        out_shape=[jax.ShapeDtypeStruct(query_sib.shape, jnp.bfloat16)] * 2
        + [part]
        + [jax.ShapeDtypeStruct(part.shape, jnp.bfloat16)] * (chips - 2)
        + [part],
        cost_estimate=pl.CostEstimate(
            flops=flops, transcendentals=rows * key_count * heads, bytes_accessed=moved_bytes
        ),
    )(core, bias, queries, query_sib, grad_out, grad_sib, *payloads)


def in_core_order(core, mine, theirs):
    return jnp.where(core == 0, jnp.concatenate([mine, theirs], -1), jnp.concatenate([theirs, mine], -1))


def local(queries, key_rows, value_rows, arriving_grad, doc_blocks):
    tokens = queries.shape[1]
    count = lax.axis_size("seq")
    if lax.axis_size("pipe") > 1:
        arriving_grad = passed_along(arriving_grad, "pipe", -1)
    grad_out = arriving_grad[0]
    position = lax.axis_index("seq")
    reach_back = (WINDOW - 1) // tokens + 1
    assert reach_back % 2 == 0 and count % reach_back == 0 and WINDOW % tokens == 0
    routes = Routes(count, reach_back)
    chips = routes.chips
    chip_in_group = (position % reach_back) // 2
    core = position % 2
    other = 1 - core
    key_width = key_rows.shape[2] // 2
    query_width = queries.shape[2] // 2
    keys, values = key_rows[0], value_rows[0]
    kv_sent = jnp.stack(
        [lax.dynamic_slice_in_dim(keys, other * key_width, key_width, 1),
         lax.dynamic_slice_in_dim(values, other * key_width, key_width, 1)]
    )
    kv_sib = moved(kv_sent, routes.sibling)
    kv_mine = jnp.stack(
        [lax.dynamic_slice_in_dim(keys, core * key_width, key_width, 1),
         lax.dynamic_slice_in_dim(values, core * key_width, key_width, 1)]
    )
    own = jnp.stack([kv_mine, kv_sib], axis=1)
    payloads = gather_window(own, routes, chip_in_group)
    (query_rows, grad_rows, doc_row), _ = lax.optimization_barrier(
        ((queries[0], grad_out, doc_blocks[0]), payloads[0])
    )
    qd_sent = jnp.stack(
        [lax.dynamic_slice_in_dim(query_rows, other * query_width, query_width, 1),
         lax.dynamic_slice_in_dim(grad_rows, other * query_width, query_width, 1)]
    )
    qd_sib = moved(qd_sent, routes.sibling)

    chip = position // 2
    block_of = lambda m, s: 2 * m + jnp.where(s == 0, core, other)
    key_blocks = [block_of(chip - chips + j, s) for j in range(chips + 1) for s in range(2)]
    token_doc = jnp.repeat(doc_row, MBLK)
    pad = (reach_back + 2) * tokens
    doc_pad = jnp.concatenate([jnp.full((pad,), -1, jnp.int32), token_doc])
    key_doc = jnp.concatenate(
        [lax.dynamic_slice_in_dim(doc_pad, b * tokens + pad, tokens, 0) for b in key_blocks]
    )
    offsets = jnp.arange(tokens, dtype=jnp.int32)
    key_pos = jnp.concatenate([b * tokens + offsets for b in key_blocks])
    masks = []
    for block in (position, position ^ 1):
        query_pos = block * tokens + offsets
        query_doc = lax.dynamic_slice_in_dim(token_doc, block * tokens, tokens, 0)
        distance = query_pos[:, None] - key_pos[None, :]
        allowed = (distance >= 0) & (distance < WINDOW) & (query_doc[:, None] == key_doc[None, :])
        masks.append(jnp.where(allowed, 0.0, MASKED_SCORE).astype(jnp.float32))
    bias = jnp.concatenate(masks + masks, axis=0)

    outs = attention_grads(
        core[None].astype(jnp.int32), bias, queries[0], qd_sib[0], grad_out, qd_sib[1], payloads
    )
    dq_mine, dq_sib, parts = outs[0], outs[1], outs[2:]
    summed = scatter_window(parts, routes, chip_in_group)
    sent = jnp.concatenate(
        [summed[0, 1].astype(jnp.bfloat16), summed[1, 1].astype(jnp.bfloat16), dq_sib], axis=-1
    )
    got = moved(sent, routes.sibling)
    grad_key = in_core_order(core, summed[0, 0].astype(jnp.bfloat16), got[:, :key_width])
    grad_value = in_core_order(
        core, summed[1, 0].astype(jnp.bfloat16), got[:, key_width : 2 * key_width]
    )
    grad_query = in_core_order(core, dq_mine, got[:, 2 * key_width :])
    return (grad_query[None], grad_key[None], grad_value[None])


def solution(mesh):
    placed = (
        P("pipe", "seq", None),
        P("pipe", "seq", None),
        P("pipe", "seq", None),
        P("pipe", "seq", None),
        P("pipe", None),
    )
    return jax.shard_map(
        local,
        mesh=mesh,
        in_specs=placed,
        out_specs=(P("pipe", "seq", None), P("pipe", "seq", None), P("pipe", "seq", None)),
        check_vma=False,
    )
```

```python
import jax
import jax.numpy as jnp
from jax import lax
from jax.experimental import pallas as pl
from jax.experimental.pallas import tpu as pltpu
from jax.sharding import PartitionSpec as P

HEADS = 32
KV_HEADS = 16
HEAD_DIM = 128
WINDOW = 1024
MBLK = 128


SCORE_SCALE = 168.0 ** (-0.5)
MASKED_SCORE = -1e30


def passed_along(value, axis, steps):
    count = lax.axis_size(axis)
    pairs = [(source, (source + steps) % count) for source in range(count)]
    return lax.ppermute(value, axis, pairs)


def moved(value, pairs):
    return lax.ppermute(value, "seq", pairs)


def reverse(pairs):
    return [(t, s) for (s, t) in pairs]


class Routes:
    def __init__(self, count, reach):
        self.reach = reach
        self.chips = reach // 2
        group_chip = lambda i: (i % reach) // 2
        self.hop = [(i, i + reach) for i in range(count - reach)]
        self.up = []
        self.down = []
        for e in range(1, self.chips):
            self.up.append([(i, i + 2 * e) for i in range(count) if group_chip(i) + e < self.chips])
            self.down.append(
                [(i, i + 2 * e - reach) for i in range(count) if group_chip(i) + e >= self.chips]
            )
        self.sibling = [(i, i ^ 1) for i in range(count)]


def gather_window(own, routes, chip_in_group):
    prev = moved(own, routes.hop)
    recv = []
    for e in range(1, routes.chips):
        sent = jnp.where(chip_in_group + e < routes.chips, own, prev)
        recv.append(moved(sent, routes.up[e - 1] + routes.down[e - 1]))
    return [prev] + recv[::-1] + [own]


def scatter_window(parts, routes, chip_in_group):
    link = jnp.bfloat16
    chips = routes.chips
    prev, own = parts[0], parts[-1]
    recv = parts[1:-1][::-1]
    for e in range(1, chips):
        pairs = reverse(routes.up[e - 1] + routes.down[e - 1])
        got = moved(recv[e - 1].astype(link), pairs).astype(jnp.float32)
        upward = chip_in_group + e < chips
        own = own + jnp.where(upward, got, 0.0)
        prev = prev + jnp.where(upward, 0.0, got)
    return own + moved(prev.astype(link), reverse(routes.hop)).astype(jnp.float32)


def attention_kernel(chips, core_ref, bias_ref, qm_ref, qs_ref, dm_ref, ds_ref, *refs):
    del core_ref
    kv_refs = refs[:chips]
    dqm_ref, dqs_ref = refs[chips], refs[chips + 1]
    part_refs = refs[chips + 2 :]
    tokens = qm_ref.shape[0]
    d = HEAD_DIM
    k = jnp.concatenate([r[0, s] for r in kv_refs for s in range(2)], axis=0)
    v = jnp.concatenate([r[1, s] for r in kv_refs for s in range(2)], axis=0)
    qs = jnp.concatenate([qm_ref[:, :d], qs_ref[:, :d], qm_ref[:, d:], qs_ref[:, d:]], axis=0)
    dos = jnp.concatenate([dm_ref[:, :d], ds_ref[:, :d], dm_ref[:, d:], ds_ref[:, d:]], axis=0)
    contract_last = (((1,), (1,)), ((), ()))
    contract_first = (((0,), (0,)), ((), ()))
    scores = lax.dot_general(qs, k, contract_last, preferred_element_type=jnp.float32)
    scores = scores * SCORE_SCALE + bias_ref[...]
    largest = jnp.max(scores, axis=1, keepdims=True)
    unscaled = jnp.exp(scores - largest)
    attn = unscaled * (1.0 / jnp.sum(unscaled, axis=1, keepdims=True))
    dattn = lax.dot_general(dos, v, contract_last, preferred_element_type=jnp.float32)
    row_delta = jnp.sum(attn * dattn, axis=1, keepdims=True)
    dscores = (attn * (dattn - row_delta)).astype(jnp.bfloat16)
    grad_q = jnp.dot(dscores, k, preferred_element_type=jnp.float32) * SCORE_SCALE
    rows = lambda j: slice(j * tokens, (j + 1) * tokens)
    dqm_ref[:, :d] = grad_q[rows(0)].astype(dqm_ref.dtype)
    dqs_ref[:, :d] = grad_q[rows(1)].astype(dqs_ref.dtype)
    dqm_ref[:, d:] = grad_q[rows(2)].astype(dqm_ref.dtype)
    dqs_ref[:, d:] = grad_q[rows(3)].astype(dqs_ref.dtype)
    grad_k = (
        lax.dot_general(dscores, qs, contract_first, preferred_element_type=jnp.float32)
        * SCORE_SCALE
    )
    grad_v = lax.dot_general(
        attn.astype(jnp.bfloat16), dos, contract_first, preferred_element_type=jnp.float32
    )
    for j, out in enumerate(part_refs):
        for s in range(2):
            out[0, s] = grad_k[rows(2 * j + s)].astype(out.dtype)
            out[1, s] = grad_v[rows(2 * j + s)].astype(out.dtype)


def attention_grads(core, bias, queries, query_sib, grad_out, grad_sib, payloads):
    tokens = queries.shape[0]
    chips = len(payloads)
    key_count = bias.shape[1]
    half = payloads[0].shape[3]
    heads = half // HEAD_DIM
    pair = 2 * HEAD_DIM
    mine = pl.BlockSpec((tokens, pair), lambda g, c: (0, c[0] * heads + g))
    other = pl.BlockSpec((tokens, pair), lambda g, c: (0, g))
    chip = pl.BlockSpec((2, 2, tokens, HEAD_DIM), lambda g, c: (0, 0, 0, g))
    part = jax.ShapeDtypeStruct(payloads[0].shape, jnp.float32)
    rows = 4 * tokens
    flops = 2 * 5 * rows * key_count * HEAD_DIM * heads
    moved_bytes = 2 * 6 * tokens * half * 2 + 2 * 2 * key_count * half * 3 + bias.size * 4
    grid_spec = pltpu.PrefetchScalarGridSpec(
        num_scalar_prefetch=1,
        grid=(heads,),
        in_specs=[pl.BlockSpec(bias.shape, lambda g, c: (0, 0)), mine, other, mine, other]
        + [chip] * chips,
        out_specs=[other, other] + [chip] * chips,
    )
    return pl.pallas_call(
        lambda *refs: attention_kernel(chips, *refs),
        grid_spec=grid_spec,
        out_shape=[jax.ShapeDtypeStruct(query_sib.shape, jnp.bfloat16)] * 2
        + [part]
        + [jax.ShapeDtypeStruct(part.shape, jnp.bfloat16)] * (chips - 2)
        + [part],
        cost_estimate=pl.CostEstimate(
            flops=flops, transcendentals=rows * key_count * heads, bytes_accessed=moved_bytes
        ),
    )(core, bias, queries, query_sib, grad_out, grad_sib, *payloads)


def in_core_order(core, mine, theirs):
    width = mine.shape[-1]
    out = jnp.zeros(mine.shape[:-1] + (2 * width,), mine.dtype)
    out = lax.dynamic_update_slice_in_dim(out, mine, core * width, out.ndim - 1)
    return lax.dynamic_update_slice_in_dim(out, theirs, (1 - core) * width, out.ndim - 1)


def local(queries, key_rows, value_rows, arriving_grad, doc_blocks):
    tokens = queries.shape[1]
    count = lax.axis_size("seq")
    if lax.axis_size("pipe") > 1:
        arriving_grad = passed_along(arriving_grad, "pipe", -1)
    grad_out = arriving_grad[0]
    position = lax.axis_index("seq")
    reach_back = (WINDOW - 1) // tokens + 1
    assert reach_back % 2 == 0 and count % reach_back == 0 and WINDOW % tokens == 0
    routes = Routes(count, reach_back)
    chips = routes.chips
    chip_in_group = (position % reach_back) // 2
    core = position % 2
    other = 1 - core
    key_width = key_rows.shape[2] // 2
    query_width = queries.shape[2] // 2
    keys, values = key_rows[0], value_rows[0]
    kv_sent = jnp.stack(
        [lax.dynamic_slice_in_dim(keys, other * key_width, key_width, 1),
         lax.dynamic_slice_in_dim(values, other * key_width, key_width, 1)]
    )
    kv_sib = moved(kv_sent, routes.sibling)
    kv_mine = jnp.stack(
        [lax.dynamic_slice_in_dim(keys, core * key_width, key_width, 1),
         lax.dynamic_slice_in_dim(values, core * key_width, key_width, 1)]
    )
    own = jnp.stack([kv_mine, kv_sib], axis=1)
    payloads = gather_window(own, routes, chip_in_group)
    (query_rows, grad_rows, doc_row), _ = lax.optimization_barrier(
        ((queries[0], grad_out, doc_blocks[0]), payloads[0])
    )
    qd_sent = jnp.stack(
        [lax.dynamic_slice_in_dim(query_rows, other * query_width, query_width, 1),
         lax.dynamic_slice_in_dim(grad_rows, other * query_width, query_width, 1)]
    )
    qd_sib = moved(qd_sent, routes.sibling)

    chip = position // 2
    block_of = lambda m, s: 2 * m + jnp.where(s == 0, core, other)
    key_blocks = [block_of(chip - chips + j, s) for j in range(chips + 1) for s in range(2)]
    token_doc = jnp.repeat(doc_row, MBLK)
    pad = (reach_back + 2) * tokens
    doc_pad = jnp.concatenate([jnp.full((pad,), -1, jnp.int32), token_doc])
    key_doc = jnp.concatenate(
        [lax.dynamic_slice_in_dim(doc_pad, b * tokens + pad, tokens, 0) for b in key_blocks]
    )
    offsets = jnp.arange(tokens, dtype=jnp.int32)
    key_pos = jnp.concatenate([b * tokens + offsets for b in key_blocks])
    masks = []
    for block in (position, position ^ 1):
        query_pos = block * tokens + offsets
        query_doc = lax.dynamic_slice_in_dim(token_doc, block * tokens, tokens, 0)
        distance = query_pos[:, None] - key_pos[None, :]
        allowed = (distance >= 0) & (distance < WINDOW) & (query_doc[:, None] == key_doc[None, :])
        masks.append(jnp.where(allowed, 0.0, MASKED_SCORE).astype(jnp.float32))
    bias = jnp.concatenate(masks + masks, axis=0)

    outs = attention_grads(
        core[None].astype(jnp.int32), bias, queries[0], qd_sib[0], grad_out, qd_sib[1], payloads
    )
    dq_mine, dq_sib, parts = outs[0], outs[1], outs[2:]
    summed = scatter_window(parts, routes, chip_in_group)
    sent = jnp.concatenate(
        [summed[0, 1].astype(jnp.bfloat16), summed[1, 1].astype(jnp.bfloat16), dq_sib], axis=-1
    )
    got = moved(sent, routes.sibling)
    grad_key = in_core_order(core, summed[0, 0].astype(jnp.bfloat16), got[:, :key_width])
    grad_value = in_core_order(
        core, summed[1, 0].astype(jnp.bfloat16), got[:, key_width : 2 * key_width]
    )
    grad_query = in_core_order(core, dq_mine, got[:, 2 * key_width :])
    return (grad_query[None], grad_key[None], grad_value[None])


def solution(mesh):
    placed = (
        P("pipe", "seq", None),
        P("pipe", "seq", None),
        P("pipe", "seq", None),
        P("pipe", "seq", None),
        P("pipe", None),
    )
    return jax.shard_map(
        local,
        mesh=mesh,
        in_specs=placed,
        out_specs=(P("pipe", "seq", None), P("pipe", "seq", None), P("pipe", "seq", None)),
        check_vma=False,
    )
```

```python
import jax
import jax.numpy as jnp
from jax import lax
from jax.experimental import pallas as pl
from jax.experimental.pallas import tpu as pltpu
from jax.sharding import PartitionSpec as P

HEADS = 32
KV_HEADS = 16
HEAD_DIM = 128
WINDOW = 1024
MBLK = 128


SCORE_SCALE = 168.0 ** (-0.5)
MASKED_SCORE = -1e30


def passed_along(value, axis, steps):
    count = lax.axis_size(axis)
    pairs = [(source, (source + steps) % count) for source in range(count)]
    return lax.ppermute(value, axis, pairs)


def moved(value, pairs):
    return lax.ppermute(value, "seq", pairs)


def reverse(pairs):
    return [(t, s) for (s, t) in pairs]


class Routes:
    def __init__(self, count, reach):
        self.reach = reach
        self.chips = reach // 2
        group_chip = lambda i: (i % reach) // 2
        self.hop = [(i, i + reach) for i in range(count - reach)]
        self.up = []
        self.down = []
        for e in range(1, self.chips):
            self.up.append([(i, i + 2 * e) for i in range(count) if group_chip(i) + e < self.chips])
            self.down.append(
                [(i, i + 2 * e - reach) for i in range(count) if group_chip(i) + e >= self.chips]
            )
        self.sibling = [(i, i ^ 1) for i in range(count)]


def gather_window(own, routes, chip_in_group):
    prev = moved(own, routes.hop)
    recv = []
    both = lax.dynamic_update_index_in_dim(jnp.stack([own, own]), prev, 1, 0)
    for e in range(1, routes.chips):
        pick = (chip_in_group + e >= routes.chips).astype(jnp.int32)
        sent = lax.dynamic_index_in_dim(both, pick, 0, keepdims=False)
        recv.append(moved(sent, routes.up[e - 1] + routes.down[e - 1]))
    return [prev] + recv[::-1] + [own]


def scatter_window(parts, routes, chip_in_group):
    link = jnp.bfloat16
    chips = routes.chips
    prev, own = parts[0], parts[-1]
    recv = parts[1:-1][::-1]
    for e in range(1, chips):
        pairs = reverse(routes.up[e - 1] + routes.down[e - 1])
        got = moved(recv[e - 1].astype(link), pairs).astype(jnp.float32)
        upward = chip_in_group + e < chips
        own = own + jnp.where(upward, got, 0.0)
        prev = prev + jnp.where(upward, 0.0, got)
    return own + moved(prev.astype(link), reverse(routes.hop)).astype(jnp.float32)


def attention_kernel(chips, core_ref, bias_ref, qm_ref, qs_ref, dm_ref, ds_ref, *refs):
    del core_ref
    kv_refs = refs[:chips]
    dqm_ref, dqs_ref = refs[chips], refs[chips + 1]
    part_refs = refs[chips + 2 :]
    tokens = qm_ref.shape[0]
    d = HEAD_DIM
    k = jnp.concatenate([r[0, s] for r in kv_refs for s in range(2)], axis=0)
    v = jnp.concatenate([r[1, s] for r in kv_refs for s in range(2)], axis=0)
    qs = jnp.concatenate([qm_ref[:, :d], qs_ref[:, :d], qm_ref[:, d:], qs_ref[:, d:]], axis=0)
    dos = jnp.concatenate([dm_ref[:, :d], ds_ref[:, :d], dm_ref[:, d:], ds_ref[:, d:]], axis=0)
    contract_last = (((1,), (1,)), ((), ()))
    contract_first = (((0,), (0,)), ((), ()))
    scores = lax.dot_general(qs, k, contract_last, preferred_element_type=jnp.float32)
    scores = scores * SCORE_SCALE + bias_ref[...]
    largest = jnp.max(scores, axis=1, keepdims=True)
    unscaled = jnp.exp(scores - largest)
    attn = unscaled * (1.0 / jnp.sum(unscaled, axis=1, keepdims=True))
    dattn = lax.dot_general(dos, v, contract_last, preferred_element_type=jnp.float32)
    row_delta = jnp.sum(attn * dattn, axis=1, keepdims=True)
    dscores = (attn * (dattn - row_delta)).astype(jnp.bfloat16)
    grad_q = jnp.dot(dscores, k, preferred_element_type=jnp.float32) * SCORE_SCALE
    rows = lambda j: slice(j * tokens, (j + 1) * tokens)
    dqm_ref[:, :d] = grad_q[rows(0)].astype(dqm_ref.dtype)
    dqs_ref[:, :d] = grad_q[rows(1)].astype(dqs_ref.dtype)
    dqm_ref[:, d:] = grad_q[rows(2)].astype(dqm_ref.dtype)
    dqs_ref[:, d:] = grad_q[rows(3)].astype(dqs_ref.dtype)
    grad_k = (
        lax.dot_general(dscores, qs, contract_first, preferred_element_type=jnp.float32)
        * SCORE_SCALE
    )
    grad_v = lax.dot_general(
        attn.astype(jnp.bfloat16), dos, contract_first, preferred_element_type=jnp.float32
    )
    for j, out in enumerate(part_refs):
        for s in range(2):
            out[0, s] = grad_k[rows(2 * j + s)].astype(out.dtype)
            out[1, s] = grad_v[rows(2 * j + s)].astype(out.dtype)


def attention_grads(core, bias, queries, query_sib, grad_out, grad_sib, payloads):
    tokens = queries.shape[0]
    chips = len(payloads)
    key_count = bias.shape[1]
    half = payloads[0].shape[3]
    heads = half // HEAD_DIM
    pair = 2 * HEAD_DIM
    mine = pl.BlockSpec((tokens, pair), lambda g, c: (0, c[0] * heads + g))
    other = pl.BlockSpec((tokens, pair), lambda g, c: (0, g))
    chip = pl.BlockSpec((2, 2, tokens, HEAD_DIM), lambda g, c: (0, 0, 0, g))
    part = jax.ShapeDtypeStruct(payloads[0].shape, jnp.float32)
    rows = 4 * tokens
    flops = 2 * 5 * rows * key_count * HEAD_DIM * heads
    moved_bytes = 2 * 6 * tokens * half * 2 + 2 * 2 * key_count * half * 3 + bias.size * 4
    grid_spec = pltpu.PrefetchScalarGridSpec(
        num_scalar_prefetch=1,
        grid=(heads,),
        in_specs=[pl.BlockSpec(bias.shape, lambda g, c: (0, 0)), mine, other, mine, other]
        + [chip] * chips,
        out_specs=[other, other] + [chip] * chips,
    )
    return pl.pallas_call(
        lambda *refs: attention_kernel(chips, *refs),
        grid_spec=grid_spec,
        out_shape=[jax.ShapeDtypeStruct(query_sib.shape, jnp.bfloat16)] * 2
        + [part]
        + [jax.ShapeDtypeStruct(part.shape, jnp.bfloat16)] * (chips - 2)
        + [part],
        cost_estimate=pl.CostEstimate(
            flops=flops, transcendentals=rows * key_count * heads, bytes_accessed=moved_bytes
        ),
    )(core, bias, queries, query_sib, grad_out, grad_sib, *payloads)


def in_core_order(core, mine, theirs):
    width = mine.shape[-1]
    out = jnp.zeros(mine.shape[:-1] + (2 * width,), mine.dtype)
    out = lax.dynamic_update_slice_in_dim(out, mine, core * width, out.ndim - 1)
    return lax.dynamic_update_slice_in_dim(out, theirs, (1 - core) * width, out.ndim - 1)


def local(queries, key_rows, value_rows, arriving_grad, doc_blocks):
    tokens = queries.shape[1]
    count = lax.axis_size("seq")
    if lax.axis_size("pipe") > 1:
        arriving_grad = passed_along(arriving_grad, "pipe", -1)
    grad_out = arriving_grad[0]
    position = lax.axis_index("seq")
    reach_back = (WINDOW - 1) // tokens + 1
    assert reach_back % 2 == 0 and count % reach_back == 0 and WINDOW % tokens == 0
    routes = Routes(count, reach_back)
    chips = routes.chips
    chip_in_group = (position % reach_back) // 2
    core = position % 2
    other = 1 - core
    key_width = key_rows.shape[2] // 2
    query_width = queries.shape[2] // 2
    keys, values = key_rows[0], value_rows[0]
    kv_sent = jnp.stack(
        [lax.dynamic_slice_in_dim(keys, other * key_width, key_width, 1),
         lax.dynamic_slice_in_dim(values, other * key_width, key_width, 1)]
    )
    kv_sib = moved(kv_sent, routes.sibling)
    kv_mine = jnp.stack(
        [lax.dynamic_slice_in_dim(keys, core * key_width, key_width, 1),
         lax.dynamic_slice_in_dim(values, core * key_width, key_width, 1)]
    )
    own = jnp.stack([kv_mine, kv_sib], axis=1)
    payloads = gather_window(own, routes, chip_in_group)
    (query_rows, grad_rows, doc_row), _ = lax.optimization_barrier(
        ((queries[0], grad_out, doc_blocks[0]), payloads[0])
    )
    qd_sent = jnp.stack(
        [lax.dynamic_slice_in_dim(query_rows, other * query_width, query_width, 1),
         lax.dynamic_slice_in_dim(grad_rows, other * query_width, query_width, 1)]
    )
    qd_sib = moved(qd_sent, routes.sibling)

    chip = position // 2
    block_of = lambda m, s: 2 * m + jnp.where(s == 0, core, other)
    key_blocks = [block_of(chip - chips + j, s) for j in range(chips + 1) for s in range(2)]
    token_doc = jnp.repeat(doc_row, MBLK)
    pad = (reach_back + 2) * tokens
    doc_pad = jnp.concatenate([jnp.full((pad,), -1, jnp.int32), token_doc])
    key_doc = jnp.concatenate(
        [lax.dynamic_slice_in_dim(doc_pad, b * tokens + pad, tokens, 0) for b in key_blocks]
    )
    offsets = jnp.arange(tokens, dtype=jnp.int32)
    key_pos = jnp.concatenate([b * tokens + offsets for b in key_blocks])
    masks = []
    for block in (position, position ^ 1):
        query_pos = block * tokens + offsets
        query_doc = lax.dynamic_slice_in_dim(token_doc, block * tokens, tokens, 0)
        distance = query_pos[:, None] - key_pos[None, :]
        allowed = (distance >= 0) & (distance < WINDOW) & (query_doc[:, None] == key_doc[None, :])
        masks.append(jnp.where(allowed, 0.0, MASKED_SCORE).astype(jnp.float32))
    bias = jnp.concatenate(masks + masks, axis=0)

    outs = attention_grads(
        core[None].astype(jnp.int32), bias, queries[0], qd_sib[0], grad_out, qd_sib[1], payloads
    )
    dq_mine, dq_sib, parts = outs[0], outs[1], outs[2:]
    summed = scatter_window(parts, routes, chip_in_group)
    sent = jnp.concatenate(
        [summed[0, 1].astype(jnp.bfloat16), summed[1, 1].astype(jnp.bfloat16), dq_sib], axis=-1
    )
    got = moved(sent, routes.sibling)
    grad_key = in_core_order(core, summed[0, 0].astype(jnp.bfloat16), got[:, :key_width])
    grad_value = in_core_order(
        core, summed[1, 0].astype(jnp.bfloat16), got[:, key_width : 2 * key_width]
    )
    grad_query = in_core_order(core, dq_mine, got[:, 2 * key_width :])
    return (grad_query[None], grad_key[None], grad_value[None])


def solution(mesh):
    placed = (
        P("pipe", "seq", None),
        P("pipe", "seq", None),
        P("pipe", "seq", None),
        P("pipe", "seq", None),
        P("pipe", None),
    )
    return jax.shard_map(
        local,
        mesh=mesh,
        in_specs=placed,
        out_specs=(P("pipe", "seq", None), P("pipe", "seq", None), P("pipe", "seq", None)),
        check_vma=False,
    )
```

```python
import jax
import jax.numpy as jnp
from jax import lax
from jax.experimental import pallas as pl
from jax.experimental.pallas import tpu as pltpu
from jax.sharding import PartitionSpec as P

HEADS = 32
KV_HEADS = 16
HEAD_DIM = 128
WINDOW = 1024
MBLK = 128


SCORE_SCALE = 168.0 ** (-0.5)
MASKED_SCORE = -1e30


def passed_along(value, axis, steps):
    count = lax.axis_size(axis)
    pairs = [(source, (source + steps) % count) for source in range(count)]
    return lax.ppermute(value, axis, pairs)


def moved(value, pairs):
    return lax.ppermute(value, "seq", pairs)


def reverse(pairs):
    return [(t, s) for (s, t) in pairs]


class Routes:
    def __init__(self, count, reach):
        self.reach = reach
        self.chips = reach // 2
        group_chip = lambda i: (i % reach) // 2
        self.hop = [(i, i + reach) for i in range(count - reach)]
        self.up = []
        self.down = []
        for e in range(1, self.chips):
            self.up.append([(i, i + 2 * e) for i in range(count) if group_chip(i) + e < self.chips])
            self.down.append(
                [(i, i + 2 * e - reach) for i in range(count) if group_chip(i) + e >= self.chips]
            )
        self.sibling = [(i, i ^ 1) for i in range(count)]


def gather_window(own, routes, chip_in_group):
    prev = moved(own, routes.hop)
    recv = []
    for e in range(1, routes.chips):
        sent = jnp.where(chip_in_group + e < routes.chips, own, prev)
        recv.append(moved(sent, routes.up[e - 1] + routes.down[e - 1]))
    return [prev] + recv[::-1] + [own]


def scatter_window(parts, routes, chip_in_group):
    link = jnp.bfloat16
    chips = routes.chips
    prev, own = parts[0], parts[-1]
    recv = parts[1:-1][::-1]
    for e in range(1, chips):
        pairs = reverse(routes.up[e - 1] + routes.down[e - 1])
        got = moved(recv[e - 1].astype(link), pairs).astype(jnp.float32)
        upward = chip_in_group + e < chips
        own = own + jnp.where(upward, got, 0.0)
        prev = prev + jnp.where(upward, 0.0, got)
    return own + moved(prev.astype(link), reverse(routes.hop)).astype(jnp.float32)


def attention_kernel(chips, core_ref, bias_ref, qm_ref, qs_ref, dm_ref, ds_ref, *refs):
    del core_ref
    kv_refs = refs[:chips]
    dqm_ref, dqs_ref = refs[chips], refs[chips + 1]
    part_refs = refs[chips + 2 :]
    tokens = qm_ref.shape[0]
    d = HEAD_DIM
    k = jnp.concatenate([r[0, s] for r in kv_refs for s in range(2)], axis=0)
    v = jnp.concatenate([r[1, s] for r in kv_refs for s in range(2)], axis=0)
    qs = jnp.concatenate([qm_ref[:, :d], qs_ref[:, :d], qm_ref[:, d:], qs_ref[:, d:]], axis=0)
    dos = jnp.concatenate([dm_ref[:, :d], ds_ref[:, :d], dm_ref[:, d:], ds_ref[:, d:]], axis=0)
    contract_last = (((1,), (1,)), ((), ()))
    contract_first = (((0,), (0,)), ((), ()))
    scores = lax.dot_general(qs, k, contract_last, preferred_element_type=jnp.float32)
    scores = scores * SCORE_SCALE + bias_ref[...]
    largest = jnp.max(scores, axis=1, keepdims=True)
    unscaled = jnp.exp(scores - largest)
    attn = unscaled * (1.0 / jnp.sum(unscaled, axis=1, keepdims=True))
    dattn = lax.dot_general(dos, v, contract_last, preferred_element_type=jnp.float32)
    row_delta = jnp.sum(attn * dattn, axis=1, keepdims=True)
    dscores = (attn * (dattn - row_delta)).astype(jnp.bfloat16)
    grad_q = jnp.dot(dscores, k, preferred_element_type=jnp.float32) * SCORE_SCALE
    rows = lambda j: slice(j * tokens, (j + 1) * tokens)
    dqm_ref[:, :d] = grad_q[rows(0)].astype(dqm_ref.dtype)
    dqs_ref[:, :d] = grad_q[rows(1)].astype(dqs_ref.dtype)
    dqm_ref[:, d:] = grad_q[rows(2)].astype(dqm_ref.dtype)
    dqs_ref[:, d:] = grad_q[rows(3)].astype(dqs_ref.dtype)
    grad_k = (
        lax.dot_general(dscores, qs, contract_first, preferred_element_type=jnp.float32)
        * SCORE_SCALE
    )
    grad_v = lax.dot_general(
        attn.astype(jnp.bfloat16), dos, contract_first, preferred_element_type=jnp.float32
    )
    for j, out in enumerate(part_refs):
        for s in range(2):
            out[0, s] = grad_k[rows(2 * j + s)].astype(out.dtype)
            out[1, s] = grad_v[rows(2 * j + s)].astype(out.dtype)


def attention_grads(core, bias, queries, query_sib, grad_out, grad_sib, payloads):
    tokens = queries.shape[0]
    chips = len(payloads)
    key_count = bias.shape[1]
    half = payloads[0].shape[3]
    heads = half // HEAD_DIM
    pair = 2 * HEAD_DIM
    mine = pl.BlockSpec((tokens, pair), lambda g, c: (0, c[0] * heads + g))
    other = pl.BlockSpec((tokens, pair), lambda g, c: (0, g))
    chip = pl.BlockSpec((2, 2, tokens, HEAD_DIM), lambda g, c: (0, 0, 0, g))
    part = jax.ShapeDtypeStruct(payloads[0].shape, jnp.float32)
    rows = 4 * tokens
    flops = 2 * 5 * rows * key_count * HEAD_DIM * heads
    moved_bytes = 2 * 6 * tokens * half * 2 + 2 * 2 * key_count * half * 3 + bias.size * 4
    grid_spec = pltpu.PrefetchScalarGridSpec(
        num_scalar_prefetch=1,
        grid=(heads,),
        in_specs=[pl.BlockSpec(bias.shape, lambda g, c: (0, 0)), mine, other, mine, other]
        + [chip] * chips,
        out_specs=[other, other] + [chip] * chips,
    )
    return pl.pallas_call(
        lambda *refs: attention_kernel(chips, *refs),
        grid_spec=grid_spec,
        out_shape=[jax.ShapeDtypeStruct(query_sib.shape, jnp.bfloat16)] * 2
        + [part]
        + [jax.ShapeDtypeStruct(part.shape, jnp.bfloat16)] * (chips - 2)
        + [part],
        cost_estimate=pl.CostEstimate(
            flops=flops, transcendentals=rows * key_count * heads, bytes_accessed=moved_bytes
        ),
    )(core, bias, queries, query_sib, grad_out, grad_sib, *payloads)


def in_core_order(core, mine, theirs):
    width = mine.shape[-1]
    out = jnp.zeros(mine.shape[:-1] + (2 * width,), mine.dtype)
    out = lax.dynamic_update_slice_in_dim(out, mine, core * width, out.ndim - 1)
    return lax.dynamic_update_slice_in_dim(out, theirs, (1 - core) * width, out.ndim - 1)


def local(queries, key_rows, value_rows, arriving_grad, doc_blocks):
    tokens = queries.shape[1]
    count = lax.axis_size("seq")
    if lax.axis_size("pipe") > 1:
        arriving_grad = passed_along(arriving_grad, "pipe", -1)
    grad_out = arriving_grad[0]
    position = lax.axis_index("seq")
    reach_back = (WINDOW - 1) // tokens + 1
    assert reach_back % 2 == 0 and count % reach_back == 0 and WINDOW % tokens == 0
    routes = Routes(count, reach_back)
    chips = routes.chips
    chip_in_group = (position % reach_back) // 2
    core = position % 2
    other = 1 - core
    key_width = key_rows.shape[2] // 2
    query_width = queries.shape[2] // 2
    keys, values = key_rows[0], value_rows[0]
    kv_sent = jnp.stack(
        [lax.dynamic_slice_in_dim(keys, other * key_width, key_width, 1),
         lax.dynamic_slice_in_dim(values, other * key_width, key_width, 1)]
    )
    kv_sib = moved(kv_sent, routes.sibling)
    kv_mine = jnp.stack(
        [lax.dynamic_slice_in_dim(keys, core * key_width, key_width, 1),
         lax.dynamic_slice_in_dim(values, core * key_width, key_width, 1)]
    )
    own = jnp.zeros((2, 2) + kv_mine.shape[1:], kv_mine.dtype)
    own = lax.dynamic_update_index_in_dim(own, kv_mine, 0, 1)
    own = lax.dynamic_update_index_in_dim(own, kv_sib, 1, 1)
    payloads = gather_window(own, routes, chip_in_group)
    (query_rows, grad_rows, doc_row), _ = lax.optimization_barrier(
        ((queries[0], grad_out, doc_blocks[0]), payloads[0])
    )
    qd_sent = jnp.stack(
        [lax.dynamic_slice_in_dim(query_rows, other * query_width, query_width, 1),
         lax.dynamic_slice_in_dim(grad_rows, other * query_width, query_width, 1)]
    )
    qd_sib = moved(qd_sent, routes.sibling)

    chip = position // 2
    block_of = lambda m, s: 2 * m + jnp.where(s == 0, core, other)
    key_blocks = [block_of(chip - chips + j, s) for j in range(chips + 1) for s in range(2)]
    token_doc = jnp.repeat(doc_row, MBLK)
    pad = (reach_back + 2) * tokens
    doc_pad = jnp.concatenate([jnp.full((pad,), -1, jnp.int32), token_doc])
    key_doc = jnp.concatenate(
        [lax.dynamic_slice_in_dim(doc_pad, b * tokens + pad, tokens, 0) for b in key_blocks]
    )
    offsets = jnp.arange(tokens, dtype=jnp.int32)
    key_pos = jnp.concatenate([b * tokens + offsets for b in key_blocks])
    masks = []
    for block in (position, position ^ 1):
        query_pos = block * tokens + offsets
        query_doc = lax.dynamic_slice_in_dim(token_doc, block * tokens, tokens, 0)
        distance = query_pos[:, None] - key_pos[None, :]
        allowed = (distance >= 0) & (distance < WINDOW) & (query_doc[:, None] == key_doc[None, :])
        masks.append(jnp.where(allowed, 0.0, MASKED_SCORE).astype(jnp.float32))
    bias = jnp.concatenate(masks + masks, axis=0)

    outs = attention_grads(
        core[None].astype(jnp.int32), bias, queries[0], qd_sib[0], grad_out, qd_sib[1], payloads
    )
    dq_mine, dq_sib, parts = outs[0], outs[1], outs[2:]
    summed = scatter_window(parts, routes, chip_in_group)
    sent = jnp.concatenate(
        [summed[0, 1].astype(jnp.bfloat16), summed[1, 1].astype(jnp.bfloat16), dq_sib], axis=-1
    )
    got = moved(sent, routes.sibling)
    grad_key = in_core_order(core, summed[0, 0].astype(jnp.bfloat16), got[:, :key_width])
    grad_value = in_core_order(
        core, summed[1, 0].astype(jnp.bfloat16), got[:, key_width : 2 * key_width]
    )
    grad_query = in_core_order(core, dq_mine, got[:, 2 * key_width :])
    return (grad_query[None], grad_key[None], grad_value[None])


def solution(mesh):
    placed = (
        P("pipe", "seq", None),
        P("pipe", "seq", None),
        P("pipe", "seq", None),
        P("pipe", "seq", None),
        P("pipe", None),
    )
    return jax.shard_map(
        local,
        mesh=mesh,
        in_specs=placed,
        out_specs=(P("pipe", "seq", None), P("pipe", "seq", None), P("pipe", "seq", None)),
        check_vma=False,
    )
```

```python
import jax
import jax.numpy as jnp
from jax import lax
from jax.experimental import pallas as pl
from jax.experimental.pallas import tpu as pltpu
from jax.sharding import PartitionSpec as P

HEADS = 32
KV_HEADS = 16
HEAD_DIM = 128
WINDOW = 1024
MBLK = 128


SCORE_SCALE = 168.0 ** (-0.5)
MASKED_SCORE = -1e30


def passed_along(value, axis, steps):
    count = lax.axis_size(axis)
    pairs = [(source, (source + steps) % count) for source in range(count)]
    return lax.ppermute(value, axis, pairs)


def moved(value, pairs):
    return lax.ppermute(value, "seq", pairs)


def reverse(pairs):
    return [(t, s) for (s, t) in pairs]


class Routes:
    def __init__(self, count, reach):
        self.reach = reach
        self.chips = reach // 2
        group_chip = lambda i: (i % reach) // 2
        self.hop = [(i, i + reach) for i in range(count - reach)]
        self.up = []
        self.down = []
        for e in range(1, self.chips):
            self.up.append([(i, i + 2 * e) for i in range(count) if group_chip(i) + e < self.chips])
            self.down.append(
                [(i, i + 2 * e - reach) for i in range(count) if group_chip(i) + e >= self.chips]
            )
        self.sibling = [(i, i ^ 1) for i in range(count)]


def gather_window(own, routes, chip_in_group):
    prev = moved(own, routes.hop)
    recv = []
    for e in range(1, routes.chips):
        sent = jnp.where(chip_in_group + e < routes.chips, own, prev)
        recv.append(moved(sent, routes.up[e - 1] + routes.down[e - 1]))
    return [prev] + recv[::-1] + [own]


def scatter_window(parts, routes, chip_in_group):
    link = jnp.bfloat16
    chips = routes.chips
    prev, own = parts[0], parts[-1]
    recv = parts[1:-1][::-1]
    for e in range(1, chips):
        pairs = reverse(routes.up[e - 1] + routes.down[e - 1])
        got = moved(recv[e - 1].astype(link), pairs).astype(jnp.float32)
        upward = chip_in_group + e < chips
        own = own + jnp.where(upward, got, 0.0)
        prev = prev + jnp.where(upward, 0.0, got)
    return own + moved(prev.astype(link), reverse(routes.hop)).astype(jnp.float32)


def attention_kernel(chips, core_ref, bias_ref, qm_ref, qs_ref, dm_ref, ds_ref, *refs):
    del core_ref
    kv_refs = refs[:chips]
    dqm_ref, dqs_ref = refs[chips], refs[chips + 1]
    part_refs = refs[chips + 2 :]
    tokens = qm_ref.shape[0]
    d = HEAD_DIM
    k = jnp.concatenate([r[0, s] for r in kv_refs for s in range(2)], axis=0)
    v = jnp.concatenate([r[1, s] for r in kv_refs for s in range(2)], axis=0)
    qs = jnp.concatenate([qm_ref[:, :d], qs_ref[:, :d], qm_ref[:, d:], qs_ref[:, d:]], axis=0)
    dos = jnp.concatenate([dm_ref[:, :d], ds_ref[:, :d], dm_ref[:, d:], ds_ref[:, d:]], axis=0)
    contract_last = (((1,), (1,)), ((), ()))
    contract_first = (((0,), (0,)), ((), ()))
    scores = lax.dot_general(qs, k, contract_last, preferred_element_type=jnp.float32)
    scores = scores * SCORE_SCALE + bias_ref[...]
    largest = jnp.max(scores, axis=1, keepdims=True)
    unscaled = jnp.exp(scores - largest)
    attn = unscaled * (1.0 / jnp.sum(unscaled, axis=1, keepdims=True))
    dattn = lax.dot_general(dos, v, contract_last, preferred_element_type=jnp.float32)
    row_delta = jnp.sum(attn * dattn, axis=1, keepdims=True)
    dscores = (attn * (dattn - row_delta)).astype(jnp.bfloat16)
    grad_q = jnp.dot(dscores, k, preferred_element_type=jnp.float32) * SCORE_SCALE
    rows = lambda j: slice(j * tokens, (j + 1) * tokens)
    dqm_ref[:, :d] = grad_q[rows(0)].astype(dqm_ref.dtype)
    dqs_ref[:, :d] = grad_q[rows(1)].astype(dqs_ref.dtype)
    dqm_ref[:, d:] = grad_q[rows(2)].astype(dqm_ref.dtype)
    dqs_ref[:, d:] = grad_q[rows(3)].astype(dqs_ref.dtype)
    grad_k = (
        lax.dot_general(dscores, qs, contract_first, preferred_element_type=jnp.float32)
        * SCORE_SCALE
    )
    grad_v = lax.dot_general(
        attn.astype(jnp.bfloat16), dos, contract_first, preferred_element_type=jnp.float32
    )
    for j, out in enumerate(part_refs):
        for s in range(2):
            out[0, s] = grad_k[rows(2 * j + s)].astype(out.dtype)
            out[1, s] = grad_v[rows(2 * j + s)].astype(out.dtype)


def attention_grads(core, bias, queries, query_sib, grad_out, grad_sib, payloads):
    tokens = queries.shape[0]
    chips = len(payloads)
    key_count = bias.shape[1]
    half = payloads[0].shape[3]
    heads = half // HEAD_DIM
    pair = 2 * HEAD_DIM
    mine = pl.BlockSpec((tokens, pair), lambda g, c: (0, c[0] * heads + g))
    other = pl.BlockSpec((tokens, pair), lambda g, c: (0, g))
    chip = pl.BlockSpec((2, 2, tokens, HEAD_DIM), lambda g, c: (0, 0, 0, g))
    part = jax.ShapeDtypeStruct(payloads[0].shape, jnp.float32)
    rows = 4 * tokens
    flops = 2 * 5 * rows * key_count * HEAD_DIM * heads
    moved_bytes = 2 * 6 * tokens * half * 2 + 2 * 2 * key_count * half * 3 + bias.size * 4
    grid_spec = pltpu.PrefetchScalarGridSpec(
        num_scalar_prefetch=1,
        grid=(heads,),
        in_specs=[pl.BlockSpec(bias.shape, lambda g, c: (0, 0)), mine, other, mine, other]
        + [chip] * chips,
        out_specs=[other, other] + [chip] * chips,
    )
    return pl.pallas_call(
        lambda *refs: attention_kernel(chips, *refs),
        grid_spec=grid_spec,
        out_shape=[jax.ShapeDtypeStruct(query_sib.shape, jnp.bfloat16)] * 2
        + [part]
        + [jax.ShapeDtypeStruct(part.shape, jnp.bfloat16)] * (chips - 2)
        + [part],
        cost_estimate=pl.CostEstimate(
            flops=flops, transcendentals=rows * key_count * heads, bytes_accessed=moved_bytes
        ),
    )(core, bias, queries, query_sib, grad_out, grad_sib, *payloads)


def in_core_order(core, mine, theirs):
    width = mine.shape[-1]
    out = jnp.zeros(mine.shape[:-1] + (2 * width,), mine.dtype)
    out = lax.dynamic_update_slice_in_dim(out, mine, core * width, out.ndim - 1)
    return lax.dynamic_update_slice_in_dim(out, theirs, (1 - core) * width, out.ndim - 1)


def local(queries, key_rows, value_rows, arriving_grad, doc_blocks):
    tokens = queries.shape[1]
    count = lax.axis_size("seq")
    if lax.axis_size("pipe") > 1:
        arriving_grad = passed_along(arriving_grad, "pipe", -1)
    grad_out = arriving_grad[0]
    position = lax.axis_index("seq")
    reach_back = (WINDOW - 1) // tokens + 1
    assert reach_back % 2 == 0 and count % reach_back == 0 and WINDOW % tokens == 0
    routes = Routes(count, reach_back)
    chips = routes.chips
    chip_in_group = (position % reach_back) // 2
    core = position % 2
    other = 1 - core
    key_width = key_rows.shape[2] // 2
    query_width = queries.shape[2] // 2
    keys, values = key_rows[0], value_rows[0]
    kv_sent = jnp.stack(
        [lax.dynamic_slice_in_dim(keys, other * key_width, key_width, 1),
         lax.dynamic_slice_in_dim(values, other * key_width, key_width, 1)]
    )
    kv_sib = moved(kv_sent, routes.sibling)
    kv_mine = jnp.stack(
        [lax.dynamic_slice_in_dim(keys, core * key_width, key_width, 1),
         lax.dynamic_slice_in_dim(values, core * key_width, key_width, 1)]
    )
    own = jnp.zeros((2, 2) + kv_mine.shape[1:], kv_mine.dtype)
    own = lax.dynamic_update_index_in_dim(own, kv_mine, 0, 1)
    own = lax.dynamic_update_index_in_dim(own, kv_sib, 1, 1)
    payloads = gather_window(own, routes, chip_in_group)
    (query_rows, grad_rows, doc_row), _ = lax.optimization_barrier(
        ((queries[0], grad_out, doc_blocks[0]), payloads[0])
    )
    qd_sent = jnp.stack(
        [lax.dynamic_slice_in_dim(query_rows, other * query_width, query_width, 1),
         lax.dynamic_slice_in_dim(grad_rows, other * query_width, query_width, 1)]
    )
    qd_sib = moved(qd_sent, routes.sibling)

    chip = position // 2
    block_of = lambda m, s: 2 * m + jnp.where(s == 0, core, other)
    key_blocks = [block_of(chip - chips + j, s) for j in range(chips + 1) for s in range(2)]
    token_doc = jnp.repeat(doc_row, MBLK)
    pad = (reach_back + 2) * tokens
    doc_pad = jnp.concatenate([jnp.full((pad,), -1, jnp.int32), token_doc])
    key_doc = jnp.concatenate(
        [lax.dynamic_slice_in_dim(doc_pad, b * tokens + pad, tokens, 0) for b in key_blocks]
    )
    offsets = jnp.arange(tokens, dtype=jnp.int32)
    key_pos = jnp.concatenate([b * tokens + offsets for b in key_blocks])
    masks = []
    for block in (position, position ^ 1):
        query_pos = block * tokens + offsets
        query_doc = lax.dynamic_slice_in_dim(token_doc, block * tokens, tokens, 0)
        distance = query_pos[:, None] - key_pos[None, :]
        allowed = (distance >= 0) & (distance < WINDOW) & (query_doc[:, None] == key_doc[None, :])
        masks.append(jnp.where(allowed, 0.0, MASKED_SCORE).astype(jnp.float32))
    bias = jnp.concatenate(masks + masks, axis=0)

    outs = attention_grads(
        core[None].astype(jnp.int32), bias, queries[0], qd_sib[0], grad_out, qd_sib[1], payloads
    )
    dq_mine, dq_sib, parts = outs[0], outs[1], outs[2:]
    summed = scatter_window(parts, routes, chip_in_group)
    sent = jnp.zeros((tokens, 2 * key_width + dq_sib.shape[1]), jnp.bfloat16)
    sent = lax.dynamic_update_slice_in_dim(sent, dq_sib, 2 * key_width, 1)
    sent = lax.dynamic_update_slice_in_dim(sent, summed[0, 1].astype(jnp.bfloat16), 0, 1)
    sent = lax.dynamic_update_slice_in_dim(sent, summed[1, 1].astype(jnp.bfloat16), key_width, 1)
    got = moved(sent, routes.sibling)
    grad_key = in_core_order(core, summed[0, 0].astype(jnp.bfloat16), got[:, :key_width])
    grad_value = in_core_order(
        core, summed[1, 0].astype(jnp.bfloat16), got[:, key_width : 2 * key_width]
    )
    grad_query = in_core_order(core, dq_mine, got[:, 2 * key_width :])
    return (grad_query[None], grad_key[None], grad_value[None])


def solution(mesh):
    placed = (
        P("pipe", "seq", None),
        P("pipe", "seq", None),
        P("pipe", "seq", None),
        P("pipe", "seq", None),
        P("pipe", None),
    )
    return jax.shard_map(
        local,
        mesh=mesh,
        in_specs=placed,
        out_specs=(P("pipe", "seq", None), P("pipe", "seq", None), P("pipe", "seq", None)),
        check_vma=False,
    )
```
